32 devices in a mesh: parts: 2 (over x), seq: 16 (over z, y, core).
Axes of the slice: x: 2, y: 2, z: 4, core: 2. Of those that a mesh axis runs over, the one named last changes fastest.
Arguments:
- queries: bfloat16 [8192, 4096], P(('parts', 'seq')), parts along dimension 0, may hold values from -6 to 6
- keys: bfloat16 [8192, 256], P(('parts', 'seq')), parts along dimension 0, may hold values from -6 to 6
- values: bfloat16 [8192, 256], P(('parts', 'seq')), parts along dimension 0, may hold values from -6 to 6
- outputs: bfloat16 [8192, 4096], P(('parts', 'seq')), parts along dimension 0, may hold values from -0.59765625 to 0.59765625
- out_grad: bfloat16 [8192, 4096], P(('parts', 'seq')), parts along dimension 0, may hold values from -6 to 6
- logsumexp: float32 [32, 8192], P(None, ('parts', 'seq')), parts along dimension 1, may hold values from 4 to 7
- doc_lengths: int32 [32], P('parts'), parts along dimension 0, may hold values from 1 to 512, 4096 in all
Outputs:
- query_grad: bfloat16 [8192, 4096], P(('parts', 'seq')), parts along dimension 0
- key_grad: bfloat16 [8192, 256], P(('parts', 'seq')), parts along dimension 0
- value_grad: bfloat16 [8192, 256], P(('parts', 'seq')), parts along dimension 0
The draws below stay inside these ranges and needn't reach their ends.
There are 2 independent parts, one for each index of `parts`. The reference program is written for one: setup_inputs(seed, part) draws one part's arguments, and reference() takes and returns one part's arrays. A program takes and returns all parts, laid end to end along the dimension named above; each array names one. Nothing has to cross between parts.
Inputs may be any that keep to these rules, and one draw needn't show every extreme that they name: `doc_lengths`: lengths of whole documents that fill the pack: they sum to 4096, and the longest has exactly 512 tokens.
All inputs are finite; a program needn't handle non-finite values.
Results may differ from the reference program's by a relative error of at most 0.0057.
Values may be sent and summed in bfloat16 or wider, within the bound.
No kernel may reach another device: no remote copies, remote signals or barrier semaphores. Data moves between devices by JAX's collectives and lax.ppermute only.
A program may use at most 64 MiB of HBM per device.

```python
import math
import jax
import jax.numpy as jnp
import numpy as np
from jax import lax

H = 32
KVH = 2
HD = 128
TOK_DEV = 256
REACH = 2
TOKENS = 4096
MOST = 512
NDOC = 16


def level_of(key, dims, pieces, smallest, top_value):
    factor_of, own = 1.0, jax.random.fold_in(key, 6)
    for position, blocks in pieces:
        steps = jnp.exp(jax.random.uniform(jax.random.fold_in(own, position), (blocks,), jnp.float32, smallest / len(pieces), top_value / len(pieces)))
        factor_of = factor_of * jnp.repeat(steps, dims[position] // blocks).reshape([-1 if axis == position else 1 for axis in range(len(dims))])
    return factor_of


def profile(number_of, total, most, skew):
    portions = [(1 << 20) // math.isqrt(standing ** skew) + 1 for standing in range(2, number_of + 1)]
    rest, counts = total - most - (number_of - 1), [1] * (number_of - 1)
    while rest > 0:
        candidates = [i for i in range(number_of - 1) if counts[i] < most]
        mass, remaining = sum([portions[i] for i in candidates]), rest
        for i in candidates:
            more = min(most - counts[i], max(1, remaining * portions[i] // mass), rest)
            counts[i] = counts[i] + more
            rest = rest - more
    return np.array([most] + counts)


def ragged_sizes(key, number_of, total, bound, slope):
    if number_of == 2:
        one = jax.random.randint(key, (), max(1, total - bound), min(bound, total - 1) + 1)
        return jnp.stack([one, total - one])
    tallies = jnp.asarray(profile(number_of, total, bound, slope), jnp.int32)
    couples = (number_of - 1) // 2
    source_of, receiver = tallies[1:1 + 2 * couples:2], tallies[2:2 + 2 * couples:2]
    margin = jnp.minimum(source_of - 1, bound - receiver)
    moved = jax.random.randint(jax.random.fold_in(key, 1), (couples,), 0, 1 << 20) % (margin + 1)
    tallies = tallies.at[1:1 + 2 * couples:2].set(source_of - moved).at[2:2 + 2 * couples:2].set(receiver + moved)
    return tallies[jax.random.permutation(jax.random.fold_in(key, 2), number_of)]


def normal_values(stream_key, shape, deviation, reach, split=(), kind=jnp.bfloat16):
    drawn = jax.random.normal(stream_key, shape, jnp.float32) * deviation
    if len(split) > 0:
        drawn = level_of(stream_key, shape, split, -0.22, 0.18) * drawn
    return jnp.clip(drawn, min=-reach, max=reach).astype(kind)


def setup_inputs(seed: int = 0, part: int = 0) -> dict:
    arg_keys = jax.random.split(jax.random.key(seed), 8)
    part_splits = jax.random.split(jax.random.fold_in(arg_keys[7], part), 8)
    queries = normal_values(part_splits[0], (TOKENS, H * HD), 1.0, 6.0, ((0, 16),))
    keys = normal_values(part_splits[1], (TOKENS, KVH * HD), 1.0, 6.0, ((0, 16),))
    values = normal_values(part_splits[2], (TOKENS, KVH * HD), 1.0, 6.0, ((0, 16),))
    outputs = normal_values(part_splits[3], (TOKENS, H * HD), 0.1, 0.59765625, ((0, 16),))
    out_grad = normal_values(part_splits[4], (TOKENS, H * HD), 1.0, 6.0, ((0, 16),))
    logsumexp = jnp.clip(4.0 + 3.0 * jax.random.uniform(part_splits[5], (H, TOKENS), jnp.float32) ** level_of(part_splits[5], (H, TOKENS), ((1, 16),), -0.2, 0.2), 4.0, 7.0)
    doc_lengths = ragged_sizes(part_splits[6], NDOC, TOKENS, MOST, 1).astype(jnp.int32)
    return {"queries": queries, "keys": keys, "values": values, "outputs": outputs, "out_grad": out_grad, "logsumexp": logsumexp, "doc_lengths": doc_lengths}


def reference(queries, keys, values, outputs, out_grad, logsumexp, doc_lengths):
    group_size = H // KVH
    scaling = 1.0 / math.sqrt(HD)
    span = REACH * TOK_DEV
    window = span + TOK_DEV
    doc_ends = jnp.cumsum(doc_lengths).astype(jnp.int32)
    places = jnp.arange(TOKENS, dtype=jnp.int32)
    doc_ids = lax.optimization_barrier(jnp.sum((doc_ends[None, :] <= places[:, None]).astype(jnp.int32), axis=1)).astype(jnp.int32)
    ids_pad = jnp.concatenate([jnp.full((span,), -1, jnp.int32), doc_ids])
    places_pad = jnp.concatenate([jnp.arange(-span, 0, dtype=jnp.int32), places])
    key_pad = jnp.concatenate([jnp.zeros((span, KVH, HD), jnp.float32), keys.astype(jnp.float32).reshape(TOKENS, KVH, HD)])
    value_pad = jnp.concatenate([jnp.zeros((span, KVH, HD), jnp.float32), values.astype(jnp.float32).reshape(TOKENS, KVH, HD)])
    query_all = queries.astype(jnp.float32).reshape(TOKENS, KVH, group_size, HD)
    grad_all = out_grad.astype(jnp.float32).reshape(TOKENS, KVH, group_size, HD)
    delta_all = lax.optimization_barrier(jnp.sum(grad_all * outputs.astype(jnp.float32).reshape(TOKENS, KVH, group_size, HD), axis=3))
    lse_all = logsumexp.astype(jnp.float32).reshape(KVH, group_size, TOKENS)

    def block_step(running, block_index):
        key_acc, value_acc = running
        row_start = (block_index * TOK_DEV).astype(jnp.int32)
        query_blk = lax.dynamic_slice_in_dim(query_all, row_start, TOK_DEV, 0)
        grad_blk = lax.dynamic_slice_in_dim(grad_all, row_start, TOK_DEV, 0)
        delta_blk = jnp.transpose(lax.dynamic_slice_in_dim(delta_all, row_start, TOK_DEV, 0), (1, 2, 0))
        lse_blk = lax.dynamic_slice_in_dim(lse_all, row_start, TOK_DEV, 2)
        query_ids = lax.dynamic_slice_in_dim(doc_ids, row_start, TOK_DEV, 0)
        query_places = lax.dynamic_slice_in_dim(places, row_start, TOK_DEV, 0)
        key_blk = lax.dynamic_slice_in_dim(key_pad, row_start, window, 0)
        value_blk = lax.dynamic_slice_in_dim(value_pad, row_start, window, 0)
        key_ids = lax.dynamic_slice_in_dim(ids_pad, row_start, window, 0)
        key_places = lax.dynamic_slice_in_dim(places_pad, row_start, window, 0)
        visible = (query_ids[:, None] == key_ids[None, :]) & (key_places[None, :] <= query_places[:, None])
        scores = jnp.einsum('qgrd,kgd->grqk', query_blk, key_blk) * scaling
        probs = jnp.where(visible[None, None], jnp.exp(scores - lse_blk[..., None]), 0.0)
        probs_low = lax.optimization_barrier(probs.astype(jnp.bfloat16)).astype(jnp.float32)
        value_term = jnp.einsum('grqk,qgrd->kgd', probs_low, grad_blk)
        prob_grad = jnp.einsum('qgrd,kgd->grqk', grad_blk, value_blk)
        score_grad = probs * (prob_grad - delta_blk[..., None])
        score_low = lax.optimization_barrier(score_grad.astype(jnp.bfloat16)).astype(jnp.float32)
        query_term = jnp.einsum('grqk,kgd->qgrd', score_low, key_blk) * scaling
        key_term = jnp.einsum('grqk,qgrd->kgd', score_low, query_blk) * scaling
        key_acc = lax.dynamic_update_slice_in_dim(key_acc, lax.dynamic_slice_in_dim(key_acc, row_start, window, 0) + key_term, row_start, 0)
        value_acc = lax.dynamic_update_slice_in_dim(value_acc, lax.dynamic_slice_in_dim(value_acc, row_start, window, 0) + value_term, row_start, 0)
        return ((key_acc, value_acc), query_term.reshape(TOK_DEV, H * HD).astype(jnp.bfloat16))
    zeros_acc = jnp.zeros((span + TOKENS, KVH, HD), jnp.float32)
    finals, query_blocks = lax.scan(block_step, (zeros_acc, zeros_acc), jnp.arange(TOKENS // TOK_DEV, dtype=jnp.int32))
    query_grad = query_blocks.reshape(TOKENS, H * HD)
    key_grad = finals[0][span:].reshape(TOKENS, KVH * HD).astype(jnp.bfloat16)
    value_grad = finals[1][span:].reshape(TOKENS, KVH * HD).astype(jnp.bfloat16)
    return (query_grad, key_grad, value_grad)
```

```python
import math

import jax
import jax.numpy as jnp
from jax import lax
from jax.experimental import pallas as pl
from jax.experimental.pallas import tpu as pltpu
from jax.sharding import PartitionSpec as P

HD = 128
MOST = 512
KEY_TILE = 128
HEADS_PER_STEP = 4
NT_DIMS = (((1,), (1,)), ((), ()))


def shifted(block, axis, distance):
    devices = range(lax.axis_size(axis))
    route = [(i - distance, i) for i in devices if i - distance in devices]
    return lax.ppermute(block, axis, route)


def make_kernel(heads_per_group, tok, win, diag_tile):
    blocks_per_group = heads_per_group // HEADS_PER_STEP
    n_tiles = win // KEY_TILE
    scale = 1.0 / math.sqrt(HD)

    def kernel(flags_ref, q_ref, do_ref, lse_ref, delta_ref, k_ref, v_ref, kt_ref, bias_ref,
               dq_ref, dk_ref, dv_ref, dqt_scr):
        g = pl.program_id(0)
        b = pl.program_id(1)

        @pl.when(b == 0)
        def _():
            dk_ref[...] = jnp.zeros_like(dk_ref)
            dv_ref[...] = jnp.zeros_like(dv_ref)

        for i in range(HEADS_PER_STEP):
            h = (g * blocks_per_group + b) * HEADS_PER_STEP + i
            cols = slice(i * HD, (i + 1) * HD)
            q = q_ref[:, cols]
            do = do_ref[:, cols]
            lse = lse_ref[pl.ds(h, 1), :]
            dl = delta_ref[pl.ds(h, 1), :]
            dqt_scr[...] = jnp.zeros_like(dqt_scr)

            for j in range(n_tiles):
                def tile(j=j, q=q, do=do, lse=lse, dl=dl):
                    rows = slice(j * KEY_TILE, (j + 1) * KEY_TILE)
                    k = k_ref[rows, :]
                    v = v_ref[rows, :]
                    st = lax.dot_general(k, q, NT_DIMS, preferred_element_type=jnp.float32)
                    p = jnp.exp(st * scale - lse + bias_ref[rows, :])
                    dv_ref[rows, :] += jnp.dot(
                        p.astype(jnp.bfloat16), do, preferred_element_type=jnp.float32)
                    dpt = lax.dot_general(v, do, NT_DIMS, preferred_element_type=jnp.float32)
                    ds = (p * (dpt - dl)).astype(jnp.bfloat16)
                    dk_ref[rows, :] += jnp.dot(ds, q, preferred_element_type=jnp.float32)
                    dqt_scr[...] += jnp.dot(
                        kt_ref[:, rows], ds, preferred_element_type=jnp.float32)

                if j >= diag_tile:
                    tile()
                else:
                    pl.when(flags_ref[j] != 0)(tile)

            dq_ref[:, cols] = (dqt_scr[...] * scale).T.astype(dq_ref.dtype)

    return kernel


def grads_kernel(flags, queries, out_grad, lse, delta, key_win, value_win, key_win_t, bias):
    tok, width = queries.shape
    win, kv_width = key_win.shape
    n_heads = width // HD
    kvh = kv_width // HD
    heads_per_group = n_heads // kvh
    blocks_per_group = heads_per_group // HEADS_PER_STEP
    diag_tile = (win - tok) // KEY_TILE
    kernel = make_kernel(heads_per_group, tok, win, diag_tile)
    hb = HEADS_PER_STEP * HD

    def head_block(g, b, flags_ref):
        return (0, g * blocks_per_group + b)

    def full(g, b, flags_ref):
        return (0, 0)

    def group_cols(g, b, flags_ref):
        return (0, g)

    def group_rows(g, b, flags_ref):
        return (g, 0)

    grid_spec = pltpu.PrefetchScalarGridSpec(
        num_scalar_prefetch=1,
        grid=(kvh, blocks_per_group),
        in_specs=[
            pl.BlockSpec((tok, hb), head_block),
            pl.BlockSpec((tok, hb), head_block),
            pl.BlockSpec((n_heads, tok), full),
            pl.BlockSpec((n_heads, tok), full),
            pl.BlockSpec((win, HD), group_cols),
            pl.BlockSpec((win, HD), group_cols),
            pl.BlockSpec((HD, win), group_rows),
            pl.BlockSpec((win, tok), full),
        ],
        out_specs=[
            pl.BlockSpec((tok, hb), head_block),
            pl.BlockSpec((win, HD), group_cols),
            pl.BlockSpec((win, HD), group_cols),
        ],
        scratch_shapes=[pltpu.VMEM((HD, tok), jnp.float32)],
    )
    return pl.pallas_call(
        kernel,
        grid_spec=grid_spec,
        out_shape=[
            jax.ShapeDtypeStruct((tok, width), jnp.bfloat16),
            jax.ShapeDtypeStruct((win, kv_width), jnp.float32),
            jax.ShapeDtypeStruct((win, kv_width), jnp.float32),
        ],
        compiler_params=pltpu.CompilerParams(
            dimension_semantics=("arbitrary", "arbitrary")),
    )(flags, queries, out_grad, lse, delta, key_win, value_win, key_win_t, bias)


def per_device(queries, keys, values, outputs, out_grad, logsumexp, doc_lengths):
    tok, width = queries.shape
    n_heads = width // HD
    reach = -(-(MOST - 1) // tok)
    win = (reach + 1) * tok
    scale = 1.0 / math.sqrt(HD)
    position = lax.axis_index("seq")
    doc_ends = jnp.cumsum(doc_lengths)

    def doc_of(places):
        return jnp.sum((doc_ends[None, :] <= places[:, None]).astype(jnp.int32), axis=1)

    query_places = position * tok + jnp.arange(tok, dtype=jnp.int32)
    query_ids = doc_of(query_places)
    key_places = (position - reach) * tok + jnp.arange(win, dtype=jnp.int32)
    key_ids = jnp.where(key_places >= 0, doc_of(key_places), -1)
    visible = (key_ids[:, None] == query_ids[None, :]) & (
        key_places[:, None] <= query_places[None, :])
    bias = jnp.where(visible, 0.0, -jnp.inf).astype(jnp.float32)
    n_tiles = win // KEY_TILE
    last_ids = key_ids[KEY_TILE - 1::KEY_TILE]
    diag_tile = (win - tok) // KEY_TILE
    flags = ((last_ids == query_ids[0])
             | (jnp.arange(n_tiles) >= diag_tile)).astype(jnp.int32)

    delta = jnp.sum(
        (out_grad.astype(jnp.float32) * outputs.astype(jnp.float32)).reshape(tok, n_heads, HD),
        axis=2,
    ).T

    key_tiles = [keys]
    value_tiles = [values]
    for hop in range(1, reach + 1):
        moved = shifted((keys, values), "seq", hop)
        key_tiles.append(moved[0])
        value_tiles.append(moved[1])
    key_win = jnp.concatenate(key_tiles[::-1], axis=0)
    value_win = jnp.concatenate(value_tiles[::-1], axis=0)
    key_win_t = key_win.T

    dq, dk_win, dv_win = grads_kernel(
        flags, queries, out_grad, logsumexp, delta, key_win, value_win, key_win_t, bias)

    def piece(arr, hop):
        return arr[(reach - hop) * tok:(reach - hop + 1) * tok]

    key_total = piece(dk_win, 0)
    value_total = piece(dv_win, 0)
    for hop in range(1, reach + 1):
        returned = shifted((piece(dk_win, hop), piece(dv_win, hop)), "seq", -hop)
        key_total = key_total + returned[0]
        value_total = value_total + returned[1]
    return (
        dq,
        (key_total * scale).astype(jnp.bfloat16),
        value_total.astype(jnp.bfloat16),
    )


def solution(mesh):
    in_specs = (
        P(("parts", "seq"), None),
        P(("parts", "seq"), None),
        P(("parts", "seq"), None),
        P(("parts", "seq"), None),
        P(("parts", "seq"), None),
        P(None, ("parts", "seq")),
        P("parts"),
    )
    out_specs = (P(("parts", "seq"), None), P(("parts", "seq"), None), P(("parts", "seq"), None))
    return jax.shard_map(
        per_device, mesh=mesh, in_specs=in_specs, out_specs=out_specs, check_vma=False
    )
```

```python
import math

import jax
import jax.numpy as jnp
from jax import lax
from jax.experimental import pallas as pl
from jax.experimental.pallas import tpu as pltpu
from jax.sharding import PartitionSpec as P

HD = 128
MOST = 512
KEY_TILE = 128
HEADS_PER_STEP = 8
NT_DIMS = (((1,), (1,)), ((), ()))


def shifted(block, axis, distance):
    devices = range(lax.axis_size(axis))
    route = [(i - distance, i) for i in devices if i - distance in devices]
    return lax.ppermute(block, axis, route)


def make_kernel(tok, reach, blocks_per_group):
    hb = HEADS_PER_STEP
    win = (reach + 1) * tok
    n_tiles = win // KEY_TILE
    tiles_per_piece = tok // KEY_TILE
    diag_tile = reach * tiles_per_piece
    scale = 1.0 / math.sqrt(HD)

    def kernel(flags_ref, q_ref, do_ref, o_ref, lse_ref, kid_ref, qid_ref, *rest):
        kv_refs = rest[:reach + 1]
        dq_ref, dkv_ref = rest[reach + 1:reach + 3]
        qs_scr, dos_scr, dqt_scr, kt_scr, bias_scr = rest[reach + 3:]
        g = pl.program_id(0)
        b = pl.program_id(1)

        @pl.when(b == 0)
        def _():
            dkv_ref[...] = jnp.zeros_like(dkv_ref)
            for piece in range(reach + 1):
                kv = kv_refs[reach - piece]
                kt_scr[:, piece * tok:(piece + 1) * tok] = (
                    kv[:, :HD].astype(jnp.float32).T.astype(jnp.bfloat16))

        @pl.when((b == 0) & (g == 0))
        def _():
            key_index = lax.broadcasted_iota(jnp.int32, (win, tok), 0) - reach * tok
            query_index = lax.broadcasted_iota(jnp.int32, (win, tok), 1)
            visible = (kid_ref[...] == qid_ref[...]) & (key_index <= query_index)
            bias_scr[...] = jnp.where(visible, 0.0, -jnp.inf).astype(jnp.float32)

        delta_rows = []
        for i in range(hb):
            cols = slice(i * HD, (i + 1) * HD)
            qs_scr[i * tok:(i + 1) * tok, :] = q_ref[:, cols]
            dos_scr[i * tok:(i + 1) * tok, :] = do_ref[:, cols]
            prod = do_ref[:, cols].astype(jnp.float32) * o_ref[:, cols].astype(jnp.float32)
            delta_rows.append(jnp.sum(prod.T, axis=0, keepdims=True))
        dl_row = jnp.concatenate(delta_rows, axis=1)
        lse_row = jnp.concatenate([lse_ref[i:i + 1, :] for i in range(hb)], axis=1)
        dqt_scr[...] = jnp.zeros_like(dqt_scr)

        for j in range(n_tiles):
            piece = j // tiles_per_piece
            kv = kv_refs[reach - piece]
            r0 = (j % tiles_per_piece) * KEY_TILE
            rows = slice(r0, r0 + KEY_TILE)
            win_rows = slice(j * KEY_TILE, (j + 1) * KEY_TILE)

            def tile(kv=kv, rows=rows, win_rows=win_rows, piece=piece):
                k = kv[rows, :HD]
                v = kv[rows, HD:]
                qs = qs_scr[...]
                dos = dos_scr[...]
                st = lax.dot_general(k, qs, NT_DIMS, preferred_element_type=jnp.float32)
                bias = bias_scr[win_rows, :]
                p = jnp.exp(st * scale - lse_row + jnp.concatenate([bias] * hb, axis=1))
                dv = jnp.dot(p.astype(jnp.bfloat16), dos, preferred_element_type=jnp.float32)
                dpt = lax.dot_general(v, dos, NT_DIMS, preferred_element_type=jnp.float32)
                ds = (p * (dpt - dl_row)).astype(jnp.bfloat16)
                dk = jnp.dot(ds, qs, preferred_element_type=jnp.float32)
                dkv_ref[piece, rows, :HD] += dk
                dkv_ref[piece, rows, HD:] += dv
                dqt_scr[...] += jnp.dot(
                    kt_scr[:, win_rows], ds, preferred_element_type=jnp.float32)

            if j >= diag_tile:
                tile()
            else:
                pl.when(flags_ref[j] != 0)(tile)

        for i in range(hb):
            dq_ref[:, i * HD:(i + 1) * HD] = (
                dqt_scr[:, i * tok:(i + 1) * tok] * scale).T.astype(dq_ref.dtype)

    return kernel


def grads_kernel(flags, queries, out_grad, outputs, lse, kid, qid, kv_pieces, reach):
    tok, width = queries.shape
    n_heads = width // HD
    kvh = kv_pieces[0].shape[1] // (2 * HD)
    heads_per_group = n_heads // kvh
    blocks_per_group = heads_per_group // HEADS_PER_STEP
    win = (reach + 1) * tok
    kernel = make_kernel(tok, reach, blocks_per_group)
    hb = HEADS_PER_STEP

    def head_block(g, b, flags_ref):
        return (0, g * blocks_per_group + b)

    def lse_block(g, b, flags_ref):
        return (g * blocks_per_group + b, 0)

    def full(g, b, flags_ref):
        return (0, 0)

    def group_cols(g, b, flags_ref):
        return (0, g)

    def group_cols3(g, b, flags_ref):
        return (0, 0, g)

    grid_spec = pltpu.PrefetchScalarGridSpec(
        num_scalar_prefetch=1,
        grid=(kvh, blocks_per_group),
        in_specs=[
            pl.BlockSpec((tok, hb * HD), head_block),
            pl.BlockSpec((tok, hb * HD), head_block),
            pl.BlockSpec((tok, hb * HD), head_block),
            pl.BlockSpec((hb, tok), lse_block),
            pl.BlockSpec((win, 1), full),
            pl.BlockSpec((1, tok), full),
        ] + [pl.BlockSpec((tok, 2 * HD), group_cols) for _ in kv_pieces],
        out_specs=[
            pl.BlockSpec((tok, hb * HD), head_block),
            pl.BlockSpec((reach + 1, tok, 2 * HD), group_cols3),
        ],
        scratch_shapes=[
            pltpu.VMEM((hb * tok, HD), jnp.bfloat16),
            pltpu.VMEM((hb * tok, HD), jnp.bfloat16),
            pltpu.VMEM((HD, hb * tok), jnp.float32),
            pltpu.VMEM((HD, win), jnp.bfloat16),
            pltpu.VMEM((win, tok), jnp.float32),
        ],
    )
    return pl.pallas_call(
        kernel,
        grid_spec=grid_spec,
        out_shape=[
            jax.ShapeDtypeStruct((tok, width), jnp.bfloat16),
            jax.ShapeDtypeStruct((reach + 1, tok, kvh * 2 * HD), jnp.float32),
        ],
        compiler_params=pltpu.CompilerParams(
            dimension_semantics=("arbitrary", "arbitrary")),
    )(flags, queries, out_grad, outputs, lse, kid, qid, *kv_pieces)


def per_device(queries, keys, values, outputs, out_grad, logsumexp, doc_lengths):
    tok, width = queries.shape
    kvh = keys.shape[1] // HD
    reach = -(-(MOST - 1) // tok)
    win = (reach + 1) * tok
    scale = 1.0 / math.sqrt(HD)
    position = lax.axis_index("seq")
    doc_ends = jnp.cumsum(doc_lengths)

    def doc_of(places):
        return jnp.sum((doc_ends[None, :] <= places[:, None]).astype(jnp.int32), axis=1)

    query_places = position * tok + jnp.arange(tok, dtype=jnp.int32)
    query_ids = doc_of(query_places)
    key_places = (position - reach) * tok + jnp.arange(win, dtype=jnp.int32)
    key_ids = jnp.where(key_places >= 0, doc_of(key_places), -1)
    n_tiles = win // KEY_TILE
    last_ids = key_ids[KEY_TILE - 1::KEY_TILE]
    diag_tile = reach * tok // KEY_TILE
    flags = ((last_ids == query_ids[0])
             | (jnp.arange(n_tiles) >= diag_tile)).astype(jnp.int32)

    kv = jnp.concatenate(
        [keys.reshape(tok, kvh, 1, HD), values.reshape(tok, kvh, 1, HD)], axis=2
    ).reshape(tok, kvh * 2 * HD)
    kv_pieces = [kv] + [shifted(kv, "seq", hop) for hop in range(1, reach + 1)]

    dq, dkv = grads_kernel(
        flags, queries, out_grad, outputs, logsumexp, key_ids[:, None], query_ids[None, :],
        kv_pieces, reach)

    total = dkv[reach]
    for hop in range(1, reach + 1):
        total = total + shifted(dkv[reach - hop], "seq", -hop)
    total = total.reshape(tok, kvh, 2, HD)
    key_total = total[:, :, 0, :].reshape(tok, kvh * HD)
    value_total = total[:, :, 1, :].reshape(tok, kvh * HD)
    return (
        dq,
        (key_total * scale).astype(jnp.bfloat16),
        value_total.astype(jnp.bfloat16),
    )


def solution(mesh):
    in_specs = (
        P(("parts", "seq"), None),
        P(("parts", "seq"), None),
        P(("parts", "seq"), None),
        P(("parts", "seq"), None),
        P(("parts", "seq"), None),
        P(None, ("parts", "seq")),
        P("parts"),
    )
    out_specs = (P(("parts", "seq"), None), P(("parts", "seq"), None), P(("parts", "seq"), None))
    return jax.shard_map(
        per_device, mesh=mesh, in_specs=in_specs, out_specs=out_specs, check_vma=False
    )
```

```python
import math

import jax
import jax.numpy as jnp
from jax import lax
from jax.experimental import pallas as pl
from jax.experimental.pallas import tpu as pltpu
from jax.sharding import PartitionSpec as P

HD = 128
MOST = 512
KEY_TILE = 128
HEADS_PER_STEP = 8
NT_DIMS = (((1,), (1,)), ((), ()))


def shifted(block, axis, distance):
    devices = range(lax.axis_size(axis))
    route = [(i - distance, i) for i in devices if i - distance in devices]
    return lax.ppermute(block, axis, route)


def make_kernel(tok, reach, remote, dq_in, dq_final, n_alias):
    hb = HEADS_PER_STEP
    pieces = list(range(reach)) if remote else [reach]
    tiles_per_piece = tok // KEY_TILE
    n_rows = len(pieces) * tok
    scale = 1.0 / math.sqrt(HD)

    def kernel(flags_ref, q_ref, do_ref, o_ref, lse_ref, bias_ref, *rest):
        rest = list(rest)
        kv_refs = [rest.pop(0) for _ in pieces]
        dqp_ref = rest.pop(0) if dq_in else None
        rest = rest[n_alias:]
        dq_ref = rest.pop(0)
        dkv_ref = rest.pop(0)
        qs_scr, dos_scr, dqt_scr, kt_scr, acc_scr = rest[-5:]
        b = pl.program_id(0)
        nb = pl.num_programs(0)

        @pl.when(b == 0)
        def _():
            acc_scr[...] = jnp.zeros_like(acc_scr)
            for n, kv in enumerate(kv_refs):
                kt_scr[:, n * tok:(n + 1) * tok] = (
                    kv[:, :HD].astype(jnp.float32).T.astype(jnp.bfloat16))

        delta_rows = []
        for i in range(hb):
            cols = slice(i * HD, (i + 1) * HD)
            qs_scr[i * tok:(i + 1) * tok, :] = q_ref[:, cols]
            dos_scr[i * tok:(i + 1) * tok, :] = do_ref[:, cols]
            prod = do_ref[:, cols].astype(jnp.float32) * o_ref[:, cols].astype(jnp.float32)
            delta_rows.append(jnp.sum(prod.T, axis=0, keepdims=True))
        dl_row = jnp.concatenate(delta_rows, axis=1)
        lse_row = jnp.concatenate([lse_ref[i:i + 1, :] for i in range(hb)], axis=1)
        dqt_scr[...] = jnp.zeros_like(dqt_scr)

        for n, piece in enumerate(pieces):
            kv = kv_refs[n]
            for t in range(tiles_per_piece):
                j = piece * tiles_per_piece + t
                rows = slice(t * KEY_TILE, (t + 1) * KEY_TILE)
                loc_rows = slice(n * tok + t * KEY_TILE, n * tok + (t + 1) * KEY_TILE)

                def tile(kv=kv, rows=rows, loc_rows=loc_rows, n=n):
                    k = kv[rows, :HD]
                    v = kv[rows, HD:]
                    qs = qs_scr[...]
                    dos = dos_scr[...]
                    st = lax.dot_general(k, qs, NT_DIMS, preferred_element_type=jnp.float32)
                    bias = bias_ref[loc_rows, :]
                    p = jnp.exp(st * scale - lse_row + jnp.concatenate([bias] * hb, axis=1))
                    dv = jnp.dot(p.astype(jnp.bfloat16), dos, preferred_element_type=jnp.float32)
                    dpt = lax.dot_general(v, dos, NT_DIMS, preferred_element_type=jnp.float32)
                    ds = (p * (dpt - dl_row)).astype(jnp.bfloat16)
                    dk = jnp.dot(ds, qs, preferred_element_type=jnp.float32)
                    acc_scr[n, rows, :HD] += dk
                    acc_scr[n, rows, HD:] += dv
                    dqt_scr[...] += jnp.dot(
                        kt_scr[:, loc_rows], ds, preferred_element_type=jnp.float32)

                if remote:
                    pl.when(flags_ref[j] != 0)(tile)
                else:
                    tile()

        for i in range(hb):
            cols = slice(i * HD, (i + 1) * HD)
            part = dqt_scr[:, i * tok:(i + 1) * tok].T
            if dq_in:
                part = part + dqp_ref[:, cols]
            if dq_final:
                dq_ref[:, cols] = (part * scale).astype(dq_ref.dtype)
            else:
                dq_ref[:, cols] = part

        @pl.when(b == nb - 1)
        def _():
            dkv_ref[...] = acc_scr[...].astype(dkv_ref.dtype)

    return kernel


def grads_call(group, remote, flags, queries, out_grad, outputs, lse, bias, kv_pieces,
               reach, dq_part=None, dq_alias=None, dkv_alias=None):
    tok, width = queries.shape
    n_heads = width // HD
    kvh = kv_pieces[0].shape[1] // (2 * HD)
    heads_per_group = n_heads // kvh
    hb = HEADS_PER_STEP
    nb = heads_per_group // hb
    dq_final = dq_part is not None
    pieces = list(range(reach)) if remote else [reach]
    n_pieces = len(pieces)

    def head_block(b, f):
        return (0, group * nb + b)

    def lse_block(b, f):
        return (group * nb + b, 0)

    def local_block(b, f):
        return (0, b)

    def bias_block(b, f):
        return (0, 0) if remote else (reach, 0)

    def kv_block(b, f):
        return (0, group)

    in_specs = [
        pl.BlockSpec((tok, hb * HD), head_block),
        pl.BlockSpec((tok, hb * HD), head_block),
        pl.BlockSpec((tok, hb * HD), head_block),
        pl.BlockSpec((hb, tok), lse_block),
        pl.BlockSpec((n_pieces * tok, tok), bias_block),
    ] + [pl.BlockSpec((tok, 2 * HD), kv_block) for _ in pieces]
    args = [queries, out_grad, outputs, lse, bias] + [kv_pieces[reach - p] for p in pieces]
    if dq_part is not None:
        in_specs.append(pl.BlockSpec((tok, hb * HD), local_block))
        args.append(dq_part)
    aliases = {}
    if dq_alias is not None:
        aliases[len(args) + 1] = 0
        in_specs.append(pl.BlockSpec(memory_space=pl.ANY))
        args.append(dq_alias)
    if dkv_alias is not None:
        aliases[len(args) + 1] = 1
        in_specs.append(pl.BlockSpec(memory_space=pl.ANY))
        args.append(dkv_alias)

    kernel = make_kernel(tok, reach, remote, dq_part is not None, dq_final, len(aliases))
    if dq_final:
        dq_shape = jax.ShapeDtypeStruct((tok, width), jnp.bfloat16)
        dq_spec = pl.BlockSpec((tok, hb * HD), head_block)
    else:
        dq_shape = jax.ShapeDtypeStruct((tok, heads_per_group * HD), jnp.float32)
        dq_spec = pl.BlockSpec((tok, hb * HD), local_block)
    if remote:
        dkv_shape = jax.ShapeDtypeStruct((n_pieces, tok, kvh * 2 * HD), jnp.bfloat16)
        dkv_spec = pl.BlockSpec((n_pieces, tok, 2 * HD), lambda b, f: (0, 0, group))
    else:
        dkv_shape = jax.ShapeDtypeStruct((n_pieces, tok, 2 * HD), jnp.float32)
        dkv_spec = pl.BlockSpec((n_pieces, tok, 2 * HD), lambda b, f: (0, 0, 0))

    grid_spec = pltpu.PrefetchScalarGridSpec(
        num_scalar_prefetch=1,
        grid=(nb,),
        in_specs=in_specs,
        out_specs=[dq_spec, dkv_spec],
        scratch_shapes=[
            pltpu.VMEM((hb * tok, HD), jnp.bfloat16),
            pltpu.VMEM((hb * tok, HD), jnp.bfloat16),
            pltpu.VMEM((HD, hb * tok), jnp.float32),
            pltpu.VMEM((HD, n_pieces * tok), jnp.bfloat16),
            pltpu.VMEM((n_pieces, tok, 2 * HD), jnp.float32),
        ],
    )
    return pl.pallas_call(
        kernel,
        grid_spec=grid_spec,
        out_shape=[dq_shape, dkv_shape],
        input_output_aliases=aliases,
        compiler_params=pltpu.CompilerParams(dimension_semantics=("arbitrary",)),
    )(flags, *args)


def per_device(queries, keys, values, outputs, out_grad, logsumexp, doc_lengths):
    tok, width = queries.shape
    kvh = keys.shape[1] // HD
    reach = -(-(MOST - 1) // tok)
    win = (reach + 1) * tok
    scale = 1.0 / math.sqrt(HD)
    position = lax.axis_index("seq")
    doc_ends = jnp.cumsum(doc_lengths)

    def doc_of(places):
        return jnp.sum((doc_ends[None, :] <= places[:, None]).astype(jnp.int32), axis=1)

    query_places = position * tok + jnp.arange(tok, dtype=jnp.int32)
    query_ids = doc_of(query_places)
    key_places = (position - reach) * tok + jnp.arange(win, dtype=jnp.int32)
    key_ids = jnp.where(key_places >= 0, doc_of(key_places), -1)
    visible = (key_ids[:, None] == query_ids[None, :]) & (
        key_places[:, None] <= query_places[None, :])
    bias = jnp.where(visible, 0.0, -jnp.inf).astype(jnp.float32)
    n_tiles = win // KEY_TILE
    last_places = (position - reach) * tok + KEY_TILE * jnp.arange(
        1, n_tiles + 1, dtype=jnp.int32) - 1
    first_doc = doc_of(position[None] * tok)
    flags = ((doc_of(last_places) == first_doc) & (last_places >= 0)).astype(jnp.int32)

    kv = jnp.concatenate(
        [keys.reshape(tok, kvh, 1, HD), values.reshape(tok, kvh, 1, HD)], axis=2
    ).reshape(tok, kvh * 2 * HD)
    kv_pieces = [kv] + [shifted(kv, "seq", hop) for hop in range(1, reach + 1)]
    common = (flags, queries, out_grad, outputs, logsumexp, bias, kv_pieces, reach)

    dq_part0, dkv_own0 = grads_call(0, False, *common)
    dq, dkv_rem = grads_call(0, True, *common, dq_part=dq_part0)
    dq_part1, dkv_rem = grads_call(1, True, *common, dkv_alias=dkv_rem)
    returned = [shifted(dkv_rem[reach - hop], "seq", -hop) for hop in range(1, reach + 1)]
    dq, dkv_own1 = grads_call(1, False, *common, dq_part=dq_part1, dq_alias=dq)

    total = jnp.concatenate([dkv_own0[0], dkv_own1[0]], axis=1)
    for r in returned:
        total = total + r.astype(jnp.float32)
    total = total.reshape(tok, kvh, 2, HD)
    key_total = total[:, :, 0, :].reshape(tok, kvh * HD)
    value_total = total[:, :, 1, :].reshape(tok, kvh * HD)
    return (
        dq,
        (key_total * scale).astype(jnp.bfloat16),
        value_total.astype(jnp.bfloat16),
    )


def solution(mesh):
    in_specs = (
        P(("parts", "seq"), None),
        P(("parts", "seq"), None),
        P(("parts", "seq"), None),
        P(("parts", "seq"), None),
        P(("parts", "seq"), None),
        P(None, ("parts", "seq")),
        P("parts"),
    )
    out_specs = (P(("parts", "seq"), None), P(("parts", "seq"), None), P(("parts", "seq"), None))
    return jax.shard_map(
        per_device, mesh=mesh, in_specs=in_specs, out_specs=out_specs, check_vma=False
    )
```

```python
import math

import jax
import jax.numpy as jnp
from jax import lax
from jax.experimental import pallas as pl
from jax.experimental.pallas import tpu as pltpu
from jax.sharding import PartitionSpec as P

HD = 128
MOST = 512
KEY_TILE = 128
HEADS_PER_STEP = 8
NT_DIMS = (((1,), (1,)), ((), ()))


def shifted(block, axis, distance):
    devices = range(lax.axis_size(axis))
    route = [(i - distance, i) for i in devices if i - distance in devices]
    return lax.ppermute(block, axis, route)


def make_kernel(tok, reach, remote, dq_in, dq_final, n_alias):
    hb = HEADS_PER_STEP
    pieces = list(range(reach)) if remote else [reach]
    tiles_per_piece = tok // KEY_TILE
    scale = 1.0 / math.sqrt(HD)

    def kernel(flags_ref, q_ref, do_ref, o_ref, lse_ref, bias_ref, *rest):
        rest = list(rest)
        kv_refs = [rest.pop(0) for _ in pieces]
        dqp_ref = rest.pop(0) if dq_in else None
        rest = rest[n_alias:]
        dq_ref = rest.pop(0)
        dkv_ref = rest.pop(0)
        qs_scr, dos_scr, dl_scr, ds_scr, dq_scr, kt_scr, acc_scr = rest[-7:]
        b = pl.program_id(0)
        nb = pl.num_programs(0)

        @pl.when(b == 0)
        def _():
            acc_scr[...] = jnp.zeros_like(acc_scr)
            for n, kv in enumerate(kv_refs):
                kt_scr[:, n * tok:(n + 1) * tok] = (
                    kv[:, :HD].astype(jnp.float32).T.astype(jnp.bfloat16))

        for i in range(hb):
            cols = slice(i * HD, (i + 1) * HD)
            qs_scr[i * tok:(i + 1) * tok, :] = q_ref[:, cols]
            dos_scr[i * tok:(i + 1) * tok, :] = do_ref[:, cols]
            prod = do_ref[:, cols].astype(jnp.float32) * o_ref[:, cols].astype(jnp.float32)
            dl_scr[i:i + 1, :] = jnp.sum(prod.T, axis=0, keepdims=True)

        def head(i, carry):
            r0 = pl.multiple_of(i * tok, tok)
            q = qs_scr[pl.ds(r0, tok), :]
            do = dos_scr[pl.ds(r0, tok), :]
            lse = lse_ref[pl.ds(i, 1), :]
            dl = dl_scr[pl.ds(i, 1), :]
            for n, piece in enumerate(pieces):
                kv = kv_refs[n]
                for t in range(tiles_per_piece):
                    j = piece * tiles_per_piece + t
                    rows = slice(t * KEY_TILE, (t + 1) * KEY_TILE)
                    loc_rows = slice(n * tok + t * KEY_TILE, n * tok + (t + 1) * KEY_TILE)

                    def tile(kv=kv, rows=rows, loc_rows=loc_rows, n=n):
                        k = kv[rows, :HD]
                        v = kv[rows, HD:]
                        st = lax.dot_general(k, q, NT_DIMS, preferred_element_type=jnp.float32)
                        p = jnp.exp(st * scale - lse + bias_ref[loc_rows, :])
                        acc_scr[n, rows, HD:] += jnp.dot(
                            p.astype(jnp.bfloat16), do, preferred_element_type=jnp.float32)
                        dpt = lax.dot_general(v, do, NT_DIMS, preferred_element_type=jnp.float32)
                        ds = (p * (dpt - dl)).astype(jnp.bfloat16)
                        acc_scr[n, rows, :HD] += jnp.dot(
                            ds, q, preferred_element_type=jnp.float32)
                        ds_scr[loc_rows, :] = ds

                    def skip(loc_rows=loc_rows):
                        ds_scr[loc_rows, :] = jnp.zeros((KEY_TILE, tok), jnp.bfloat16)

                    if remote:
                        pl.when(flags_ref[j] != 0)(tile)
                        pl.when(flags_ref[j] == 0)(skip)
                    else:
                        tile()
            dqt = jnp.dot(kt_scr[...], ds_scr[...], preferred_element_type=jnp.float32)
            dq_scr[pl.ds(r0, tok), :] = dqt.T
            return carry

        lax.fori_loop(0, hb, head, 0)

        for i in range(hb):
            cols = slice(i * HD, (i + 1) * HD)
            part = dq_scr[i * tok:(i + 1) * tok, :]
            if dq_in:
                part = part + dqp_ref[:, cols]
            if dq_final:
                dq_ref[:, cols] = (part * scale).astype(dq_ref.dtype)
            else:
                dq_ref[:, cols] = part

        @pl.when(b == nb - 1)
        def _():
            dkv_ref[...] = acc_scr[...].astype(dkv_ref.dtype)

    return kernel


def grads_call(group, remote, flags, queries, out_grad, outputs, lse, bias, kv_pieces,
               reach, dq_part=None, dq_alias=None, dkv_alias=None):
    tok, width = queries.shape
    n_heads = width // HD
    kvh = kv_pieces[0].shape[1] // (2 * HD)
    heads_per_group = n_heads // kvh
    hb = HEADS_PER_STEP
    nb = heads_per_group // hb
    dq_final = dq_part is not None
    pieces = list(range(reach)) if remote else [reach]
    n_pieces = len(pieces)

    def head_block(b, f):
        return (0, group * nb + b)

    def lse_block(b, f):
        return (group * nb + b, 0)

    def local_block(b, f):
        return (0, b)

    def bias_block(b, f):
        return (0, 0) if remote else (reach, 0)

    def kv_block(b, f):
        return (0, group)

    in_specs = [
        pl.BlockSpec((tok, hb * HD), head_block),
        pl.BlockSpec((tok, hb * HD), head_block),
        pl.BlockSpec((tok, hb * HD), head_block),
        pl.BlockSpec((hb, tok), lse_block),
        pl.BlockSpec((n_pieces * tok, tok), bias_block),
    ] + [pl.BlockSpec((tok, 2 * HD), kv_block) for _ in pieces]
    args = [queries, out_grad, outputs, lse, bias] + [kv_pieces[reach - p] for p in pieces]
    if dq_part is not None:
        in_specs.append(pl.BlockSpec((tok, hb * HD), local_block))
        args.append(dq_part)
    aliases = {}
    if dq_alias is not None:
        aliases[len(args) + 1] = 0
        in_specs.append(pl.BlockSpec(memory_space=pl.ANY))
        args.append(dq_alias)
    if dkv_alias is not None:
        aliases[len(args) + 1] = 1
        in_specs.append(pl.BlockSpec(memory_space=pl.ANY))
        args.append(dkv_alias)

    kernel = make_kernel(tok, reach, remote, dq_part is not None, dq_final, len(aliases))
    if dq_final:
        dq_shape = jax.ShapeDtypeStruct((tok, width), jnp.bfloat16)
        dq_spec = pl.BlockSpec((tok, hb * HD), head_block)
    else:
        dq_shape = jax.ShapeDtypeStruct((tok, heads_per_group * HD), jnp.float32)
        dq_spec = pl.BlockSpec((tok, hb * HD), local_block)
    if remote:
        dkv_shape = jax.ShapeDtypeStruct((n_pieces, tok, kvh * 2 * HD), jnp.bfloat16)
        dkv_spec = pl.BlockSpec((n_pieces, tok, 2 * HD), lambda b, f: (0, 0, group))
    else:
        dkv_shape = jax.ShapeDtypeStruct((n_pieces, tok, 2 * HD), jnp.float32)
        dkv_spec = pl.BlockSpec((n_pieces, tok, 2 * HD), lambda b, f: (0, 0, 0))

    grid_spec = pltpu.PrefetchScalarGridSpec(
        num_scalar_prefetch=1,
        grid=(nb,),
        in_specs=in_specs,
        out_specs=[dq_spec, dkv_spec],
        scratch_shapes=[
            pltpu.VMEM((hb * tok, HD), jnp.bfloat16),
            pltpu.VMEM((hb * tok, HD), jnp.bfloat16),
            pltpu.VMEM((hb, tok), jnp.float32),
            pltpu.VMEM((n_pieces * tok, tok), jnp.bfloat16),
            pltpu.VMEM((hb * tok, HD), jnp.float32),
            pltpu.VMEM((HD, n_pieces * tok), jnp.bfloat16),
            pltpu.VMEM((n_pieces, tok, 2 * HD), jnp.float32),
        ],
    )
    return pl.pallas_call(
        kernel,
        grid_spec=grid_spec,
        out_shape=[dq_shape, dkv_shape],
        input_output_aliases=aliases,
        compiler_params=pltpu.CompilerParams(dimension_semantics=("arbitrary",)),
    )(flags, *args)


def per_device(queries, keys, values, outputs, out_grad, logsumexp, doc_lengths):
    tok, width = queries.shape
    kvh = keys.shape[1] // HD
    reach = -(-(MOST - 1) // tok)
    win = (reach + 1) * tok
    scale = 1.0 / math.sqrt(HD)
    position = lax.axis_index("seq")
    doc_ends = jnp.cumsum(doc_lengths)

    def doc_of(places):
        return jnp.sum((doc_ends[None, :] <= places[:, None]).astype(jnp.int32), axis=1)

    query_places = position * tok + jnp.arange(tok, dtype=jnp.int32)
    query_ids = doc_of(query_places)
    key_places = (position - reach) * tok + jnp.arange(win, dtype=jnp.int32)
    key_ids = jnp.where(key_places >= 0, doc_of(key_places), -1)
    visible = (key_ids[:, None] == query_ids[None, :]) & (
        key_places[:, None] <= query_places[None, :])
    bias = jnp.where(visible, 0.0, -jnp.inf).astype(jnp.float32)
    n_tiles = win // KEY_TILE
    last_places = (position - reach) * tok + KEY_TILE * jnp.arange(
        1, n_tiles + 1, dtype=jnp.int32) - 1
    first_doc = doc_of(position[None] * tok)
    flags = ((doc_of(last_places) == first_doc) & (last_places >= 0)).astype(jnp.int32)

    kv = jnp.concatenate(
        [keys.reshape(tok, kvh, 1, HD), values.reshape(tok, kvh, 1, HD)], axis=2
    ).reshape(tok, kvh * 2 * HD)
    kv_pieces = [kv] + [shifted(kv, "seq", hop) for hop in range(1, reach + 1)]
    common = (flags, queries, out_grad, outputs, logsumexp, bias, kv_pieces, reach)

    dq_part0, dkv_own0 = grads_call(0, False, *common)
    dq, dkv_rem = grads_call(0, True, *common, dq_part=dq_part0)
    dq_part1, dkv_rem = grads_call(1, True, *common, dkv_alias=dkv_rem)
    returned = [shifted(dkv_rem[reach - hop], "seq", -hop) for hop in range(1, reach + 1)]
    dq, dkv_own1 = grads_call(1, False, *common, dq_part=dq_part1, dq_alias=dq)

    total = jnp.concatenate([dkv_own0[0], dkv_own1[0]], axis=1)
    for r in returned:
        total = total + r.astype(jnp.float32)
    total = total.reshape(tok, kvh, 2, HD)
    key_total = total[:, :, 0, :].reshape(tok, kvh * HD)
    value_total = total[:, :, 1, :].reshape(tok, kvh * HD)
    return (
        dq,
        (key_total * scale).astype(jnp.bfloat16),
        value_total.astype(jnp.bfloat16),
    )


def solution(mesh):
    in_specs = (
        P(("parts", "seq"), None),
        P(("parts", "seq"), None),
        P(("parts", "seq"), None),
        P(("parts", "seq"), None),
        P(("parts", "seq"), None),
        P(None, ("parts", "seq")),
        P("parts"),
    )
    out_specs = (P(("parts", "seq"), None), P(("parts", "seq"), None), P(("parts", "seq"), None))
    return jax.shard_map(
        per_device, mesh=mesh, in_specs=in_specs, out_specs=out_specs, check_vma=False
    )
```

```python
import math

import jax
import jax.numpy as jnp
from jax import lax
from jax.experimental import pallas as pl
from jax.experimental.pallas import tpu as pltpu
from jax.sharding import PartitionSpec as P

HD = 128
MOST = 512
KEY_TILE = 128
HEADS_PER_STEP = 8
NT_DIMS = (((1,), (1,)), ((), ()))


def shifted(block, axis, distance):
    devices = range(lax.axis_size(axis))
    route = [(i - distance, i) for i in devices if i - distance in devices]
    return lax.ppermute(block, axis, route)


def make_kernel(tok, reach, remote, dq_in, dq_final, n_alias):
    hb = HEADS_PER_STEP
    pieces = list(range(reach)) if remote else [reach]
    tiles_per_piece = tok // KEY_TILE
    sentinel = (reach + 1) * tiles_per_piece
    scale = 1.0 / math.sqrt(HD)

    def kernel(flags_ref, q_ref, do_ref, o_ref, lse_ref, bias_ref, *rest):
        rest = list(rest)
        kv_refs = [rest.pop(0) for _ in pieces]
        dqp_ref = rest.pop(0) if dq_in else None
        rest = rest[n_alias:]
        dq_ref = rest.pop(0)
        dkv_ref = rest.pop(0)
        qs_scr, dos_scr, dl_scr, p_scr, ds_scr, kt_scr, acc_scr = rest[-7:]
        b = pl.program_id(0)
        nb = pl.num_programs(0)
        always = flags_ref[sentinel] != 0

        @pl.when(b == 0)
        def _():
            acc_scr[...] = jnp.zeros_like(acc_scr)
            for n, kv in enumerate(kv_refs):
                kt_scr[:, n * tok:(n + 1) * tok] = (
                    kv[:, :HD].astype(jnp.float32).T.astype(jnp.bfloat16))

        for i in range(hb):
            cols = slice(i * HD, (i + 1) * HD)
            qs_scr[i * tok:(i + 1) * tok, :] = q_ref[:, cols]
            dos_scr[i * tok:(i + 1) * tok, :] = do_ref[:, cols]
            prod = do_ref[:, cols].astype(jnp.float32) * o_ref[:, cols].astype(jnp.float32)
            dl_scr[i:i + 1, :] = jnp.sum(prod.T, axis=0, keepdims=True)

        for n, piece in enumerate(pieces):
            kv = kv_refs[n]
            for t in range(tiles_per_piece):
                j = piece * tiles_per_piece + t
                rows = slice(t * KEY_TILE, (t + 1) * KEY_TILE)
                loc_rows = slice(n * tok + t * KEY_TILE, n * tok + (t + 1) * KEY_TILE)

                def tile(kv=kv, rows=rows, loc_rows=loc_rows, n=n):
                    k = kv[rows, :HD]
                    v = kv[rows, HD:]
                    for i in range(hb):
                        cols = slice(i * HD, (i + 1) * HD)
                        qcols = slice(i * tok, (i + 1) * tok)
                        st = lax.dot_general(
                            k, q_ref[:, cols], NT_DIMS, preferred_element_type=jnp.float32)
                        p = jnp.exp(st * scale - lse_ref[i:i + 1, :] + bias_ref[loc_rows, :])
                        p_scr[:, qcols] = p.astype(jnp.bfloat16)
                        dpt = lax.dot_general(
                            v, do_ref[:, cols], NT_DIMS, preferred_element_type=jnp.float32)
                        ds_scr[loc_rows, qcols] = (
                            p * (dpt - dl_scr[i:i + 1, :])).astype(jnp.bfloat16)

                    @pl.when(always)
                    def _():
                        acc_scr[n, rows, HD:] += jnp.dot(
                            p_scr[...], dos_scr[...], preferred_element_type=jnp.float32)
                        acc_scr[n, rows, :HD] += jnp.dot(
                            ds_scr[loc_rows, :], qs_scr[...], preferred_element_type=jnp.float32)

                def skip(loc_rows=loc_rows):
                    ds_scr[loc_rows, :] = jnp.zeros((KEY_TILE, hb * tok), jnp.bfloat16)

                pl.when(flags_ref[j] != 0)(tile)
                if remote:
                    pl.when(flags_ref[j] == 0)(skip)

        @pl.when(always)
        def _():
            for i in range(hb):
                cols = slice(i * HD, (i + 1) * HD)
                dqt = jnp.dot(kt_scr[...], ds_scr[:, i * tok:(i + 1) * tok],
                              preferred_element_type=jnp.float32)
                part = dqt.T
                if dq_in:
                    part = part + dqp_ref[:, cols]
                if dq_final:
                    dq_ref[:, cols] = (part * scale).astype(dq_ref.dtype)
                else:
                    dq_ref[:, cols] = part

        @pl.when(b == nb - 1)
        def _():
            dkv_ref[...] = acc_scr[...].astype(dkv_ref.dtype)

    return kernel


def grads_call(group, remote, flags, queries, out_grad, outputs, lse, bias, kv_pieces,
               reach, dq_part=None, dq_alias=None, dkv_alias=None):
    tok, width = queries.shape
    n_heads = width // HD
    kvh = kv_pieces[0].shape[1] // (2 * HD)
    heads_per_group = n_heads // kvh
    hb = HEADS_PER_STEP
    nb = heads_per_group // hb
    dq_final = dq_part is not None
    pieces = list(range(reach)) if remote else [reach]
    n_pieces = len(pieces)

    def head_block(b, f):
        return (0, group * nb + b)

    def lse_block(b, f):
        return (group * nb + b, 0)

    def local_block(b, f):
        return (0, b)

    def bias_block(b, f):
        return (0, 0) if remote else (reach, 0)

    def kv_block(b, f):
        return (0, group)

    in_specs = [
        pl.BlockSpec((tok, hb * HD), head_block),
        pl.BlockSpec((tok, hb * HD), head_block),
        pl.BlockSpec((tok, hb * HD), head_block),
        pl.BlockSpec((hb, tok), lse_block),
        pl.BlockSpec((n_pieces * tok, tok), bias_block),
    ] + [pl.BlockSpec((tok, 2 * HD), kv_block) for _ in pieces]
    args = [queries, out_grad, outputs, lse, bias] + [kv_pieces[reach - p] for p in pieces]
    if dq_part is not None:
        in_specs.append(pl.BlockSpec((tok, hb * HD), local_block))
        args.append(dq_part)
    aliases = {}
    if dq_alias is not None:
        aliases[len(args) + 1] = 0
        in_specs.append(pl.BlockSpec(memory_space=pl.ANY))
        args.append(dq_alias)
    if dkv_alias is not None:
        aliases[len(args) + 1] = 1
        in_specs.append(pl.BlockSpec(memory_space=pl.ANY))
        args.append(dkv_alias)

    kernel = make_kernel(tok, reach, remote, dq_part is not None, dq_final, len(aliases))
    if dq_final:
        dq_shape = jax.ShapeDtypeStruct((tok, width), jnp.bfloat16)
        dq_spec = pl.BlockSpec((tok, hb * HD), head_block)
    else:
        dq_shape = jax.ShapeDtypeStruct((tok, heads_per_group * HD), jnp.float32)
        dq_spec = pl.BlockSpec((tok, hb * HD), local_block)
    if remote:
        dkv_shape = jax.ShapeDtypeStruct((n_pieces, tok, kvh * 2 * HD), jnp.bfloat16)
        dkv_spec = pl.BlockSpec((n_pieces, tok, 2 * HD), lambda b, f: (0, 0, group))
    else:
        dkv_shape = jax.ShapeDtypeStruct((n_pieces, tok, 2 * HD), jnp.float32)
        dkv_spec = pl.BlockSpec((n_pieces, tok, 2 * HD), lambda b, f: (0, 0, 0))

    grid_spec = pltpu.PrefetchScalarGridSpec(
        num_scalar_prefetch=1,
        grid=(nb,),
        in_specs=in_specs,
        out_specs=[dq_spec, dkv_spec],
        scratch_shapes=[
            pltpu.VMEM((hb * tok, HD), jnp.bfloat16),
            pltpu.VMEM((hb * tok, HD), jnp.bfloat16),
            pltpu.VMEM((hb, tok), jnp.float32),
            pltpu.VMEM((KEY_TILE, hb * tok), jnp.bfloat16),
            pltpu.VMEM((n_pieces * tok, hb * tok), jnp.bfloat16),
            pltpu.VMEM((HD, n_pieces * tok), jnp.bfloat16),
            pltpu.VMEM((n_pieces, tok, 2 * HD), jnp.float32),
        ],
    )
    return pl.pallas_call(
        kernel,
        grid_spec=grid_spec,
        out_shape=[dq_shape, dkv_shape],
        input_output_aliases=aliases,
        compiler_params=pltpu.CompilerParams(dimension_semantics=("arbitrary",)),
    )(flags, *args)


def per_device(queries, keys, values, outputs, out_grad, logsumexp, doc_lengths):
    tok, width = queries.shape
    kvh = keys.shape[1] // HD
    reach = -(-(MOST - 1) // tok)
    win = (reach + 1) * tok
    scale = 1.0 / math.sqrt(HD)
    position = lax.axis_index("seq")
    doc_ends = jnp.cumsum(doc_lengths)

    def doc_of(places):
        return jnp.sum((doc_ends[None, :] <= places[:, None]).astype(jnp.int32), axis=1)

    query_places = position * tok + jnp.arange(tok, dtype=jnp.int32)
    query_ids = doc_of(query_places)
    key_places = (position - reach) * tok + jnp.arange(win, dtype=jnp.int32)
    key_ids = jnp.where(key_places >= 0, doc_of(key_places), -1)
    visible = (key_ids[:, None] == query_ids[None, :]) & (
        key_places[:, None] <= query_places[None, :])
    bias = jnp.where(visible, 0.0, -jnp.inf).astype(jnp.float32)
    n_tiles = win // KEY_TILE
    last_places = (position - reach) * tok + KEY_TILE * jnp.arange(
        1, n_tiles + 1, dtype=jnp.int32) - 1
    first_doc = doc_of(position[None] * tok)
    flags = jnp.concatenate([
        ((doc_of(last_places) == first_doc) & (last_places >= 0))
        | (jnp.arange(n_tiles) >= reach * tok // KEY_TILE),
        jnp.ones((1,), jnp.bool_)]).astype(jnp.int32)

    kv = jnp.concatenate(
        [keys.reshape(tok, kvh, 1, HD), values.reshape(tok, kvh, 1, HD)], axis=2
    ).reshape(tok, kvh * 2 * HD)
    kv_pieces = [kv] + [shifted(kv, "seq", hop) for hop in range(1, reach + 1)]
    common = (flags, queries, out_grad, outputs, logsumexp, bias, kv_pieces, reach)

    dq_part0, dkv_own0 = grads_call(0, False, *common)
    dq, dkv_rem = grads_call(0, True, *common, dq_part=dq_part0)
    dq_part1, dkv_rem = grads_call(1, True, *common, dkv_alias=dkv_rem)
    returned = [shifted(dkv_rem[reach - hop], "seq", -hop) for hop in range(1, reach + 1)]
    dq, dkv_own1 = grads_call(1, False, *common, dq_part=dq_part1, dq_alias=dq)

    total = jnp.concatenate([dkv_own0[0], dkv_own1[0]], axis=1)
    for r in returned:
        total = total + r.astype(jnp.float32)
    total = total.reshape(tok, kvh, 2, HD)
    key_total = total[:, :, 0, :].reshape(tok, kvh * HD)
    value_total = total[:, :, 1, :].reshape(tok, kvh * HD)
    return (
        dq,
        (key_total * scale).astype(jnp.bfloat16),
        value_total.astype(jnp.bfloat16),
    )


def solution(mesh):
    in_specs = (
        P(("parts", "seq"), None),
        P(("parts", "seq"), None),
        P(("parts", "seq"), None),
        P(("parts", "seq"), None),
        P(("parts", "seq"), None),
        P(None, ("parts", "seq")),
        P("parts"),
    )
    out_specs = (P(("parts", "seq"), None), P(("parts", "seq"), None), P(("parts", "seq"), None))
    return jax.shard_map(
        per_device, mesh=mesh, in_specs=in_specs, out_specs=out_specs, check_vma=False
    )
```

```python
import math

import jax
import jax.numpy as jnp
from jax import lax
from jax.experimental import pallas as pl
from jax.experimental.pallas import tpu as pltpu
from jax.sharding import PartitionSpec as P

HD = 128
MOST = 512
KEY_TILE = 128
HEADS_PER_STEP = 8
NT_DIMS = (((1,), (1,)), ((), ()))


def shifted(block, axis, distance):
    devices = range(lax.axis_size(axis))
    route = [(i - distance, i) for i in devices if i - distance in devices]
    return lax.ppermute(block, axis, route)


def make_kernel(tok, reach, remote, dq_in, dq_final, n_alias):
    hb = HEADS_PER_STEP
    pieces = list(range(reach)) if remote else [reach]
    tiles_per_piece = tok // KEY_TILE
    n_rows = len(pieces) * tok
    scale = 1.0 / math.sqrt(HD)

    def kernel(flags_ref, q_ref, do_ref, o_ref, lse_ref, bias_ref, *rest):
        rest = list(rest)
        kv_refs = [rest.pop(0) for _ in pieces]
        dqp_ref = rest.pop(0) if dq_in else None
        rest = rest[n_alias:]
        dq_ref = rest.pop(0)
        dkv_ref = rest.pop(0)
        qs_scr, dos_scr, dqt_scr, kt_scr, acc_scr = rest[-5:]
        b = pl.program_id(0)
        nb = pl.num_programs(0)

        @pl.when(b == 0)
        def _():
            acc_scr[...] = jnp.zeros_like(acc_scr)
            for n, kv in enumerate(kv_refs):
                kt_scr[:, n * tok:(n + 1) * tok] = (
                    kv[:, :HD].astype(jnp.float32).T.astype(jnp.bfloat16))

        delta_rows = []
        for i in range(hb):
            cols = slice(i * HD, (i + 1) * HD)
            qs_scr[i * tok:(i + 1) * tok, :] = q_ref[:, cols]
            dos_scr[i * tok:(i + 1) * tok, :] = do_ref[:, cols]
            prod = do_ref[:, cols].astype(jnp.float32) * o_ref[:, cols].astype(jnp.float32)
            delta_rows.append(jnp.sum(prod.T, axis=0, keepdims=True))
        dl_row = jnp.concatenate(delta_rows, axis=1)
        lse_row = jnp.concatenate([lse_ref[i:i + 1, :] for i in range(hb)], axis=1)
        dqt_scr[...] = jnp.zeros_like(dqt_scr)

        for n, piece in enumerate(pieces):
            kv = kv_refs[n]
            for t in range(tiles_per_piece):
                j = piece * tiles_per_piece + t
                rows = slice(t * KEY_TILE, (t + 1) * KEY_TILE)
                loc_rows = slice(n * tok + t * KEY_TILE, n * tok + (t + 1) * KEY_TILE)

                def tile(kv=kv, rows=rows, loc_rows=loc_rows, n=n):
                    k = kv[rows, :HD]
                    v = kv[rows, HD:]
                    qs = qs_scr[...]
                    dos = dos_scr[...]
                    st = lax.dot_general(k, qs, NT_DIMS, preferred_element_type=jnp.float32)
                    bias = bias_ref[loc_rows, :]
                    p = jnp.exp(st * scale - lse_row + jnp.concatenate([bias] * hb, axis=1))
                    dv = jnp.dot(p.astype(jnp.bfloat16), dos, preferred_element_type=jnp.float32)
                    dpt = lax.dot_general(v, dos, NT_DIMS, preferred_element_type=jnp.float32)
                    ds = (p * (dpt - dl_row)).astype(jnp.bfloat16)
                    dk = jnp.dot(ds, qs, preferred_element_type=jnp.float32)
                    acc_scr[n, rows, :HD] += dk
                    acc_scr[n, rows, HD:] += dv
                    dqt_scr[...] += jnp.dot(
                        kt_scr[:, loc_rows], ds, preferred_element_type=jnp.float32)

                if remote:
                    pl.when(flags_ref[j] != 0)(tile)
                else:
                    tile()

        for i in range(hb):
            cols = slice(i * HD, (i + 1) * HD)
            part = dqt_scr[:, i * tok:(i + 1) * tok].T
            if dq_in:
                part = part + dqp_ref[:, cols]
            if dq_final:
                dq_ref[:, cols] = (part * scale).astype(dq_ref.dtype)
            else:
                dq_ref[:, cols] = part

        @pl.when(b == nb - 1)
        def _():
            dkv_ref[...] = acc_scr[...].astype(dkv_ref.dtype)

    return kernel


def grads_call(group, remote, flags, queries, out_grad, outputs, lse, bias, kv_pieces,
               reach, dq_part=None, dq_alias=None, dkv_alias=None):
    tok, width = queries.shape
    n_heads = width // HD
    kvh = kv_pieces[0].shape[1] // (2 * HD)
    heads_per_group = n_heads // kvh
    hb = HEADS_PER_STEP
    nb = heads_per_group // hb
    dq_final = dq_part is not None
    pieces = list(range(reach)) if remote else [reach]
    n_pieces = len(pieces)

    def head_block(b, f):
        return (0, group * nb + b)

    def lse_block(b, f):
        return (group * nb + b, 0)

    def local_block(b, f):
        return (0, b)

    def bias_block(b, f):
        return (0, 0) if remote else (reach, 0)

    def kv_block(b, f):
        return (0, group)

    in_specs = [
        pl.BlockSpec((tok, hb * HD), head_block),
        pl.BlockSpec((tok, hb * HD), head_block),
        pl.BlockSpec((tok, hb * HD), head_block),
        pl.BlockSpec((hb, tok), lse_block),
        pl.BlockSpec((n_pieces * tok, tok), bias_block),
    ] + [pl.BlockSpec((tok, 2 * HD), kv_block) for _ in pieces]
    args = [queries, out_grad, outputs, lse, bias] + [kv_pieces[reach - p] for p in pieces]
    if dq_part is not None:
        in_specs.append(pl.BlockSpec((tok, hb * HD), local_block))
        args.append(dq_part)
    aliases = {}
    if dq_alias is not None:
        aliases[len(args) + 1] = 0
        in_specs.append(pl.BlockSpec(memory_space=pl.ANY))
        args.append(dq_alias)
    if dkv_alias is not None:
        aliases[len(args) + 1] = 1
        in_specs.append(pl.BlockSpec(memory_space=pl.ANY))
        args.append(dkv_alias)

    kernel = make_kernel(tok, reach, remote, dq_part is not None, dq_final, len(aliases))
    if dq_final:
        dq_shape = jax.ShapeDtypeStruct((tok, width), jnp.bfloat16)
        dq_spec = pl.BlockSpec((tok, hb * HD), head_block)
    else:
        dq_shape = jax.ShapeDtypeStruct((tok, heads_per_group * HD), jnp.float32)
        dq_spec = pl.BlockSpec((tok, hb * HD), local_block)
    if remote:
        dkv_shape = jax.ShapeDtypeStruct((n_pieces, tok, kvh * 2 * HD), jnp.bfloat16)
        dkv_spec = pl.BlockSpec((n_pieces, tok, 2 * HD), lambda b, f: (0, 0, group))
    else:
        dkv_shape = jax.ShapeDtypeStruct((n_pieces, tok, 2 * HD), jnp.float32)
        dkv_spec = pl.BlockSpec((n_pieces, tok, 2 * HD), lambda b, f: (0, 0, 0))

    grid_spec = pltpu.PrefetchScalarGridSpec(
        num_scalar_prefetch=1,
        grid=(nb,),
        in_specs=in_specs,
        out_specs=[dq_spec, dkv_spec],
        scratch_shapes=[
            pltpu.VMEM((hb * tok, HD), jnp.bfloat16),
            pltpu.VMEM((hb * tok, HD), jnp.bfloat16),
            pltpu.VMEM((HD, hb * tok), jnp.float32),
            pltpu.VMEM((HD, n_pieces * tok), jnp.bfloat16),
            pltpu.VMEM((n_pieces, tok, 2 * HD), jnp.float32),
        ],
    )
    return pl.pallas_call(
        kernel,
        grid_spec=grid_spec,
        out_shape=[dq_shape, dkv_shape],
        input_output_aliases=aliases,
        compiler_params=pltpu.CompilerParams(dimension_semantics=("arbitrary",)),
    )(flags, *args)


def per_device(queries, keys, values, outputs, out_grad, logsumexp, doc_lengths):
    tok, width = queries.shape
    kvh = keys.shape[1] // HD
    reach = -(-(MOST - 1) // tok)
    win = (reach + 1) * tok
    scale = 1.0 / math.sqrt(HD)
    position = lax.axis_index("seq")
    doc_ends = jnp.cumsum(doc_lengths)

    def doc_of(places):
        return jnp.sum((doc_ends[None, :] <= places[:, None]).astype(jnp.int32), axis=1)

    query_places = position * tok + jnp.arange(tok, dtype=jnp.int32)
    query_ids = doc_of(query_places)
    key_places = (position - reach) * tok + jnp.arange(win, dtype=jnp.int32)
    key_ids = jnp.where(key_places >= 0, doc_of(key_places), -1)
    visible = (key_ids[:, None] == query_ids[None, :]) & (
        key_places[:, None] <= query_places[None, :])
    bias = jnp.where(visible, 0.0, -jnp.inf).astype(jnp.float32)
    n_tiles = win // KEY_TILE
    last_places = (position - reach) * tok + KEY_TILE * jnp.arange(
        1, n_tiles + 1, dtype=jnp.int32) - 1
    first_doc = doc_of(position[None] * tok)
    flags = ((doc_of(last_places) == first_doc) & (last_places >= 0)).astype(jnp.int32)

    kv = jnp.concatenate(
        [part for g in range(kvh)
         for part in (keys[:, g * HD:(g + 1) * HD], values[:, g * HD:(g + 1) * HD])], axis=1)
    kv_pieces = [kv] + [shifted(kv, "seq", hop) for hop in range(1, reach + 1)]
    common = (flags, queries, out_grad, outputs, logsumexp, bias, kv_pieces, reach)

    dq_part0, dkv_own0 = grads_call(0, False, *common)
    dq, dkv_rem = grads_call(0, True, *common, dq_part=dq_part0)
    dq_part1, dkv_rem = grads_call(1, True, *common, dkv_alias=dkv_rem)
    returned = [shifted(dkv_rem[reach - hop], "seq", -hop) for hop in range(1, reach + 1)]
    dq, dkv_own1 = grads_call(1, False, *common, dq_part=dq_part1, dq_alias=dq)

    total = jnp.concatenate([dkv_own0[0], dkv_own1[0]], axis=1)
    for r in returned:
        total = total + r.astype(jnp.float32)
    key_total = jnp.concatenate(
        [total[:, (2 * g) * HD:(2 * g + 1) * HD] for g in range(kvh)], axis=1)
    value_total = jnp.concatenate(
        [total[:, (2 * g + 1) * HD:(2 * g + 2) * HD] for g in range(kvh)], axis=1)
    return (
        dq,
        (key_total * scale).astype(jnp.bfloat16),
        value_total.astype(jnp.bfloat16),
    )


def solution(mesh):
    in_specs = (
        P(("parts", "seq"), None),
        P(("parts", "seq"), None),
        P(("parts", "seq"), None),
        P(("parts", "seq"), None),
        P(("parts", "seq"), None),
        P(None, ("parts", "seq")),
        P("parts"),
    )
    out_specs = (P(("parts", "seq"), None), P(("parts", "seq"), None), P(("parts", "seq"), None))
    return jax.shard_map(
        per_device, mesh=mesh, in_specs=in_specs, out_specs=out_specs, check_vma=False
    )
```

```python
import math

import jax
import jax.numpy as jnp
from jax import lax
from jax.experimental import pallas as pl
from jax.experimental.pallas import tpu as pltpu
from jax.sharding import PartitionSpec as P

HD = 128
MOST = 512
KEY_TILE = 128
QUERY_TILE = 128
HEADS_PER_STEP = 8
NT_DIMS = (((1,), (1,)), ((), ()))


def shifted(block, axis, distance):
    devices = range(lax.axis_size(axis))
    route = [(i - distance, i) for i in devices if i - distance in devices]
    return lax.ppermute(block, axis, route)


def make_kernel(tok, reach, remote, dq_in, dq_final, n_alias):
    hb = HEADS_PER_STEP
    pieces = list(range(reach)) if remote else [reach]
    tiles_per_piece = tok // KEY_TILE
    n_halves = tok // QUERY_TILE
    span = hb * QUERY_TILE
    scale = 1.0 / math.sqrt(HD)

    def kernel(flags_ref, q_ref, do_ref, o_ref, lse_ref, bias_ref, *rest):
        rest = list(rest)
        kv_refs = [rest.pop(0) for _ in pieces]
        dqp_ref = rest.pop(0) if dq_in else None
        rest = rest[n_alias:]
        dq_ref = rest.pop(0)
        dkv_ref = rest.pop(0)
        qs_scr, dos_scr, dqt_scr, kt_scr, acc_scr = rest[-5:]
        b = pl.program_id(0)
        nb = pl.num_programs(0)

        @pl.when(b == 0)
        def _():
            acc_scr[...] = jnp.zeros_like(acc_scr)
            for n, kv in enumerate(kv_refs):
                kt_scr[:, n * tok:(n + 1) * tok] = (
                    kv[:, :HD].astype(jnp.float32).T.astype(jnp.bfloat16))

        delta_rows = []
        for i in range(hb):
            cols = slice(i * HD, (i + 1) * HD)
            for h in range(n_halves):
                dst = slice(h * span + i * QUERY_TILE, h * span + (i + 1) * QUERY_TILE)
                src = slice(h * QUERY_TILE, (h + 1) * QUERY_TILE)
                qs_scr[dst, :] = q_ref[src, cols]
                dos_scr[dst, :] = do_ref[src, cols]
            prod = do_ref[:, cols].astype(jnp.float32) * o_ref[:, cols].astype(jnp.float32)
            delta_rows.append(jnp.sum(prod.T, axis=0, keepdims=True))
        dl_row = jnp.concatenate(
            [delta_rows[i][:, h * QUERY_TILE:(h + 1) * QUERY_TILE]
             for h in range(n_halves) for i in range(hb)], axis=1)
        lse_row = jnp.concatenate(
            [lse_ref[i:i + 1, h * QUERY_TILE:(h + 1) * QUERY_TILE]
             for h in range(n_halves) for i in range(hb)], axis=1)
        dqt_scr[...] = jnp.zeros_like(dqt_scr)

        for n, piece in enumerate(pieces):
            kv = kv_refs[n]
            for t in range(tiles_per_piece):
                j = piece * tiles_per_piece + t
                rows = slice(t * KEY_TILE, (t + 1) * KEY_TILE)
                loc_rows = slice(n * tok + t * KEY_TILE, n * tok + (t + 1) * KEY_TILE)
                for h in range(n_halves):
                    lanes = slice(h * span, (h + 1) * span)

                    def block(kv=kv, rows=rows, loc_rows=loc_rows, n=n, h=h, lanes=lanes):
                        k = kv[rows, :HD]
                        v = kv[rows, HD:]
                        qs = qs_scr[lanes, :]
                        dos = dos_scr[lanes, :]
                        st = lax.dot_general(k, qs, NT_DIMS, preferred_element_type=jnp.float32)
                        bias = bias_ref[loc_rows, h * QUERY_TILE:(h + 1) * QUERY_TILE]
                        p = jnp.exp(st * scale - lse_row[:, lanes]
                                    + jnp.concatenate([bias] * hb, axis=1))
                        dv = jnp.dot(p.astype(jnp.bfloat16), dos,
                                     preferred_element_type=jnp.float32)
                        dpt = lax.dot_general(v, dos, NT_DIMS, preferred_element_type=jnp.float32)
                        ds = (p * (dpt - dl_row[:, lanes])).astype(jnp.bfloat16)
                        dk = jnp.dot(ds, qs, preferred_element_type=jnp.float32)
                        acc_scr[n, rows, :HD] += dk
                        acc_scr[n, rows, HD:] += dv
                        dqt_scr[:, lanes] += jnp.dot(
                            kt_scr[:, loc_rows], ds, preferred_element_type=jnp.float32)

                    pl.when(flags_ref[j * n_halves + h] != 0)(block)

        for i in range(hb):
            cols = slice(i * HD, (i + 1) * HD)
            part = jnp.concatenate(
                [dqt_scr[:, h * span + i * QUERY_TILE:h * span + (i + 1) * QUERY_TILE].T
                 for h in range(n_halves)], axis=0)
            if dq_in:
                part = part + dqp_ref[:, cols]
            if dq_final:
                dq_ref[:, cols] = (part * scale).astype(dq_ref.dtype)
            else:
                dq_ref[:, cols] = part

        @pl.when(b == nb - 1)
        def _():
            dkv_ref[...] = acc_scr[...].astype(dkv_ref.dtype)

    return kernel


def grads_call(group, remote, flags, queries, out_grad, outputs, lse, bias, kv_pieces,
               reach, dq_part=None, dq_alias=None, dkv_alias=None):
    tok, width = queries.shape
    n_heads = width // HD
    kvh = kv_pieces[0].shape[1] // (2 * HD)
    heads_per_group = n_heads // kvh
    hb = HEADS_PER_STEP
    nb = heads_per_group // hb
    dq_final = dq_part is not None
    pieces = list(range(reach)) if remote else [reach]
    n_pieces = len(pieces)

    def head_block(b, f):
        return (0, group * nb + b)

    def lse_block(b, f):
        return (group * nb + b, 0)

    def local_block(b, f):
        return (0, b)

    def bias_block(b, f):
        return (0, 0) if remote else (reach, 0)

    def kv_block(b, f):
        return (0, group)

    in_specs = [
        pl.BlockSpec((tok, hb * HD), head_block),
        pl.BlockSpec((tok, hb * HD), head_block),
        pl.BlockSpec((tok, hb * HD), head_block),
        pl.BlockSpec((hb, tok), lse_block),
        pl.BlockSpec((n_pieces * tok, tok), bias_block),
    ] + [pl.BlockSpec((tok, 2 * HD), kv_block) for _ in pieces]
    args = [queries, out_grad, outputs, lse, bias] + [kv_pieces[reach - p] for p in pieces]
    if dq_part is not None:
        in_specs.append(pl.BlockSpec((tok, hb * HD), local_block))
        args.append(dq_part)
    aliases = {}
    if dq_alias is not None:
        aliases[len(args) + 1] = 0
        in_specs.append(pl.BlockSpec(memory_space=pl.ANY))
        args.append(dq_alias)
    if dkv_alias is not None:
        aliases[len(args) + 1] = 1
        in_specs.append(pl.BlockSpec(memory_space=pl.ANY))
        args.append(dkv_alias)

    kernel = make_kernel(tok, reach, remote, dq_part is not None, dq_final, len(aliases))
    if dq_final:
        dq_shape = jax.ShapeDtypeStruct((tok, width), jnp.bfloat16)
        dq_spec = pl.BlockSpec((tok, hb * HD), head_block)
    else:
        dq_shape = jax.ShapeDtypeStruct((tok, heads_per_group * HD), jnp.float32)
        dq_spec = pl.BlockSpec((tok, hb * HD), local_block)
    if remote:
        dkv_shape = jax.ShapeDtypeStruct((n_pieces, tok, kvh * 2 * HD), jnp.bfloat16)
        dkv_spec = pl.BlockSpec((n_pieces, tok, 2 * HD), lambda b, f: (0, 0, group))
    else:
        dkv_shape = jax.ShapeDtypeStruct((n_pieces, tok, 2 * HD), jnp.float32)
        dkv_spec = pl.BlockSpec((n_pieces, tok, 2 * HD), lambda b, f: (0, 0, 0))

    grid_spec = pltpu.PrefetchScalarGridSpec(
        num_scalar_prefetch=1,
        grid=(nb,),
        in_specs=in_specs,
        out_specs=[dq_spec, dkv_spec],
        scratch_shapes=[
            pltpu.VMEM((hb * tok, HD), jnp.bfloat16),
            pltpu.VMEM((hb * tok, HD), jnp.bfloat16),
            pltpu.VMEM((HD, hb * tok), jnp.float32),
            pltpu.VMEM((HD, n_pieces * tok), jnp.bfloat16),
            pltpu.VMEM((n_pieces, tok, 2 * HD), jnp.float32),
        ],
    )
    return pl.pallas_call(
        kernel,
        grid_spec=grid_spec,
        out_shape=[dq_shape, dkv_shape],
        input_output_aliases=aliases,
        compiler_params=pltpu.CompilerParams(dimension_semantics=("arbitrary",)),
    )(flags, *args)


def per_device(queries, keys, values, outputs, out_grad, logsumexp, doc_lengths):
    tok, width = queries.shape
    kvh = keys.shape[1] // HD
    reach = -(-(MOST - 1) // tok)
    win = (reach + 1) * tok
    scale = 1.0 / math.sqrt(HD)
    position = lax.axis_index("seq")
    doc_ends = jnp.cumsum(doc_lengths)

    def doc_of(places):
        return jnp.sum((doc_ends[None, :] <= places[:, None]).astype(jnp.int32), axis=1)

    query_places = position * tok + jnp.arange(tok, dtype=jnp.int32)
    query_ids = doc_of(query_places)
    key_places = (position - reach) * tok + jnp.arange(win, dtype=jnp.int32)
    key_ids = jnp.where(key_places >= 0, doc_of(key_places), -1)
    visible = (key_ids[:, None] == query_ids[None, :]) & (
        key_places[:, None] <= query_places[None, :])
    bias = jnp.where(visible, 0.0, -jnp.inf).astype(jnp.float32)
    key_lo = (position - reach) * tok + KEY_TILE * jnp.arange(win // KEY_TILE, dtype=jnp.int32)
    key_hi = key_lo + KEY_TILE - 1
    query_lo = position * tok + QUERY_TILE * jnp.arange(tok // QUERY_TILE, dtype=jnp.int32)
    query_hi = query_lo + QUERY_TILE - 1
    same_doc = doc_of(key_hi)[:, None] == doc_of(query_lo)[None, :]
    flags = ((key_lo[:, None] <= query_hi[None, :]) & (key_hi[:, None] >= 0)
             & ((key_hi[:, None] >= query_lo[None, :]) | same_doc)).astype(jnp.int32).reshape(-1)

    kv = jnp.concatenate(
        [part for g in range(kvh)
         for part in (keys[:, g * HD:(g + 1) * HD], values[:, g * HD:(g + 1) * HD])], axis=1)
    kv_pieces = [kv] + [shifted(kv, "seq", hop) for hop in range(1, reach + 1)]
    common = (flags, queries, out_grad, outputs, logsumexp, bias, kv_pieces, reach)

    dq_part0, dkv_own0 = grads_call(0, False, *common)
    dq, dkv_rem = grads_call(0, True, *common, dq_part=dq_part0)
    dq_part1, dkv_rem = grads_call(1, True, *common, dkv_alias=dkv_rem)
    returned = [shifted(dkv_rem[reach - hop], "seq", -hop) for hop in range(1, reach + 1)]
    dq, dkv_own1 = grads_call(1, False, *common, dq_part=dq_part1, dq_alias=dq)

    total = jnp.concatenate([dkv_own0[0], dkv_own1[0]], axis=1)
    for r in returned:
        total = total + r.astype(jnp.float32)
    key_total = jnp.concatenate(
        [total[:, (2 * g) * HD:(2 * g + 1) * HD] for g in range(kvh)], axis=1)
    value_total = jnp.concatenate(
        [total[:, (2 * g + 1) * HD:(2 * g + 2) * HD] for g in range(kvh)], axis=1)
    return (
        dq,
        (key_total * scale).astype(jnp.bfloat16),
        value_total.astype(jnp.bfloat16),
    )


def solution(mesh):
    in_specs = (
        P(("parts", "seq"), None),
        P(("parts", "seq"), None),
        P(("parts", "seq"), None),
        P(("parts", "seq"), None),
        P(("parts", "seq"), None),
        P(None, ("parts", "seq")),
        P("parts"),
    )
    out_specs = (P(("parts", "seq"), None), P(("parts", "seq"), None), P(("parts", "seq"), None))
    return jax.shard_map(
        per_device, mesh=mesh, in_specs=in_specs, out_specs=out_specs, check_vma=False
    )
```

```python
import math

import jax
import jax.numpy as jnp
from jax import lax
from jax.experimental import pallas as pl
from jax.experimental.pallas import tpu as pltpu
from jax.sharding import PartitionSpec as P

HD = 128
MOST = 512
KEY_TILE = 128
HEADS_PER_STEP = 8
NT_DIMS = (((1,), (1,)), ((), ()))


def shifted(block, axis, distance):
    devices = range(lax.axis_size(axis))
    route = [(i - distance, i) for i in devices if i - distance in devices]
    return lax.ppermute(block, axis, route)


def make_kernel(tok, reach, remote, dq_in, dq_final, n_alias):
    hb = HEADS_PER_STEP
    pieces = list(range(reach)) if remote else [reach]
    tiles_per_piece = tok // KEY_TILE
    n_rows = len(pieces) * tok
    scale = 1.0 / math.sqrt(HD)

    def kernel(flags_ref, q_ref, do_ref, o_ref, lse_ref, bias_ref, *rest):
        rest = list(rest)
        kv_refs = [rest.pop(0) for _ in pieces]
        dqp_ref = rest.pop(0) if dq_in else None
        rest = rest[n_alias:]
        dq_ref = rest.pop(0)
        dkv_refs = [rest.pop(0) for _ in pieces]
        qs_scr, dos_scr, dqt_scr, kt_scr, acc_scr = rest[-5:]
        b = pl.program_id(0)
        nb = pl.num_programs(0)

        @pl.when(b == 0)
        def _():
            acc_scr[...] = jnp.zeros_like(acc_scr)
            for n, kv in enumerate(kv_refs):
                kt_scr[:, n * tok:(n + 1) * tok] = (
                    kv[:, :HD].astype(jnp.float32).T.astype(jnp.bfloat16))

        delta_rows = []
        for i in range(hb):
            cols = slice(i * HD, (i + 1) * HD)
            qs_scr[i * tok:(i + 1) * tok, :] = q_ref[:, cols]
            dos_scr[i * tok:(i + 1) * tok, :] = do_ref[:, cols]
            prod = do_ref[:, cols].astype(jnp.float32) * o_ref[:, cols].astype(jnp.float32)
            delta_rows.append(jnp.sum(prod.T, axis=0, keepdims=True))
        dl_row = jnp.concatenate(delta_rows, axis=1)
        lse_row = jnp.concatenate([lse_ref[i:i + 1, :] for i in range(hb)], axis=1)
        dqt_scr[...] = jnp.zeros_like(dqt_scr)

        for n, piece in enumerate(pieces):
            kv = kv_refs[n]
            for t in range(tiles_per_piece):
                j = piece * tiles_per_piece + t
                rows = slice(t * KEY_TILE, (t + 1) * KEY_TILE)
                loc_rows = slice(n * tok + t * KEY_TILE, n * tok + (t + 1) * KEY_TILE)

                def tile(kv=kv, rows=rows, loc_rows=loc_rows, n=n):
                    k = kv[rows, :HD]
                    v = kv[rows, HD:]
                    qs = qs_scr[...]
                    dos = dos_scr[...]
                    st = lax.dot_general(k, qs, NT_DIMS, preferred_element_type=jnp.float32)
                    bias = bias_ref[loc_rows, :]
                    p = jnp.exp(st * scale - lse_row + jnp.concatenate([bias] * hb, axis=1))
                    dv = jnp.dot(p.astype(jnp.bfloat16), dos, preferred_element_type=jnp.float32)
                    dpt = lax.dot_general(v, dos, NT_DIMS, preferred_element_type=jnp.float32)
                    ds = (p * (dpt - dl_row)).astype(jnp.bfloat16)
                    dk = jnp.dot(ds, qs, preferred_element_type=jnp.float32)
                    acc_scr[n, rows, :HD] += dk
                    acc_scr[n, rows, HD:] += dv
                    dqt_scr[...] += jnp.dot(
                        kt_scr[:, loc_rows], ds, preferred_element_type=jnp.float32)

                if remote:
                    pl.when(flags_ref[j] != 0)(tile)
                else:
                    tile()

        for i in range(hb):
            cols = slice(i * HD, (i + 1) * HD)
            part = dqt_scr[:, i * tok:(i + 1) * tok].T
            if dq_in:
                part = part + dqp_ref[:, cols]
            if dq_final:
                dq_ref[:, cols] = (part * scale).astype(dq_ref.dtype)
            else:
                dq_ref[:, cols] = part

        @pl.when(b == nb - 1)
        def _():
            for n, dkv_ref in enumerate(dkv_refs):
                dkv_ref[...] = acc_scr[n].astype(dkv_ref.dtype)

    return kernel


def grads_call(group, remote, flags, queries, out_grad, outputs, lse, bias, kv_pieces,
               reach, dq_part=None, dq_alias=None, dkv_alias=None):
    tok, width = queries.shape
    n_heads = width // HD
    kvh = kv_pieces[0].shape[1] // (2 * HD)
    heads_per_group = n_heads // kvh
    hb = HEADS_PER_STEP
    nb = heads_per_group // hb
    dq_final = dq_part is not None
    pieces = list(range(reach)) if remote else [reach]
    n_pieces = len(pieces)

    def head_block(b, f):
        return (0, group * nb + b)

    def lse_block(b, f):
        return (group * nb + b, 0)

    def local_block(b, f):
        return (0, b)

    def bias_block(b, f):
        return (0, 0)

    def kv_block(b, f):
        return (0, group)

    in_specs = [
        pl.BlockSpec((tok, hb * HD), head_block),
        pl.BlockSpec((tok, hb * HD), head_block),
        pl.BlockSpec((tok, hb * HD), head_block),
        pl.BlockSpec((hb, tok), lse_block),
        pl.BlockSpec((n_pieces * tok, tok), bias_block),
    ] + [pl.BlockSpec((tok, 2 * HD), kv_block) for _ in pieces]
    args = [queries, out_grad, outputs, lse, bias] + [kv_pieces[reach - p] for p in pieces]
    if dq_part is not None:
        in_specs.append(pl.BlockSpec((tok, hb * HD), local_block))
        args.append(dq_part)
    aliases = {}
    if dq_alias is not None:
        aliases[len(args) + 1] = 0
        in_specs.append(pl.BlockSpec(memory_space=pl.ANY))
        args.append(dq_alias)
    if dkv_alias is not None:
        for n, piece_arr in enumerate(dkv_alias):
            aliases[len(args) + 1] = 1 + n
            in_specs.append(pl.BlockSpec(memory_space=pl.ANY))
            args.append(piece_arr)

    kernel = make_kernel(tok, reach, remote, dq_part is not None, dq_final, len(aliases))
    if dq_final:
        dq_shape = jax.ShapeDtypeStruct((tok, width), jnp.bfloat16)
        dq_spec = pl.BlockSpec((tok, hb * HD), head_block)
    else:
        dq_shape = jax.ShapeDtypeStruct((tok, heads_per_group * HD), jnp.float32)
        dq_spec = pl.BlockSpec((tok, hb * HD), local_block)
    if remote:
        dkv_shape = jax.ShapeDtypeStruct((tok, kvh * 2 * HD), jnp.bfloat16)
        dkv_spec = pl.BlockSpec((tok, 2 * HD), lambda b, f: (0, group))
    else:
        dkv_shape = jax.ShapeDtypeStruct((tok, 2 * HD), jnp.float32)
        dkv_spec = pl.BlockSpec((tok, 2 * HD), lambda b, f: (0, 0))

    grid_spec = pltpu.PrefetchScalarGridSpec(
        num_scalar_prefetch=1,
        grid=(nb,),
        in_specs=in_specs,
        out_specs=[dq_spec] + [dkv_spec] * n_pieces,
        scratch_shapes=[
            pltpu.VMEM((hb * tok, HD), jnp.bfloat16),
            pltpu.VMEM((hb * tok, HD), jnp.bfloat16),
            pltpu.VMEM((HD, hb * tok), jnp.float32),
            pltpu.VMEM((HD, n_pieces * tok), jnp.bfloat16),
            pltpu.VMEM((n_pieces, tok, 2 * HD), jnp.float32),
        ],
    )
    outs = pl.pallas_call(
        kernel,
        grid_spec=grid_spec,
        out_shape=[dq_shape] + [dkv_shape] * n_pieces,
        input_output_aliases=aliases,
        compiler_params=pltpu.CompilerParams(dimension_semantics=("arbitrary",)),
    )(flags, *args)
    return outs[0], outs[1:]


def per_device(queries, keys, values, outputs, out_grad, logsumexp, doc_lengths):
    tok, width = queries.shape
    kvh = keys.shape[1] // HD
    reach = -(-(MOST - 1) // tok)
    win = (reach + 1) * tok
    scale = 1.0 / math.sqrt(HD)
    position = lax.axis_index("seq")
    doc_ends = jnp.cumsum(doc_lengths)

    def doc_of(places):
        return jnp.sum((doc_ends[None, :] <= places[:, None]).astype(jnp.int32), axis=1)

    query_places = position * tok + jnp.arange(tok, dtype=jnp.int32)
    query_ids = doc_of(query_places)
    key_places = (position - reach) * tok + jnp.arange(win, dtype=jnp.int32)
    key_ids = jnp.where(key_places >= 0, doc_of(key_places), -1)
    own_visible = (query_ids[:, None] == query_ids[None, :]) & (
        query_places[:, None] <= query_places[None, :])
    bias_own = jnp.where(own_visible, 0.0, -jnp.inf).astype(jnp.float32)
    remote_ids = key_ids[:reach * tok]
    bias_rem = jnp.where(remote_ids[:, None] == query_ids[None, :], 0.0, -jnp.inf
                         ).astype(jnp.float32)
    n_tiles = win // KEY_TILE
    last_places = (position - reach) * tok + KEY_TILE * jnp.arange(
        1, n_tiles + 1, dtype=jnp.int32) - 1
    first_doc = doc_of(position[None] * tok)
    flags = ((doc_of(last_places) == first_doc) & (last_places >= 0)).astype(jnp.int32)

    kv = jnp.concatenate(
        [part for g in range(kvh)
         for part in (keys[:, g * HD:(g + 1) * HD], values[:, g * HD:(g + 1) * HD])], axis=1)
    kv_pieces = [kv] + [shifted(kv, "seq", hop) for hop in range(1, reach + 1)]
    no_flags = jnp.zeros((n_tiles,), jnp.int32)
    own = (no_flags, queries, out_grad, outputs, logsumexp, bias_own, kv_pieces, reach)
    rem = (flags, queries, out_grad, outputs, logsumexp, bias_rem, kv_pieces, reach)

    dq_part0, (dkv_own0,) = grads_call(0, False, *own)
    dq, dkv_rem = grads_call(0, True, *rem, dq_part=dq_part0)
    dq_part1, dkv_rem = grads_call(1, True, *rem, dkv_alias=dkv_rem)
    returned = [shifted(dkv_rem[reach - hop], "seq", -hop) for hop in range(1, reach + 1)]
    dq, (dkv_own1,) = grads_call(1, False, *own, dq_part=dq_part1, dq_alias=dq)

    total = jnp.concatenate([dkv_own0, dkv_own1], axis=1)
    for r in returned:
        total = total + r.astype(jnp.float32)
    key_total = jnp.concatenate(
        [total[:, (2 * g) * HD:(2 * g + 1) * HD] for g in range(kvh)], axis=1)
    value_total = jnp.concatenate(
        [total[:, (2 * g + 1) * HD:(2 * g + 2) * HD] for g in range(kvh)], axis=1)
    return (
        dq,
        (key_total * scale).astype(jnp.bfloat16),
        value_total.astype(jnp.bfloat16),
    )


def solution(mesh):
    in_specs = (
        P(("parts", "seq"), None),
        P(("parts", "seq"), None),
        P(("parts", "seq"), None),
        P(("parts", "seq"), None),
        P(("parts", "seq"), None),
        P(None, ("parts", "seq")),
        P("parts"),
    )
    out_specs = (P(("parts", "seq"), None), P(("parts", "seq"), None), P(("parts", "seq"), None))
    return jax.shard_map(
        per_device, mesh=mesh, in_specs=in_specs, out_specs=out_specs, check_vma=False
    )
```

```python
import math

import jax
import jax.numpy as jnp
from jax import lax
from jax.experimental import pallas as pl
from jax.experimental.pallas import tpu as pltpu
from jax.sharding import PartitionSpec as P

HD = 128
MOST = 512
KEY_TILE = 256
HEADS_PER_STEP = 8
NT_DIMS = (((1,), (1,)), ((), ()))


def shifted(block, axis, distance):
    devices = range(lax.axis_size(axis))
    route = [(i - distance, i) for i in devices if i - distance in devices]
    return lax.ppermute(block, axis, route)


def make_kernel(tok, reach, remote, dq_in, dq_final, n_alias):
    hb = HEADS_PER_STEP
    pieces = list(range(reach)) if remote else [reach]
    tiles_per_piece = tok // KEY_TILE
    n_rows = len(pieces) * tok
    scale = 1.0 / math.sqrt(HD)

    def kernel(flags_ref, q_ref, do_ref, o_ref, lse_ref, bias_ref, *rest):
        rest = list(rest)
        kv_refs = [rest.pop(0) for _ in pieces]
        dqp_ref = rest.pop(0) if dq_in else None
        rest = rest[n_alias:]
        dq_ref = rest.pop(0)
        dkv_refs = [rest.pop(0) for _ in pieces]
        qs_scr, dos_scr, dqt_scr, kt_scr, acc_scr = rest[-5:]
        b = pl.program_id(0)
        nb = pl.num_programs(0)

        @pl.when(b == 0)
        def _():
            acc_scr[...] = jnp.zeros_like(acc_scr)
            for n, kv in enumerate(kv_refs):
                kt_scr[:, n * tok:(n + 1) * tok] = (
                    kv[:, :HD].astype(jnp.float32).T.astype(jnp.bfloat16))

        delta_rows = []
        for i in range(hb):
            cols = slice(i * HD, (i + 1) * HD)
            qs_scr[i * tok:(i + 1) * tok, :] = q_ref[:, cols]
            dos_scr[i * tok:(i + 1) * tok, :] = do_ref[:, cols]
            prod = do_ref[:, cols].astype(jnp.float32) * o_ref[:, cols].astype(jnp.float32)
            delta_rows.append(jnp.sum(prod.T, axis=0, keepdims=True))
        dl_row = jnp.concatenate(delta_rows, axis=1)
        lse_row = jnp.concatenate([lse_ref[i:i + 1, :] for i in range(hb)], axis=1)
        dqt_scr[...] = jnp.zeros_like(dqt_scr)

        for n, piece in enumerate(pieces):
            kv = kv_refs[n]
            for t in range(tiles_per_piece):
                j = piece * tiles_per_piece + t
                rows = slice(t * KEY_TILE, (t + 1) * KEY_TILE)
                loc_rows = slice(n * tok + t * KEY_TILE, n * tok + (t + 1) * KEY_TILE)

                def tile(kv=kv, rows=rows, loc_rows=loc_rows, n=n):
                    k = kv[rows, :HD]
                    v = kv[rows, HD:]
                    qs = qs_scr[...]
                    dos = dos_scr[...]
                    st = lax.dot_general(k, qs, NT_DIMS, preferred_element_type=jnp.float32)
                    bias = bias_ref[loc_rows, :]
                    p = jnp.exp(st * scale - lse_row + jnp.concatenate([bias] * hb, axis=1))
                    dv = jnp.dot(p.astype(jnp.bfloat16), dos, preferred_element_type=jnp.float32)
                    dpt = lax.dot_general(v, dos, NT_DIMS, preferred_element_type=jnp.float32)
                    ds = (p * (dpt - dl_row)).astype(jnp.bfloat16)
                    dk = jnp.dot(ds, qs, preferred_element_type=jnp.float32)
                    acc_scr[n, rows, :HD] += dk
                    acc_scr[n, rows, HD:] += dv
                    dqt_scr[...] += jnp.dot(
                        kt_scr[:, loc_rows], ds, preferred_element_type=jnp.float32)

                if remote:
                    pl.when(flags_ref[j] != 0)(tile)
                else:
                    tile()

        for i in range(hb):
            cols = slice(i * HD, (i + 1) * HD)
            part = dqt_scr[:, i * tok:(i + 1) * tok].T
            if dq_in:
                part = part + dqp_ref[:, cols]
            if dq_final:
                dq_ref[:, cols] = (part * scale).astype(dq_ref.dtype)
            else:
                dq_ref[:, cols] = part

        @pl.when(b == nb - 1)
        def _():
            for n, dkv_ref in enumerate(dkv_refs):
                dkv_ref[...] = acc_scr[n].astype(dkv_ref.dtype)

    return kernel


def grads_call(group, remote, flags, queries, out_grad, outputs, lse, bias, kv_pieces,
               reach, dq_part=None, dq_alias=None, dkv_alias=None):
    tok, width = queries.shape
    n_heads = width // HD
    kvh = kv_pieces[0].shape[1] // (2 * HD)
    heads_per_group = n_heads // kvh
    hb = HEADS_PER_STEP
    nb = heads_per_group // hb
    dq_final = dq_part is not None
    pieces = list(range(reach)) if remote else [reach]
    n_pieces = len(pieces)

    def head_block(b, f):
        return (0, group * nb + b)

    def lse_block(b, f):
        return (group * nb + b, 0)

    def local_block(b, f):
        return (0, b)

    def bias_block(b, f):
        return (0, 0)

    def kv_block(b, f):
        return (0, group)

    in_specs = [
        pl.BlockSpec((tok, hb * HD), head_block),
        pl.BlockSpec((tok, hb * HD), head_block),
        pl.BlockSpec((tok, hb * HD), head_block),
        pl.BlockSpec((hb, tok), lse_block),
        pl.BlockSpec((n_pieces * tok, tok), bias_block),
    ] + [pl.BlockSpec((tok, 2 * HD), kv_block) for _ in pieces]
    args = [queries, out_grad, outputs, lse, bias] + [kv_pieces[reach - p] for p in pieces]
    if dq_part is not None:
        in_specs.append(pl.BlockSpec((tok, hb * HD), local_block))
        args.append(dq_part)
    aliases = {}
    if dq_alias is not None:
        aliases[len(args) + 1] = 0
        in_specs.append(pl.BlockSpec(memory_space=pl.ANY))
        args.append(dq_alias)
    if dkv_alias is not None:
        for n, piece_arr in enumerate(dkv_alias):
            aliases[len(args) + 1] = 1 + n
            in_specs.append(pl.BlockSpec(memory_space=pl.ANY))
            args.append(piece_arr)

    kernel = make_kernel(tok, reach, remote, dq_part is not None, dq_final, len(aliases))
    if dq_final:
        dq_shape = jax.ShapeDtypeStruct((tok, width), jnp.bfloat16)
        dq_spec = pl.BlockSpec((tok, hb * HD), head_block)
    else:
        dq_shape = jax.ShapeDtypeStruct((tok, heads_per_group * HD), jnp.float32)
        dq_spec = pl.BlockSpec((tok, hb * HD), local_block)
    if remote:
        dkv_shape = jax.ShapeDtypeStruct((tok, kvh * 2 * HD), jnp.bfloat16)
        dkv_spec = pl.BlockSpec((tok, 2 * HD), lambda b, f: (0, group))
    else:
        dkv_shape = jax.ShapeDtypeStruct((tok, 2 * HD), jnp.float32)
        dkv_spec = pl.BlockSpec((tok, 2 * HD), lambda b, f: (0, 0))

    grid_spec = pltpu.PrefetchScalarGridSpec(
        num_scalar_prefetch=1,
        grid=(nb,),
        in_specs=in_specs,
        out_specs=[dq_spec] + [dkv_spec] * n_pieces,
        scratch_shapes=[
            pltpu.VMEM((hb * tok, HD), jnp.bfloat16),
            pltpu.VMEM((hb * tok, HD), jnp.bfloat16),
            pltpu.VMEM((HD, hb * tok), jnp.float32),
            pltpu.VMEM((HD, n_pieces * tok), jnp.bfloat16),
            pltpu.VMEM((n_pieces, tok, 2 * HD), jnp.float32),
        ],
    )
    outs = pl.pallas_call(
        kernel,
        grid_spec=grid_spec,
        out_shape=[dq_shape] + [dkv_shape] * n_pieces,
        input_output_aliases=aliases,
        compiler_params=pltpu.CompilerParams(dimension_semantics=("arbitrary",)),
    )(flags, *args)
    return outs[0], outs[1:]


def per_device(queries, keys, values, outputs, out_grad, logsumexp, doc_lengths):
    tok, width = queries.shape
    kvh = keys.shape[1] // HD
    reach = -(-(MOST - 1) // tok)
    win = (reach + 1) * tok
    scale = 1.0 / math.sqrt(HD)
    position = lax.axis_index("seq")
    doc_ends = jnp.cumsum(doc_lengths)

    def doc_of(places):
        return jnp.sum((doc_ends[None, :] <= places[:, None]).astype(jnp.int32), axis=1)

    query_places = position * tok + jnp.arange(tok, dtype=jnp.int32)
    query_ids = doc_of(query_places)
    key_places = (position - reach) * tok + jnp.arange(win, dtype=jnp.int32)
    key_ids = jnp.where(key_places >= 0, doc_of(key_places), -1)
    own_visible = (query_ids[:, None] == query_ids[None, :]) & (
        query_places[:, None] <= query_places[None, :])
    bias_own = jnp.where(own_visible, 0.0, -jnp.inf).astype(jnp.float32)
    remote_ids = key_ids[:reach * tok]
    bias_rem = jnp.where(remote_ids[:, None] == query_ids[None, :], 0.0, -jnp.inf
                         ).astype(jnp.float32)
    n_tiles = win // KEY_TILE
    last_places = (position - reach) * tok + KEY_TILE * jnp.arange(
        1, n_tiles + 1, dtype=jnp.int32) - 1
    first_doc = doc_of(position[None] * tok)
    flags = ((doc_of(last_places) == first_doc) & (last_places >= 0)).astype(jnp.int32)

    kv = jnp.concatenate(
        [part for g in range(kvh)
         for part in (keys[:, g * HD:(g + 1) * HD], values[:, g * HD:(g + 1) * HD])], axis=1)
    kv_pieces = [kv] + [shifted(kv, "seq", hop) for hop in range(1, reach + 1)]
    no_flags = jnp.zeros((n_tiles,), jnp.int32)
    own = (no_flags, queries, out_grad, outputs, logsumexp, bias_own, kv_pieces, reach)
    rem = (flags, queries, out_grad, outputs, logsumexp, bias_rem, kv_pieces, reach)

    dq_part0, (dkv_own0,) = grads_call(0, False, *own)
    dq, dkv_rem = grads_call(0, True, *rem, dq_part=dq_part0)
    dq_part1, dkv_rem = grads_call(1, True, *rem, dkv_alias=dkv_rem)
    returned = [shifted(dkv_rem[reach - hop], "seq", -hop) for hop in range(1, reach + 1)]
    dq, (dkv_own1,) = grads_call(1, False, *own, dq_part=dq_part1, dq_alias=dq)

    total = jnp.concatenate([dkv_own0, dkv_own1], axis=1)
    for r in returned:
        total = total + r.astype(jnp.float32)
    key_total = jnp.concatenate(
        [total[:, (2 * g) * HD:(2 * g + 1) * HD] for g in range(kvh)], axis=1)
    value_total = jnp.concatenate(
        [total[:, (2 * g + 1) * HD:(2 * g + 2) * HD] for g in range(kvh)], axis=1)
    return (
        dq,
        (key_total * scale).astype(jnp.bfloat16),
        value_total.astype(jnp.bfloat16),
    )


def solution(mesh):
    in_specs = (
        P(("parts", "seq"), None),
        P(("parts", "seq"), None),
        P(("parts", "seq"), None),
        P(("parts", "seq"), None),
        P(("parts", "seq"), None),
        P(None, ("parts", "seq")),
        P("parts"),
    )
    out_specs = (P(("parts", "seq"), None), P(("parts", "seq"), None), P(("parts", "seq"), None))
    return jax.shard_map(
        per_device, mesh=mesh, in_specs=in_specs, out_specs=out_specs, check_vma=False
    )
```

```python
import math

import jax
import jax.numpy as jnp
from jax import lax
from jax.experimental import pallas as pl
from jax.experimental.pallas import tpu as pltpu
from jax.sharding import PartitionSpec as P

HD = 128
MOST = 512
KEY_TILE = 256
HEADS_PER_STEP = 8
NT_DIMS = (((1,), (1,)), ((), ()))


def shifted(block, axis, distance):
    devices = range(lax.axis_size(axis))
    route = [(i - distance, i) for i in devices if i - distance in devices]
    return lax.ppermute(block, axis, route)


def make_kernel(tok, reach, remote, dq_in, dq_final, n_alias):
    hb = HEADS_PER_STEP
    pieces = list(range(reach)) if remote else [reach]
    tiles_per_piece = tok // KEY_TILE
    n_rows = len(pieces) * tok
    scale = 1.0 / math.sqrt(HD)

    def kernel(flags_ref, q_ref, do_ref, o_ref, lse_ref, bias_ref, *rest):
        rest = list(rest)
        kv_refs = [rest.pop(0) for _ in pieces]
        dqp_ref = rest.pop(0) if dq_in else None
        rest = rest[n_alias:]
        dq_ref = rest.pop(0)
        dkv_refs = [rest.pop(0) for _ in pieces]
        qs_scr, dos_scr, dqt_scr, kt_scr, acc_scr = rest[-5:]
        b = pl.program_id(0)
        nb = pl.num_programs(0)

        @pl.when(b == 0)
        def _():
            acc_scr[...] = jnp.zeros_like(acc_scr)
            for n, kv in enumerate(kv_refs):
                kt_scr[:, n * tok:(n + 1) * tok] = (
                    kv[:, :HD].astype(jnp.float32).T.astype(jnp.bfloat16))

        delta_rows = []
        for i in range(hb):
            cols = slice(i * HD, (i + 1) * HD)
            qs_scr[i * tok:(i + 1) * tok, :] = q_ref[:, cols]
            dos_scr[i * tok:(i + 1) * tok, :] = do_ref[:, cols]
            prod = do_ref[:, cols].astype(jnp.float32) * o_ref[:, cols].astype(jnp.float32)
            delta_rows.append(jnp.sum(prod.T, axis=0, keepdims=True))
        dl_row = jnp.concatenate(delta_rows, axis=1)
        lse_row = jnp.concatenate([lse_ref[i:i + 1, :] for i in range(hb)], axis=1)
        dqt_scr[...] = jnp.zeros_like(dqt_scr)

        for n, piece in enumerate(pieces):
            kv = kv_refs[n]
            for t in range(tiles_per_piece):
                j = piece * tiles_per_piece + t
                rows = slice(t * KEY_TILE, (t + 1) * KEY_TILE)
                loc_rows = slice(n * tok + t * KEY_TILE, n * tok + (t + 1) * KEY_TILE)

                def tile(kv=kv, rows=rows, loc_rows=loc_rows, n=n):
                    k = kv[rows, :HD]
                    v = kv[rows, HD:]
                    qs = qs_scr[...]
                    dos = dos_scr[...]
                    st = lax.dot_general(k, qs, NT_DIMS, preferred_element_type=jnp.float32)
                    bias = bias_ref[loc_rows, :]
                    p = jnp.exp(st * scale - lse_row + jnp.concatenate([bias] * hb, axis=1))
                    dv = jnp.dot(p.astype(jnp.bfloat16), dos, preferred_element_type=jnp.float32)
                    dpt = lax.dot_general(v, dos, NT_DIMS, preferred_element_type=jnp.float32)
                    ds = (p * (dpt - dl_row)).astype(jnp.bfloat16)
                    dk = jnp.dot(ds, qs, preferred_element_type=jnp.float32)
                    acc_scr[n, rows, :HD] += dk
                    acc_scr[n, rows, HD:] += dv
                    dqt_scr[...] += jnp.dot(
                        kt_scr[:, loc_rows], ds, preferred_element_type=jnp.float32)

                if remote:
                    pl.when(flags_ref[j] != 0)(tile)
                else:
                    tile()

        for i in range(hb):
            cols = slice(i * HD, (i + 1) * HD)
            part = dqt_scr[:, i * tok:(i + 1) * tok].T
            if dq_in:
                part = part + dqp_ref[:, cols]
            if dq_final:
                dq_ref[:, cols] = (part * scale).astype(dq_ref.dtype)
            else:
                dq_ref[:, cols] = part

        @pl.when(b == nb - 1)
        def _():
            for n, dkv_ref in enumerate(dkv_refs):
                dkv_ref[...] = acc_scr[n].astype(dkv_ref.dtype)

    return kernel


def grads_call(group, remote, flags, queries, out_grad, outputs, lse, bias, kv_pieces,
               reach, dq_part=None, dq_alias=None, dkv_alias=None):
    tok, width = queries.shape
    n_heads = width // HD
    kvh = kv_pieces[0].shape[1] // (2 * HD)
    heads_per_group = n_heads // kvh
    hb = HEADS_PER_STEP
    nb = heads_per_group // hb
    dq_final = dq_part is not None
    pieces = list(range(reach)) if remote else [reach]
    n_pieces = len(pieces)

    def head_block(b, *f):
        return (0, group * nb + b)

    def lse_block(b, *f):
        return (group * nb + b, 0)

    def local_block(b, *f):
        return (0, b)

    def bias_block(b, *f):
        return (0, 0)

    def kv_block(b, *f):
        return (0, group)

    in_specs = [
        pl.BlockSpec((tok, hb * HD), head_block),
        pl.BlockSpec((tok, hb * HD), head_block),
        pl.BlockSpec((tok, hb * HD), head_block),
        pl.BlockSpec((hb, tok), lse_block),
        pl.BlockSpec((n_pieces * tok, tok), bias_block),
    ] + [pl.BlockSpec((tok, 2 * HD), kv_block) for _ in pieces]
    args = [queries, out_grad, outputs, lse, bias] + [kv_pieces[reach - p] for p in pieces]
    if dq_part is not None:
        in_specs.append(pl.BlockSpec((tok, hb * HD), local_block))
        args.append(dq_part)
    aliases = {}
    if dq_alias is not None:
        aliases[len(args) + int(remote)] = 0
        in_specs.append(pl.BlockSpec(memory_space=pl.ANY))
        args.append(dq_alias)
    if dkv_alias is not None:
        for n, piece_arr in enumerate(dkv_alias):
            aliases[len(args) + int(remote)] = 1 + n
            in_specs.append(pl.BlockSpec(memory_space=pl.ANY))
            args.append(piece_arr)

    kernel = make_kernel(tok, reach, remote, dq_part is not None, dq_final, len(aliases))
    if dq_final:
        dq_shape = jax.ShapeDtypeStruct((tok, width), jnp.bfloat16)
        dq_spec = pl.BlockSpec((tok, hb * HD), head_block)
    else:
        dq_shape = jax.ShapeDtypeStruct((tok, heads_per_group * HD), jnp.float32)
        dq_spec = pl.BlockSpec((tok, hb * HD), local_block)
    if remote:
        dkv_shape = jax.ShapeDtypeStruct((tok, kvh * 2 * HD), jnp.bfloat16)
        dkv_spec = pl.BlockSpec((tok, 2 * HD), lambda b, *f: (0, group))
    else:
        dkv_shape = jax.ShapeDtypeStruct((tok, kvh * 2 * HD), jnp.float32)
        dkv_spec = pl.BlockSpec((tok, 2 * HD), lambda b, *f: (0, group))

    if not remote:
        body = kernel

        def kernel(*refs):
            body(None, *refs)

    grid_spec = pltpu.PrefetchScalarGridSpec(
        num_scalar_prefetch=1 if remote else 0,
        grid=(nb,),
        in_specs=in_specs,
        out_specs=[dq_spec] + [dkv_spec] * n_pieces,
        scratch_shapes=[
            pltpu.VMEM((hb * tok, HD), jnp.bfloat16),
            pltpu.VMEM((hb * tok, HD), jnp.bfloat16),
            pltpu.VMEM((HD, hb * tok), jnp.float32),
            pltpu.VMEM((HD, n_pieces * tok), jnp.bfloat16),
            pltpu.VMEM((n_pieces, tok, 2 * HD), jnp.float32),
        ],
    )
    outs = pl.pallas_call(
        kernel,
        grid_spec=grid_spec,
        out_shape=[dq_shape] + [dkv_shape] * n_pieces,
        input_output_aliases=aliases,
        compiler_params=pltpu.CompilerParams(dimension_semantics=("arbitrary",)),
    )(*([flags] if remote else []), *args)
    return outs[0], outs[1:]


def per_device(queries, keys, values, outputs, out_grad, logsumexp, doc_lengths):
    tok, width = queries.shape
    kvh = keys.shape[1] // HD
    reach = -(-(MOST - 1) // tok)
    win = (reach + 1) * tok
    scale = 1.0 / math.sqrt(HD)
    position = lax.axis_index("seq")
    doc_ends = jnp.cumsum(doc_lengths)

    def doc_of(places):
        return jnp.sum((doc_ends[None, :] <= places[:, None]).astype(jnp.int32), axis=1)

    query_places = position * tok + jnp.arange(tok, dtype=jnp.int32)
    query_ids = doc_of(query_places)
    key_places = (position - reach) * tok + jnp.arange(win, dtype=jnp.int32)
    key_ids = jnp.where(key_places >= 0, doc_of(key_places), -1)
    own_visible = (query_ids[:, None] == query_ids[None, :]) & (
        query_places[:, None] <= query_places[None, :])
    bias_own = jnp.where(own_visible, 0.0, -jnp.inf).astype(jnp.float32)
    remote_ids = key_ids[:reach * tok]
    bias_rem = jnp.where(remote_ids[:, None] == query_ids[None, :], 0.0, -jnp.inf
                         ).astype(jnp.float32)
    n_tiles = win // KEY_TILE
    last_places = (position - reach) * tok + KEY_TILE * jnp.arange(
        1, n_tiles + 1, dtype=jnp.int32) - 1
    first_doc = doc_of(position[None] * tok)
    flags = ((doc_of(last_places) == first_doc) & (last_places >= 0)).astype(jnp.int32)

    kv = jnp.concatenate(
        [part for g in range(kvh)
         for part in (keys[:, g * HD:(g + 1) * HD], values[:, g * HD:(g + 1) * HD])], axis=1)
    kv_pieces = [kv] + [shifted(kv, "seq", hop) for hop in range(1, reach + 1)]
    own = (None, queries, out_grad, outputs, logsumexp, bias_own, kv_pieces, reach)
    rem = (flags, queries, out_grad, outputs, logsumexp, bias_rem, kv_pieces, reach)

    dq_part0, (dkv_own0,) = grads_call(0, False, *own)
    dq, dkv_rem = grads_call(0, True, *rem, dq_part=dq_part0)
    dq_part1, dkv_rem = grads_call(1, True, *rem, dkv_alias=dkv_rem)
    returned = [shifted(dkv_rem[reach - hop], "seq", -hop) for hop in range(1, reach + 1)]
    dq, (total,) = grads_call(1, False, *own, dq_part=dq_part1, dq_alias=dq,
                              dkv_alias=[dkv_own0])

    for r in returned:
        total = total + r.astype(jnp.float32)
    key_total = jnp.concatenate(
        [total[:, (2 * g) * HD:(2 * g + 1) * HD] for g in range(kvh)], axis=1)
    value_total = jnp.concatenate(
        [total[:, (2 * g + 1) * HD:(2 * g + 2) * HD] for g in range(kvh)], axis=1)
    return (
        dq,
        (key_total * scale).astype(jnp.bfloat16),
        value_total.astype(jnp.bfloat16),
    )


def solution(mesh):
    in_specs = (
        P(("parts", "seq"), None),
        P(("parts", "seq"), None),
        P(("parts", "seq"), None),
        P(("parts", "seq"), None),
        P(("parts", "seq"), None),
        P(None, ("parts", "seq")),
        P("parts"),
    )
    out_specs = (P(("parts", "seq"), None), P(("parts", "seq"), None), P(("parts", "seq"), None))
    return jax.shard_map(
        per_device, mesh=mesh, in_specs=in_specs, out_specs=out_specs, check_vma=False
    )
```

```python
import math

import jax
import jax.numpy as jnp
from jax import lax
from jax.experimental import pallas as pl
from jax.experimental.pallas import tpu as pltpu
from jax.sharding import PartitionSpec as P

HD = 128
MOST = 512
KEY_TILE = 256
HEADS_PER_STEP = 8
NT_DIMS = (((1,), (1,)), ((), ()))


def shifted(block, axis, distance):
    devices = range(lax.axis_size(axis))
    route = [(i - distance, i) for i in devices if i - distance in devices]
    return lax.ppermute(block, axis, route)


def make_kernel(tok, reach, remote, dq_in, dq_final, n_alias):
    hb = HEADS_PER_STEP
    pieces = list(range(reach)) if remote else [reach]
    tiles_per_piece = tok // KEY_TILE
    n_rows = len(pieces) * tok
    scale = 1.0 / math.sqrt(HD)

    def kernel(flags_ref, q_ref, do_ref, o_ref, lse_ref, bias_ref, *rest):
        rest = list(rest)
        kv_refs = [rest.pop(0) for _ in pieces]
        dqp_ref = rest.pop(0) if dq_in else None
        rest = rest[n_alias:]
        dq_ref = rest.pop(0)
        dkv_refs = [rest.pop(0) for _ in pieces]
        qs_scr, dos_scr, dqt_scr, kt_scr, acc_scr = rest[-5:]
        b = pl.program_id(0)
        nb = pl.num_programs(0)

        @pl.when(b == 0)
        def _():
            acc_scr[...] = jnp.zeros_like(acc_scr)
            for n, kv in enumerate(kv_refs):
                kt_scr[:, n * tok:(n + 1) * tok] = (
                    kv[:, :HD].astype(jnp.float32).T.astype(jnp.bfloat16))

        delta_rows = []
        for i in range(hb):
            cols = slice(i * HD, (i + 1) * HD)
            qs_scr[i * tok:(i + 1) * tok, :] = q_ref[:, cols]
            dos_scr[i * tok:(i + 1) * tok, :] = do_ref[:, cols]
            prod = do_ref[:, cols].astype(jnp.float32) * o_ref[:, cols].astype(jnp.float32)
            delta_rows.append(jnp.sum(prod.T, axis=0, keepdims=True))
        dl_row = jnp.concatenate(delta_rows, axis=1)
        lse_row = jnp.concatenate([lse_ref[i:i + 1, :] for i in range(hb)], axis=1)
        dqt_scr[...] = jnp.zeros_like(dqt_scr)

        for n, piece in enumerate(pieces):
            kv = kv_refs[n]
            for t in range(tiles_per_piece):
                j = piece * tiles_per_piece + t
                rows = slice(t * KEY_TILE, (t + 1) * KEY_TILE)
                loc_rows = slice(n * tok + t * KEY_TILE, n * tok + (t + 1) * KEY_TILE)

                def tile(kv=kv, rows=rows, loc_rows=loc_rows, n=n):
                    k = kv[rows, :HD]
                    v = kv[rows, HD:]
                    qs = qs_scr[...]
                    dos = dos_scr[...]
                    st = lax.dot_general(k, qs, NT_DIMS, preferred_element_type=jnp.float32)
                    bias = bias_ref[loc_rows, :]
                    p = jnp.exp(st * scale - lse_row + jnp.concatenate([bias] * hb, axis=1))
                    dv = jnp.dot(p.astype(jnp.bfloat16), dos, preferred_element_type=jnp.float32)
                    dpt = lax.dot_general(v, dos, NT_DIMS, preferred_element_type=jnp.float32)
                    ds = (p * (dpt - dl_row)).astype(jnp.bfloat16)
                    dk = jnp.dot(ds, qs, preferred_element_type=jnp.float32)
                    acc_scr[n, rows, :HD] += dk
                    acc_scr[n, rows, HD:] += dv
                    dqt_scr[...] += jnp.dot(
                        kt_scr[:, loc_rows], ds, preferred_element_type=jnp.float32)

                if remote:
                    pl.when(flags_ref[j] != 0)(tile)
                else:
                    tile()

        for i in range(hb):
            cols = slice(i * HD, (i + 1) * HD)
            part = dqt_scr[:, i * tok:(i + 1) * tok].T
            if dq_in:
                part = part + dqp_ref[:, cols]
            if dq_final:
                dq_ref[:, cols] = (part * scale).astype(dq_ref.dtype)
            else:
                dq_ref[:, cols] = part

        @pl.when(b == nb - 1)
        def _():
            for n, dkv_ref in enumerate(dkv_refs):
                dkv_ref[...] = acc_scr[n].astype(dkv_ref.dtype)

    return kernel


def grads_call(group, remote, flags, queries, out_grad, outputs, lse, bias, kv_pieces,
               reach, dq_part=None, dq_alias=None, dkv_alias=None):
    tok, width = queries.shape
    n_heads = width // HD
    kvh = kv_pieces[0].shape[1] // (2 * HD)
    heads_per_group = n_heads // kvh
    hb = HEADS_PER_STEP
    nb = heads_per_group // hb
    dq_final = dq_part is not None
    pieces = list(range(reach)) if remote else [reach]
    n_pieces = len(pieces)

    def head_block(b, *f):
        return (0, group * nb + b)

    def lse_block(b, *f):
        return (group * nb + b, 0)

    def local_block(b, *f):
        return (0, b)

    def bias_block(b, *f):
        return (0, 0)

    def kv_block(b, *f):
        return (0, group)

    in_specs = [
        pl.BlockSpec((tok, hb * HD), head_block),
        pl.BlockSpec((tok, hb * HD), head_block),
        pl.BlockSpec((tok, hb * HD), head_block),
        pl.BlockSpec((hb, tok), lse_block),
        pl.BlockSpec((n_pieces * tok, tok), bias_block),
    ] + [pl.BlockSpec((tok, 2 * HD), kv_block) for _ in pieces]
    args = [queries, out_grad, outputs, lse, bias] + [kv_pieces[reach - p] for p in pieces]
    if dq_part is not None:
        in_specs.append(pl.BlockSpec((tok, hb * HD), local_block))
        args.append(dq_part)
    aliases = {}
    if dq_alias is not None:
        aliases[len(args) + int(remote)] = 0
        in_specs.append(pl.BlockSpec(memory_space=pl.ANY))
        args.append(dq_alias)
    if dkv_alias is not None:
        for n, piece_arr in enumerate(dkv_alias):
            aliases[len(args) + int(remote)] = 1 + n
            in_specs.append(pl.BlockSpec(memory_space=pl.ANY))
            args.append(piece_arr)

    kernel = make_kernel(tok, reach, remote, dq_part is not None, dq_final, len(aliases))
    if dq_final:
        dq_shape = jax.ShapeDtypeStruct((tok, width), jnp.bfloat16)
        dq_spec = pl.BlockSpec((tok, hb * HD), head_block)
    else:
        dq_shape = jax.ShapeDtypeStruct((tok, heads_per_group * HD), jnp.float32)
        dq_spec = pl.BlockSpec((tok, hb * HD), local_block)
    if remote:
        dkv_shape = jax.ShapeDtypeStruct((tok, kvh * 2 * HD), jnp.bfloat16)
        dkv_spec = pl.BlockSpec((tok, 2 * HD), lambda b, *f: (0, group))
    else:
        dkv_shape = jax.ShapeDtypeStruct((tok, kvh * 2 * HD), jnp.float32)
        dkv_spec = pl.BlockSpec((tok, 2 * HD), lambda b, *f: (0, group))

    if not remote:
        body = kernel

        def kernel(*refs):
            body(None, *refs)

    grid_spec = pltpu.PrefetchScalarGridSpec(
        num_scalar_prefetch=1 if remote else 0,
        grid=(nb,),
        in_specs=in_specs,
        out_specs=[dq_spec] + [dkv_spec] * n_pieces,
        scratch_shapes=[
            pltpu.VMEM((hb * tok, HD), jnp.bfloat16),
            pltpu.VMEM((hb * tok, HD), jnp.bfloat16),
            pltpu.VMEM((HD, hb * tok), jnp.float32),
            pltpu.VMEM((HD, n_pieces * tok), jnp.bfloat16),
            pltpu.VMEM((n_pieces, tok, 2 * HD), jnp.float32),
        ],
    )
    outs = pl.pallas_call(
        kernel,
        grid_spec=grid_spec,
        out_shape=[dq_shape] + [dkv_shape] * n_pieces,
        input_output_aliases=aliases,
        compiler_params=pltpu.CompilerParams(dimension_semantics=("arbitrary",)),
    )(*([flags] if remote else []), *args)
    return outs[0], outs[1:]


def combine_call(total, returned, kvh, scale):
    tok = total.shape[0]

    def kernel(t_ref, *rest):
        r_refs = rest[:len(returned)]
        dk_ref, dv_ref = rest[len(returned):]
        tot = t_ref[...]
        for r in r_refs:
            tot = tot + r[...].astype(jnp.float32)
        for g in range(kvh):
            dk_ref[:, g * HD:(g + 1) * HD] = (
                tot[:, 2 * g * HD:(2 * g + 1) * HD] * scale).astype(dk_ref.dtype)
            dv_ref[:, g * HD:(g + 1) * HD] = (
                tot[:, (2 * g + 1) * HD:(2 * g + 2) * HD]).astype(dv_ref.dtype)

    out = jax.ShapeDtypeStruct((tok, kvh * HD), jnp.bfloat16)
    return pl.pallas_call(kernel, out_shape=[out, out])(total, *returned)


def per_device(queries, keys, values, outputs, out_grad, logsumexp, doc_lengths):
    tok, width = queries.shape
    kvh = keys.shape[1] // HD
    reach = -(-(MOST - 1) // tok)
    win = (reach + 1) * tok
    scale = 1.0 / math.sqrt(HD)
    position = lax.axis_index("seq")
    doc_ends = jnp.cumsum(doc_lengths)

    def doc_of(places):
        return jnp.sum((doc_ends[None, :] <= places[:, None]).astype(jnp.int32), axis=1)

    query_places = position * tok + jnp.arange(tok, dtype=jnp.int32)
    query_ids = doc_of(query_places)
    key_places = (position - reach) * tok + jnp.arange(win, dtype=jnp.int32)
    key_ids = jnp.where(key_places >= 0, doc_of(key_places), -1)
    own_visible = (query_ids[:, None] == query_ids[None, :]) & (
        query_places[:, None] <= query_places[None, :])
    bias_own = jnp.where(own_visible, 0.0, -jnp.inf).astype(jnp.float32)
    remote_ids = key_ids[:reach * tok]
    bias_rem = jnp.where(remote_ids[:, None] == query_ids[None, :], 0.0, -jnp.inf
                         ).astype(jnp.float32)
    n_tiles = win // KEY_TILE
    last_places = (position - reach) * tok + KEY_TILE * jnp.arange(
        1, n_tiles + 1, dtype=jnp.int32) - 1
    first_doc = doc_of(position[None] * tok)
    flags = ((doc_of(last_places) == first_doc) & (last_places >= 0)).astype(jnp.int32)

    kv = jnp.concatenate(
        [part for g in range(kvh)
         for part in (keys[:, g * HD:(g + 1) * HD], values[:, g * HD:(g + 1) * HD])], axis=1)
    kv_pieces = [kv] + [shifted(kv, "seq", hop) for hop in range(1, reach + 1)]
    own = (None, queries, out_grad, outputs, logsumexp, bias_own, kv_pieces, reach)
    rem = (flags, queries, out_grad, outputs, logsumexp, bias_rem, kv_pieces, reach)

    dq_part0, (dkv_own0,) = grads_call(0, False, *own)
    dq, dkv_rem = grads_call(0, True, *rem, dq_part=dq_part0)
    dq_part1, dkv_rem = grads_call(1, True, *rem, dkv_alias=dkv_rem)
    returned = [shifted(dkv_rem[reach - hop], "seq", -hop) for hop in range(1, reach + 1)]
    dq, (total,) = grads_call(1, False, *own, dq_part=dq_part1, dq_alias=dq,
                              dkv_alias=[dkv_own0])

    key_grad, value_grad = combine_call(total, returned, kvh, scale)
    return dq, key_grad, value_grad


def solution(mesh):
    in_specs = (
        P(("parts", "seq"), None),
        P(("parts", "seq"), None),
        P(("parts", "seq"), None),
        P(("parts", "seq"), None),
        P(("parts", "seq"), None),
        P(None, ("parts", "seq")),
        P("parts"),
    )
    out_specs = (P(("parts", "seq"), None), P(("parts", "seq"), None), P(("parts", "seq"), None))
    return jax.shard_map(
        per_device, mesh=mesh, in_specs=in_specs, out_specs=out_specs, check_vma=False
    )
```

```python
import math

import jax
import jax.numpy as jnp
from jax import lax
from jax.experimental import pallas as pl
from jax.experimental.pallas import tpu as pltpu
from jax.sharding import PartitionSpec as P

HD = 128
MOST = 512
KEY_TILE = 256
HEADS_PER_STEP = 8
NT_DIMS = (((1,), (1,)), ((), ()))


def shifted(block, axis, distance):
    devices = range(lax.axis_size(axis))
    route = [(i - distance, i) for i in devices if i - distance in devices]
    return lax.ppermute(block, axis, route)


def make_kernel(tok, reach, remote, dq_in, dq_final, n_alias):
    hb = HEADS_PER_STEP
    pieces = list(range(reach)) if remote else [reach]
    tiles_per_piece = tok // KEY_TILE
    n_rows = len(pieces) * tok
    scale = 1.0 / math.sqrt(HD)

    def kernel(flags_ref, q_ref, do_ref, o_ref, lse_ref, bias_ref, *rest):
        rest = list(rest)
        kv_refs = [rest.pop(0) for _ in pieces]
        dqp_ref = rest.pop(0) if dq_in else None
        rest = rest[n_alias:]
        dq_ref = rest.pop(0)
        dkv_refs = [rest.pop(0) for _ in pieces]
        qs_scr, dos_scr, dqt_scr, kt_scr, acc_scr = rest[-5:]
        b = pl.program_id(0)
        nb = pl.num_programs(0)

        @pl.when(b == 0)
        def _():
            acc_scr[...] = jnp.zeros_like(acc_scr)
            for n, kv in enumerate(kv_refs):
                kt_scr[:, n * tok:(n + 1) * tok] = (
                    kv[:, :HD].astype(jnp.float32).T.astype(jnp.bfloat16))

        delta_rows = []
        for i in range(hb):
            cols = slice(i * HD, (i + 1) * HD)
            qs_scr[i * tok:(i + 1) * tok, :] = q_ref[:, cols]
            dos_scr[i * tok:(i + 1) * tok, :] = do_ref[:, cols]
            prod = do_ref[:, cols].astype(jnp.float32) * o_ref[:, cols].astype(jnp.float32)
            delta_rows.append(jnp.sum(prod.T, axis=0, keepdims=True))
        dl_row = jnp.concatenate(delta_rows, axis=1)
        lse_row = jnp.concatenate([lse_ref[i:i + 1, :] for i in range(hb)], axis=1)
        dqt_scr[...] = jnp.zeros_like(dqt_scr)

        for n, piece in enumerate(pieces):
            kv = kv_refs[n]
            for t in range(tiles_per_piece):
                j = piece * tiles_per_piece + t
                rows = slice(t * KEY_TILE, (t + 1) * KEY_TILE)
                loc_rows = slice(n * tok + t * KEY_TILE, n * tok + (t + 1) * KEY_TILE)

                def tile(kv=kv, rows=rows, loc_rows=loc_rows, n=n):
                    k = kv[rows, :HD]
                    v = kv[rows, HD:]
                    qs = qs_scr[...]
                    dos = dos_scr[...]
                    st = lax.dot_general(k, qs, NT_DIMS, preferred_element_type=jnp.float32)
                    bias = bias_ref[loc_rows, :]
                    p = jnp.exp(st * scale - lse_row + jnp.concatenate([bias] * hb, axis=1))
                    dv = jnp.dot(p.astype(jnp.bfloat16), dos, preferred_element_type=jnp.float32)
                    dpt = lax.dot_general(v, dos, NT_DIMS, preferred_element_type=jnp.float32)
                    ds = (p * (dpt - dl_row)).astype(jnp.bfloat16)
                    dk = jnp.dot(ds, qs, preferred_element_type=jnp.float32)
                    acc_scr[n, rows, :HD] += dk
                    acc_scr[n, rows, HD:] += dv
                    dqt_scr[...] += jnp.dot(
                        kt_scr[:, loc_rows], ds, preferred_element_type=jnp.float32)

                if remote:
                    pl.when(flags_ref[j] != 0)(tile)
                else:
                    tile()

        for i in range(hb):
            cols = slice(i * HD, (i + 1) * HD)
            part = dqt_scr[:, i * tok:(i + 1) * tok].T
            if dq_in:
                part = part + dqp_ref[:, cols]
            if dq_final:
                dq_ref[:, cols] = (part * scale).astype(dq_ref.dtype)
            else:
                dq_ref[:, cols] = part

        @pl.when(b == nb - 1)
        def _():
            for n, dkv_ref in enumerate(dkv_refs):
                dkv_ref[...] = acc_scr[n].astype(dkv_ref.dtype)

    return kernel


def grads_call(group, remote, flags, queries, out_grad, outputs, lse, bias, kv_pieces,
               reach, dq_part=None, dq_alias=None, dkv_alias=None):
    tok, width = queries.shape
    n_heads = width // HD
    kvh = kv_pieces[0].shape[1] // (2 * HD)
    heads_per_group = n_heads // kvh
    hb = HEADS_PER_STEP
    nb = heads_per_group // hb
    dq_final = dq_part is not None
    pieces = list(range(reach)) if remote else [reach]
    n_pieces = len(pieces)

    def head_block(b, *f):
        return (0, group * nb + b)

    def lse_block(b, *f):
        return (group * nb + b, 0)

    def local_block(b, *f):
        return (0, b)

    def bias_block(b, *f):
        return (0, 0)

    def kv_block(b, *f):
        return (0, group)

    in_specs = [
        pl.BlockSpec((tok, hb * HD), head_block),
        pl.BlockSpec((tok, hb * HD), head_block),
        pl.BlockSpec((tok, hb * HD), head_block),
        pl.BlockSpec((hb, tok), lse_block),
        pl.BlockSpec((n_pieces * tok, tok), bias_block),
    ] + [pl.BlockSpec((tok, 2 * HD), kv_block) for _ in pieces]
    args = [queries, out_grad, outputs, lse, bias] + [kv_pieces[reach - p] for p in pieces]
    if dq_part is not None:
        in_specs.append(pl.BlockSpec((tok, hb * HD), local_block))
        args.append(dq_part)
    aliases = {}
    if dq_alias is not None:
        aliases[len(args) + int(remote)] = 0
        in_specs.append(pl.BlockSpec(memory_space=pl.ANY))
        args.append(dq_alias)
    if dkv_alias is not None:
        for n, piece_arr in enumerate(dkv_alias):
            aliases[len(args) + int(remote)] = 1 + n
            in_specs.append(pl.BlockSpec(memory_space=pl.ANY))
            args.append(piece_arr)

    kernel = make_kernel(tok, reach, remote, dq_part is not None, dq_final, len(aliases))
    if dq_final:
        dq_shape = jax.ShapeDtypeStruct((tok, width), jnp.bfloat16)
        dq_spec = pl.BlockSpec((tok, hb * HD), head_block)
    else:
        dq_shape = jax.ShapeDtypeStruct((tok, heads_per_group * HD), jnp.float32)
        dq_spec = pl.BlockSpec((tok, hb * HD), local_block)
    if remote:
        dkv_shape = jax.ShapeDtypeStruct((tok, kvh * 2 * HD), jnp.bfloat16)
        dkv_spec = pl.BlockSpec((tok, 2 * HD), lambda b, *f: (0, group))
    else:
        dkv_shape = jax.ShapeDtypeStruct((tok, kvh * 2 * HD), jnp.float32)
        dkv_spec = pl.BlockSpec((tok, 2 * HD), lambda b, *f: (0, group))

    if not remote:
        body = kernel

        def kernel(*refs):
            body(None, *refs)

    grid_spec = pltpu.PrefetchScalarGridSpec(
        num_scalar_prefetch=1 if remote else 0,
        grid=(nb,),
        in_specs=in_specs,
        out_specs=[dq_spec] + [dkv_spec] * n_pieces,
        scratch_shapes=[
            pltpu.VMEM((hb * tok, HD), jnp.bfloat16),
            pltpu.VMEM((hb * tok, HD), jnp.bfloat16),
            pltpu.VMEM((HD, hb * tok), jnp.float32),
            pltpu.VMEM((HD, n_pieces * tok), jnp.bfloat16),
            pltpu.VMEM((n_pieces, tok, 2 * HD), jnp.float32),
        ],
    )
    outs = pl.pallas_call(
        kernel,
        grid_spec=grid_spec,
        out_shape=[dq_shape] + [dkv_shape] * n_pieces,
        input_output_aliases=aliases,
        compiler_params=pltpu.CompilerParams(dimension_semantics=("arbitrary",)),
    )(*([flags] if remote else []), *args)
    return outs[0], outs[1:]


def per_device(queries, keys, values, outputs, out_grad, logsumexp, doc_lengths):
    tok, width = queries.shape
    kvh = keys.shape[1] // HD
    reach = -(-(MOST - 1) // tok)
    win = (reach + 1) * tok
    scale = 1.0 / math.sqrt(HD)
    position = lax.axis_index("seq")
    doc_ends = jnp.cumsum(doc_lengths)

    def doc_of(places):
        return jnp.sum((doc_ends[None, :] <= places[:, None]).astype(jnp.int32), axis=1)

    key_places = (position - reach) * tok + jnp.arange(win, dtype=jnp.int32)
    key_ids = jnp.where(key_places >= 0, doc_of(key_places), -1)
    query_ids = key_ids[reach * tok:]
    query_index = jnp.arange(tok, dtype=jnp.int32)
    own_visible = (query_ids[:, None] == query_ids[None, :]) & (
        query_index[:, None] <= query_index[None, :])
    bias_own = jnp.where(own_visible, 0.0, -jnp.inf).astype(jnp.float32)
    remote_ids = key_ids[:reach * tok]
    bias_rem = jnp.where(remote_ids[:, None] == query_ids[None, :], 0.0, -jnp.inf
                         ).astype(jnp.float32)
    n_tiles = win // KEY_TILE
    flags = (key_ids[KEY_TILE - 1::KEY_TILE] == query_ids[0]).astype(jnp.int32)

    kv = jnp.concatenate(
        [part for g in range(kvh)
         for part in (keys[:, g * HD:(g + 1) * HD], values[:, g * HD:(g + 1) * HD])], axis=1)
    kv_pieces = [kv] + [shifted(kv, "seq", hop) for hop in range(1, reach + 1)]
    own = (None, queries, out_grad, outputs, logsumexp, bias_own, kv_pieces, reach)
    rem = (flags, queries, out_grad, outputs, logsumexp, bias_rem, kv_pieces, reach)

    dq_part0, (dkv_own0,) = grads_call(0, False, *own)
    dq, dkv_rem = grads_call(0, True, *rem, dq_part=dq_part0)
    dq_part1, dkv_rem = grads_call(1, True, *rem, dkv_alias=dkv_rem)
    returned = [shifted(dkv_rem[reach - hop], "seq", -hop) for hop in range(1, reach + 1)]
    dq, (total,) = grads_call(1, False, *own, dq_part=dq_part1, dq_alias=dq,
                              dkv_alias=[dkv_own0])

    for r in returned:
        total = total + r.astype(jnp.float32)
    key_total = jnp.concatenate(
        [total[:, (2 * g) * HD:(2 * g + 1) * HD] for g in range(kvh)], axis=1)
    value_total = jnp.concatenate(
        [total[:, (2 * g + 1) * HD:(2 * g + 2) * HD] for g in range(kvh)], axis=1)
    return (
        dq,
        (key_total * scale).astype(jnp.bfloat16),
        value_total.astype(jnp.bfloat16),
    )


def solution(mesh):
    in_specs = (
        P(("parts", "seq"), None),
        P(("parts", "seq"), None),
        P(("parts", "seq"), None),
        P(("parts", "seq"), None),
        P(("parts", "seq"), None),
        P(None, ("parts", "seq")),
        P("parts"),
    )
    out_specs = (P(("parts", "seq"), None), P(("parts", "seq"), None), P(("parts", "seq"), None))
    return jax.shard_map(
        per_device, mesh=mesh, in_specs=in_specs, out_specs=out_specs, check_vma=False
    )
```

```python
import math

import jax
import jax.numpy as jnp
from jax import lax
from jax.experimental import pallas as pl
from jax.experimental.pallas import tpu as pltpu
from jax.sharding import PartitionSpec as P

HD = 128
MOST = 512
KEY_TILE = 256
HEADS_PER_STEP = 16
NT_DIMS = (((1,), (1,)), ((), ()))


def shifted(block, axis, distance):
    devices = range(lax.axis_size(axis))
    route = [(i - distance, i) for i in devices if i - distance in devices]
    return lax.ppermute(block, axis, route)


def make_kernel(tok, reach, remote, dq_in, dq_final, n_alias):
    hb = HEADS_PER_STEP
    pieces = list(range(reach)) if remote else [reach]
    tiles_per_piece = tok // KEY_TILE
    n_rows = len(pieces) * tok
    scale = 1.0 / math.sqrt(HD)

    def kernel(flags_ref, q_ref, do_ref, o_ref, lse_ref, bias_ref, *rest):
        rest = list(rest)
        kv_refs = [rest.pop(0) for _ in pieces]
        dqp_ref = rest.pop(0) if dq_in else None
        rest = rest[n_alias:]
        dq_ref = rest.pop(0)
        dkv_refs = [rest.pop(0) for _ in pieces]
        qs_scr, dos_scr, dqt_scr, kt_scr, acc_scr = rest[-5:]
        b = pl.program_id(0)
        nb = pl.num_programs(0)

        @pl.when(b == 0)
        def _():
            acc_scr[...] = jnp.zeros_like(acc_scr)
            for n, kv in enumerate(kv_refs):
                kt_scr[:, n * tok:(n + 1) * tok] = (
                    kv[:, :HD].astype(jnp.float32).T.astype(jnp.bfloat16))

        delta_rows = []
        for i in range(hb):
            cols = slice(i * HD, (i + 1) * HD)
            qs_scr[i * tok:(i + 1) * tok, :] = q_ref[:, cols]
            dos_scr[i * tok:(i + 1) * tok, :] = do_ref[:, cols]
            prod = do_ref[:, cols].astype(jnp.float32) * o_ref[:, cols].astype(jnp.float32)
            delta_rows.append(jnp.sum(prod.T, axis=0, keepdims=True))
        dl_row = jnp.concatenate(delta_rows, axis=1)
        lse_row = jnp.concatenate([lse_ref[i:i + 1, :] for i in range(hb)], axis=1)
        dqt_scr[...] = jnp.zeros_like(dqt_scr)

        for n, piece in enumerate(pieces):
            kv = kv_refs[n]
            for t in range(tiles_per_piece):
                j = piece * tiles_per_piece + t
                rows = slice(t * KEY_TILE, (t + 1) * KEY_TILE)
                loc_rows = slice(n * tok + t * KEY_TILE, n * tok + (t + 1) * KEY_TILE)

                def tile(kv=kv, rows=rows, loc_rows=loc_rows, n=n):
                    k = kv[rows, :HD]
                    v = kv[rows, HD:]
                    qs = qs_scr[...]
                    dos = dos_scr[...]
                    st = lax.dot_general(k, qs, NT_DIMS, preferred_element_type=jnp.float32)
                    bias = bias_ref[loc_rows, :]
                    p = jnp.exp(st * scale - lse_row + jnp.concatenate([bias] * hb, axis=1))
                    dv = jnp.dot(p.astype(jnp.bfloat16), dos, preferred_element_type=jnp.float32)
                    dpt = lax.dot_general(v, dos, NT_DIMS, preferred_element_type=jnp.float32)
                    ds = (p * (dpt - dl_row)).astype(jnp.bfloat16)
                    dk = jnp.dot(ds, qs, preferred_element_type=jnp.float32)
                    acc_scr[n, rows, :HD] += dk
                    acc_scr[n, rows, HD:] += dv
                    dqt_scr[...] += jnp.dot(
                        kt_scr[:, loc_rows], ds, preferred_element_type=jnp.float32)

                if remote:
                    pl.when(flags_ref[j] != 0)(tile)
                else:
                    tile()

        for i in range(hb):
            cols = slice(i * HD, (i + 1) * HD)
            part = dqt_scr[:, i * tok:(i + 1) * tok].T
            if dq_in:
                part = part + dqp_ref[:, cols]
            if dq_final:
                dq_ref[:, cols] = (part * scale).astype(dq_ref.dtype)
            else:
                dq_ref[:, cols] = part

        @pl.when(b == nb - 1)
        def _():
            for n, dkv_ref in enumerate(dkv_refs):
                dkv_ref[...] = acc_scr[n].astype(dkv_ref.dtype)

    return kernel


def grads_call(group, remote, flags, queries, out_grad, outputs, lse, bias, kv_pieces,
               reach, dq_part=None, dq_alias=None, dkv_alias=None):
    tok, width = queries.shape
    n_heads = width // HD
    kvh = kv_pieces[0].shape[1] // (2 * HD)
    heads_per_group = n_heads // kvh
    hb = HEADS_PER_STEP
    nb = heads_per_group // hb
    dq_final = dq_part is not None
    pieces = list(range(reach)) if remote else [reach]
    n_pieces = len(pieces)

    def head_block(b, *f):
        return (0, group * nb + b)

    def lse_block(b, *f):
        return (group * nb + b, 0)

    def local_block(b, *f):
        return (0, b)

    def bias_block(b, *f):
        return (0, 0)

    def kv_block(b, *f):
        return (0, group)

    in_specs = [
        pl.BlockSpec((tok, hb * HD), head_block),
        pl.BlockSpec((tok, hb * HD), head_block),
        pl.BlockSpec((tok, hb * HD), head_block),
        pl.BlockSpec((hb, tok), lse_block),
        pl.BlockSpec((n_pieces * tok, tok), bias_block),
    ] + [pl.BlockSpec((tok, 2 * HD), kv_block) for _ in pieces]
    args = [queries, out_grad, outputs, lse, bias] + [kv_pieces[reach - p] for p in pieces]
    if dq_part is not None:
        in_specs.append(pl.BlockSpec((tok, hb * HD), local_block))
        args.append(dq_part)
    aliases = {}
    if dq_alias is not None:
        aliases[len(args) + int(remote)] = 0
        in_specs.append(pl.BlockSpec(memory_space=pl.ANY))
        args.append(dq_alias)
    if dkv_alias is not None:
        for n, piece_arr in enumerate(dkv_alias):
            aliases[len(args) + int(remote)] = 1 + n
            in_specs.append(pl.BlockSpec(memory_space=pl.ANY))
            args.append(piece_arr)

    kernel = make_kernel(tok, reach, remote, dq_part is not None, dq_final, len(aliases))
    if dq_final:
        dq_shape = jax.ShapeDtypeStruct((tok, width), jnp.bfloat16)
        dq_spec = pl.BlockSpec((tok, hb * HD), head_block)
    else:
        dq_shape = jax.ShapeDtypeStruct((tok, heads_per_group * HD), jnp.float32)
        dq_spec = pl.BlockSpec((tok, hb * HD), local_block)
    if remote:
        dkv_shape = jax.ShapeDtypeStruct((tok, kvh * 2 * HD), jnp.bfloat16)
        dkv_spec = pl.BlockSpec((tok, 2 * HD), lambda b, *f: (0, group))
    else:
        dkv_shape = jax.ShapeDtypeStruct((tok, kvh * 2 * HD), jnp.float32)
        dkv_spec = pl.BlockSpec((tok, 2 * HD), lambda b, *f: (0, group))

    if not remote:
        body = kernel

        def kernel(*refs):
            body(None, *refs)

    grid_spec = pltpu.PrefetchScalarGridSpec(
        num_scalar_prefetch=1 if remote else 0,
        grid=(nb,),
        in_specs=in_specs,
        out_specs=[dq_spec] + [dkv_spec] * n_pieces,
        scratch_shapes=[
            pltpu.VMEM((hb * tok, HD), jnp.bfloat16),
            pltpu.VMEM((hb * tok, HD), jnp.bfloat16),
            pltpu.VMEM((HD, hb * tok), jnp.float32),
            pltpu.VMEM((HD, n_pieces * tok), jnp.bfloat16),
            pltpu.VMEM((n_pieces, tok, 2 * HD), jnp.float32),
        ],
    )
    outs = pl.pallas_call(
        kernel,
        grid_spec=grid_spec,
        out_shape=[dq_shape] + [dkv_shape] * n_pieces,
        input_output_aliases=aliases,
        compiler_params=pltpu.CompilerParams(dimension_semantics=("arbitrary",)),
    )(*([flags] if remote else []), *args)
    return outs[0], outs[1:]


def per_device(queries, keys, values, outputs, out_grad, logsumexp, doc_lengths):
    tok, width = queries.shape
    kvh = keys.shape[1] // HD
    reach = -(-(MOST - 1) // tok)
    win = (reach + 1) * tok
    scale = 1.0 / math.sqrt(HD)
    position = lax.axis_index("seq")
    doc_ends = jnp.cumsum(doc_lengths)

    def doc_of(places):
        return jnp.sum((doc_ends[None, :] <= places[:, None]).astype(jnp.int32), axis=1)

    key_places = (position - reach) * tok + jnp.arange(win, dtype=jnp.int32)
    key_ids = jnp.where(key_places >= 0, doc_of(key_places), -1)
    query_ids = key_ids[reach * tok:]
    query_index = jnp.arange(tok, dtype=jnp.int32)
    own_visible = (query_ids[:, None] == query_ids[None, :]) & (
        query_index[:, None] <= query_index[None, :])
    bias_own = jnp.where(own_visible, 0.0, -jnp.inf).astype(jnp.float32)
    remote_ids = key_ids[:reach * tok]
    bias_rem = jnp.where(remote_ids[:, None] == query_ids[None, :], 0.0, -jnp.inf
                         ).astype(jnp.float32)
    n_tiles = win // KEY_TILE
    flags = (key_ids[KEY_TILE - 1::KEY_TILE] == query_ids[0]).astype(jnp.int32)

    kv = jnp.concatenate(
        [part for g in range(kvh)
         for part in (keys[:, g * HD:(g + 1) * HD], values[:, g * HD:(g + 1) * HD])], axis=1)
    kv_pieces = [kv] + [shifted(kv, "seq", hop) for hop in range(1, reach + 1)]
    own = (None, queries, out_grad, outputs, logsumexp, bias_own, kv_pieces, reach)
    rem = (flags, queries, out_grad, outputs, logsumexp, bias_rem, kv_pieces, reach)

    dq_part0, (dkv_own0,) = grads_call(0, False, *own)
    dq, dkv_rem = grads_call(0, True, *rem, dq_part=dq_part0)
    dq_part1, dkv_rem = grads_call(1, True, *rem, dkv_alias=dkv_rem)
    returned = [shifted(dkv_rem[reach - hop], "seq", -hop) for hop in range(1, reach + 1)]
    dq, (total,) = grads_call(1, False, *own, dq_part=dq_part1, dq_alias=dq,
                              dkv_alias=[dkv_own0])

    for r in returned:
        total = total + r.astype(jnp.float32)
    key_total = jnp.concatenate(
        [total[:, (2 * g) * HD:(2 * g + 1) * HD] for g in range(kvh)], axis=1)
    value_total = jnp.concatenate(
        [total[:, (2 * g + 1) * HD:(2 * g + 2) * HD] for g in range(kvh)], axis=1)
    return (
        dq,
        (key_total * scale).astype(jnp.bfloat16),
        value_total.astype(jnp.bfloat16),
    )


def solution(mesh):
    in_specs = (
        P(("parts", "seq"), None),
        P(("parts", "seq"), None),
        P(("parts", "seq"), None),
        P(("parts", "seq"), None),
        P(("parts", "seq"), None),
        P(None, ("parts", "seq")),
        P("parts"),
    )
    out_specs = (P(("parts", "seq"), None), P(("parts", "seq"), None), P(("parts", "seq"), None))
    return jax.shard_map(
        per_device, mesh=mesh, in_specs=in_specs, out_specs=out_specs, check_vma=False
    )
```

```python
import math

import jax
import jax.numpy as jnp
from jax import lax
from jax.experimental import pallas as pl
from jax.experimental.pallas import tpu as pltpu
from jax.sharding import PartitionSpec as P

HD = 128
MOST = 512
KEY_TILE = 256
HEADS_PER_STEP = 8
NT_DIMS = (((1,), (1,)), ((), ()))


def shifted(block, axis, distance):
    devices = range(lax.axis_size(axis))
    route = [(i - distance, i) for i in devices if i - distance in devices]
    return lax.ppermute(block, axis, route)


def make_kernel(tok, pieces, remote, dq_in, dq_final, n_alias):
    hb = HEADS_PER_STEP
    tiles_per_piece = tok // KEY_TILE
    n_rows = len(pieces) * tok
    scale = 1.0 / math.sqrt(HD)

    def kernel(flags_ref, q_ref, do_ref, o_ref, lse_ref, bias_ref, *rest):
        rest = list(rest)
        kv_refs = [rest.pop(0) for _ in pieces]
        dqp_ref = rest.pop(0) if dq_in else None
        rest = rest[n_alias:]
        dq_ref = rest.pop(0)
        dkv_refs = [rest.pop(0) for _ in pieces]
        qs_scr, dos_scr, dqt_scr, kt_scr, acc_scr = rest[-5:]
        b = pl.program_id(0)
        nb = pl.num_programs(0)

        @pl.when(b == 0)
        def _():
            acc_scr[...] = jnp.zeros_like(acc_scr)
            for n, kv in enumerate(kv_refs):
                kt_scr[:, n * tok:(n + 1) * tok] = (
                    kv[:, :HD].astype(jnp.float32).T.astype(jnp.bfloat16))

        delta_rows = []
        for i in range(hb):
            cols = slice(i * HD, (i + 1) * HD)
            qs_scr[i * tok:(i + 1) * tok, :] = q_ref[:, cols]
            dos_scr[i * tok:(i + 1) * tok, :] = do_ref[:, cols]
            prod = do_ref[:, cols].astype(jnp.float32) * o_ref[:, cols].astype(jnp.float32)
            delta_rows.append(jnp.sum(prod.T, axis=0, keepdims=True))
        dl_row = jnp.concatenate(delta_rows, axis=1)
        lse_row = jnp.concatenate([lse_ref[i:i + 1, :] for i in range(hb)], axis=1)
        dqt_scr[...] = jnp.zeros_like(dqt_scr)

        for n, piece in enumerate(pieces):
            kv = kv_refs[n]
            for t in range(tiles_per_piece):
                j = piece * tiles_per_piece + t
                rows = slice(t * KEY_TILE, (t + 1) * KEY_TILE)
                loc_rows = slice(n * tok + t * KEY_TILE, n * tok + (t + 1) * KEY_TILE)

                def tile(kv=kv, rows=rows, loc_rows=loc_rows, n=n):
                    k = kv[rows, :HD]
                    v = kv[rows, HD:]
                    qs = qs_scr[...]
                    dos = dos_scr[...]
                    st = lax.dot_general(k, qs, NT_DIMS, preferred_element_type=jnp.float32)
                    bias = bias_ref[loc_rows, :]
                    p = jnp.exp(st * scale - lse_row + jnp.concatenate([bias] * hb, axis=1))
                    dv = jnp.dot(p.astype(jnp.bfloat16), dos, preferred_element_type=jnp.float32)
                    dpt = lax.dot_general(v, dos, NT_DIMS, preferred_element_type=jnp.float32)
                    ds = (p * (dpt - dl_row)).astype(jnp.bfloat16)
                    dk = jnp.dot(ds, qs, preferred_element_type=jnp.float32)
                    acc_scr[n, rows, :HD] += dk
                    acc_scr[n, rows, HD:] += dv
                    dqt_scr[...] += jnp.dot(
                        kt_scr[:, loc_rows], ds, preferred_element_type=jnp.float32)

                if remote:
                    pl.when(flags_ref[j] != 0)(tile)
                else:
                    tile()

        for i in range(hb):
            cols = slice(i * HD, (i + 1) * HD)
            part = dqt_scr[:, i * tok:(i + 1) * tok].T
            if dq_in:
                part = part + dqp_ref[:, cols]
            if dq_final:
                dq_ref[:, cols] = (part * scale).astype(dq_ref.dtype)
            else:
                dq_ref[:, cols] = part

        @pl.when(b == nb - 1)
        def _():
            for n, dkv_ref in enumerate(dkv_refs):
                dkv_ref[...] = acc_scr[n].astype(dkv_ref.dtype)

    return kernel


def grads_call(group, pieces, flags, queries, out_grad, outputs, lse, bias, kv_pieces,
               reach, dq_part=None, dq_final=False, dq_alias=None, dkv_alias=None):
    remote = pieces[0] < reach
    tok, width = queries.shape
    n_heads = width // HD
    kvh = kv_pieces[0].shape[1] // (2 * HD)
    heads_per_group = n_heads // kvh
    hb = HEADS_PER_STEP
    nb = heads_per_group // hb
    n_pieces = len(pieces)

    def head_block(b, *f):
        return (0, group * nb + b)

    def lse_block(b, *f):
        return (group * nb + b, 0)

    def local_block(b, *f):
        return (0, b)

    def bias_block(b, *f):
        return (pieces[0], 0) if remote else (0, 0)

    def kv_block(b, *f):
        return (0, group)

    in_specs = [
        pl.BlockSpec((tok, hb * HD), head_block),
        pl.BlockSpec((tok, hb * HD), head_block),
        pl.BlockSpec((tok, hb * HD), head_block),
        pl.BlockSpec((hb, tok), lse_block),
        pl.BlockSpec((n_pieces * tok, tok), bias_block),
    ] + [pl.BlockSpec((tok, 2 * HD), kv_block) for _ in pieces]
    args = [queries, out_grad, outputs, lse, bias] + [kv_pieces[reach - p] for p in pieces]
    if dq_part is not None:
        in_specs.append(pl.BlockSpec((tok, hb * HD), local_block))
        args.append(dq_part)
    aliases = {}
    if dq_alias is not None:
        aliases[len(args) + int(remote)] = 0
        in_specs.append(pl.BlockSpec(memory_space=pl.ANY))
        args.append(dq_alias)
    if dkv_alias is not None:
        for n, piece_arr in enumerate(dkv_alias):
            aliases[len(args) + int(remote)] = 1 + n
            in_specs.append(pl.BlockSpec(memory_space=pl.ANY))
            args.append(piece_arr)

    kernel = make_kernel(tok, pieces, remote, dq_part is not None, dq_final, len(aliases))
    if dq_final:
        dq_shape = jax.ShapeDtypeStruct((tok, width), jnp.bfloat16)
        dq_spec = pl.BlockSpec((tok, hb * HD), head_block)
    else:
        dq_shape = jax.ShapeDtypeStruct((tok, heads_per_group * HD), jnp.float32)
        dq_spec = pl.BlockSpec((tok, hb * HD), local_block)
    if remote:
        dkv_shape = jax.ShapeDtypeStruct((tok, kvh * 2 * HD), jnp.bfloat16)
        dkv_spec = pl.BlockSpec((tok, 2 * HD), lambda b, *f: (0, group))
    else:
        dkv_shape = jax.ShapeDtypeStruct((tok, kvh * 2 * HD), jnp.float32)
        dkv_spec = pl.BlockSpec((tok, 2 * HD), lambda b, *f: (0, group))

    if not remote:
        body = kernel

        def kernel(*refs):
            body(None, *refs)

    grid_spec = pltpu.PrefetchScalarGridSpec(
        num_scalar_prefetch=1 if remote else 0,
        grid=(nb,),
        in_specs=in_specs,
        out_specs=[dq_spec] + [dkv_spec] * n_pieces,
        scratch_shapes=[
            pltpu.VMEM((hb * tok, HD), jnp.bfloat16),
            pltpu.VMEM((hb * tok, HD), jnp.bfloat16),
            pltpu.VMEM((HD, hb * tok), jnp.float32),
            pltpu.VMEM((HD, n_pieces * tok), jnp.bfloat16),
            pltpu.VMEM((n_pieces, tok, 2 * HD), jnp.float32),
        ],
    )
    outs = pl.pallas_call(
        kernel,
        grid_spec=grid_spec,
        out_shape=[dq_shape] + [dkv_shape] * n_pieces,
        input_output_aliases=aliases,
        compiler_params=pltpu.CompilerParams(dimension_semantics=("arbitrary",)),
    )(*([flags] if remote else []), *args)
    return outs[0], outs[1:]


def per_device(queries, keys, values, outputs, out_grad, logsumexp, doc_lengths):
    tok, width = queries.shape
    kvh = keys.shape[1] // HD
    reach = -(-(MOST - 1) // tok)
    win = (reach + 1) * tok
    scale = 1.0 / math.sqrt(HD)
    position = lax.axis_index("seq")
    doc_ends = jnp.cumsum(doc_lengths)

    def doc_of(places):
        return jnp.sum((doc_ends[None, :] <= places[:, None]).astype(jnp.int32), axis=1)

    key_places = (position - reach) * tok + jnp.arange(win, dtype=jnp.int32)
    key_ids = jnp.where(key_places >= 0, doc_of(key_places), -1)
    query_ids = key_ids[reach * tok:]
    query_index = jnp.arange(tok, dtype=jnp.int32)
    own_visible = (query_ids[:, None] == query_ids[None, :]) & (
        query_index[:, None] <= query_index[None, :])
    bias_own = jnp.where(own_visible, 0.0, -jnp.inf).astype(jnp.float32)
    remote_ids = key_ids[:reach * tok]
    bias_rem = jnp.where(remote_ids[:, None] == query_ids[None, :], 0.0, -jnp.inf
                         ).astype(jnp.float32)
    n_tiles = win // KEY_TILE
    flags = (key_ids[KEY_TILE - 1::KEY_TILE] == query_ids[0]).astype(jnp.int32)

    kv = jnp.concatenate(
        [part for g in range(kvh)
         for part in (keys[:, g * HD:(g + 1) * HD], values[:, g * HD:(g + 1) * HD])], axis=1)
    kv_pieces = [kv] + [shifted(kv, "seq", hop) for hop in range(1, reach + 1)]
    own = (None, queries, out_grad, outputs, logsumexp, bias_own, kv_pieces, reach)
    rem = (flags, queries, out_grad, outputs, logsumexp, bias_rem, kv_pieces, reach)

    dq_part0, (dkv_own0,) = grads_call(0, [reach], *own)
    dq_part1 = None
    dq = None
    returned = []
    for piece in range(reach):
        last = piece == reach - 1
        dq0, piece0 = grads_call(0, [piece], *rem, dq_part=dq_part0, dq_final=last)
        dq_part1, piece_all = grads_call(1, [piece], *rem, dq_part=dq_part1,
                                         dkv_alias=piece0)
        if last:
            dq = dq0
        else:
            dq_part0 = dq0
        returned.append(shifted(piece_all[0], "seq", piece - reach))
    returned = returned[::-1]
    dq, (total,) = grads_call(1, [reach], *own, dq_part=dq_part1, dq_final=True, dq_alias=dq,
                              dkv_alias=[dkv_own0])

    for r in returned:
        total = total + r.astype(jnp.float32)
    key_total = jnp.concatenate(
        [total[:, (2 * g) * HD:(2 * g + 1) * HD] for g in range(kvh)], axis=1)
    value_total = jnp.concatenate(
        [total[:, (2 * g + 1) * HD:(2 * g + 2) * HD] for g in range(kvh)], axis=1)
    return (
        dq,
        (key_total * scale).astype(jnp.bfloat16),
        value_total.astype(jnp.bfloat16),
    )


def solution(mesh):
    in_specs = (
        P(("parts", "seq"), None),
        P(("parts", "seq"), None),
        P(("parts", "seq"), None),
        P(("parts", "seq"), None),
        P(("parts", "seq"), None),
        P(None, ("parts", "seq")),
        P("parts"),
    )
    out_specs = (P(("parts", "seq"), None), P(("parts", "seq"), None), P(("parts", "seq"), None))
    return jax.shard_map(
        per_device, mesh=mesh, in_specs=in_specs, out_specs=out_specs, check_vma=False
    )
```

```python
import math

import jax
import jax.numpy as jnp
from jax import lax
from jax.experimental import pallas as pl
from jax.experimental.pallas import tpu as pltpu
from jax.sharding import PartitionSpec as P

HD = 128
MOST = 512
KEY_TILE = 256
HEADS_PER_STEP = 8
NT_DIMS = (((1,), (1,)), ((), ()))


def shifted(block, axis, distance):
    devices = range(lax.axis_size(axis))
    route = [(i - distance, i) for i in devices if i - distance in devices]
    return lax.ppermute(block, axis, route)


def make_kernel(tok, reach, remote, dq_in, dq_final, n_alias):
    hb = HEADS_PER_STEP
    pieces = list(range(reach)) if remote else [reach]
    tiles_per_piece = tok // KEY_TILE
    n_rows = len(pieces) * tok
    scale = 1.0 / math.sqrt(HD)

    def kernel(flags_ref, q_ref, do_ref, o_ref, lse_ref, bias_ref, *rest):
        rest = list(rest)
        kv_refs = [rest.pop(0) for _ in pieces]
        dqp_ref = rest.pop(0) if dq_in else None
        rest = rest[n_alias:]
        dq_ref = rest.pop(0)
        dkv_refs = [rest.pop(0) for _ in pieces]
        qs_scr, dos_scr, dqt_scr, kt_scr, acc_scr = rest[-5:]
        b = pl.program_id(0)
        nb = pl.num_programs(0)

        @pl.when(b == 0)
        def _():
            acc_scr[...] = jnp.zeros_like(acc_scr)
            for n, kv in enumerate(kv_refs):
                kt_scr[:, n * tok:(n + 1) * tok] = (
                    kv[:, :HD].astype(jnp.float32).T.astype(jnp.bfloat16))

        delta_rows = []
        for i in range(hb):
            cols = slice(i * HD, (i + 1) * HD)
            qs_scr[i * tok:(i + 1) * tok, :] = q_ref[:, cols]
            dos_scr[i * tok:(i + 1) * tok, :] = do_ref[:, cols]
            prod = do_ref[:, cols].astype(jnp.float32) * o_ref[:, cols].astype(jnp.float32)
            delta_rows.append(jnp.sum(prod.T, axis=0, keepdims=True))
        dl_row = jnp.concatenate(delta_rows, axis=1)
        lse_row = jnp.concatenate([lse_ref[i:i + 1, :] for i in range(hb)], axis=1)
        dqt_scr[...] = jnp.zeros_like(dqt_scr)

        for n, piece in enumerate(pieces):
            kv = kv_refs[n]
            for t in range(tiles_per_piece):
                j = piece * tiles_per_piece + t
                rows = slice(t * KEY_TILE, (t + 1) * KEY_TILE)
                loc_rows = slice(n * tok + t * KEY_TILE, n * tok + (t + 1) * KEY_TILE)

                def tile(kv=kv, rows=rows, loc_rows=loc_rows, n=n):
                    k = kv[rows, :HD]
                    v = kv[rows, HD:]
                    qs = qs_scr[...]
                    dos = dos_scr[...]
                    st = lax.dot_general(k, qs, NT_DIMS, preferred_element_type=jnp.float32)
                    bias = bias_ref[loc_rows, :]
                    p = jnp.exp(st * scale - lse_row + jnp.concatenate([bias] * hb, axis=1))
                    dv = jnp.dot(p.astype(jnp.bfloat16), dos, preferred_element_type=jnp.float32)
                    dpt = lax.dot_general(v, dos, NT_DIMS, preferred_element_type=jnp.float32)
                    ds = (p * (dpt - dl_row)).astype(jnp.bfloat16)
                    dk = jnp.dot(ds, qs, preferred_element_type=jnp.float32)
                    acc_scr[n, rows, :HD] += dk
                    acc_scr[n, rows, HD:] += dv
                    dqt_scr[...] += jnp.dot(
                        kt_scr[:, loc_rows], ds, preferred_element_type=jnp.float32)

                tile()

        for i in range(hb):
            cols = slice(i * HD, (i + 1) * HD)
            part = dqt_scr[:, i * tok:(i + 1) * tok].T
            if dq_in:
                part = part + dqp_ref[:, cols]
            if dq_final:
                dq_ref[:, cols] = (part * scale).astype(dq_ref.dtype)
            else:
                dq_ref[:, cols] = part

        @pl.when(b == nb - 1)
        def _():
            for n, dkv_ref in enumerate(dkv_refs):
                dkv_ref[...] = acc_scr[n].astype(dkv_ref.dtype)

    return kernel


def grads_call(group, remote, flags, queries, out_grad, outputs, lse, bias, kv_pieces,
               reach, dq_part=None, dq_alias=None, dkv_alias=None):
    tok, width = queries.shape
    n_heads = width // HD
    kvh = kv_pieces[0].shape[1] // (2 * HD)
    heads_per_group = n_heads // kvh
    hb = HEADS_PER_STEP
    nb = heads_per_group // hb
    dq_final = dq_part is not None
    pieces = list(range(reach)) if remote else [reach]
    n_pieces = len(pieces)

    def head_block(b, *f):
        return (0, group * nb + b)

    def lse_block(b, *f):
        return (group * nb + b, 0)

    def local_block(b, *f):
        return (0, b)

    def bias_block(b, *f):
        return (0, 0)

    def kv_block(b, *f):
        return (0, group)

    in_specs = [
        pl.BlockSpec((tok, hb * HD), head_block),
        pl.BlockSpec((tok, hb * HD), head_block),
        pl.BlockSpec((tok, hb * HD), head_block),
        pl.BlockSpec((hb, tok), lse_block),
        pl.BlockSpec((n_pieces * tok, tok), bias_block),
    ] + [pl.BlockSpec((tok, 2 * HD), kv_block) for _ in pieces]
    args = [queries, out_grad, outputs, lse, bias] + [kv_pieces[reach - p] for p in pieces]
    if dq_part is not None:
        in_specs.append(pl.BlockSpec((tok, hb * HD), local_block))
        args.append(dq_part)
    aliases = {}
    if dq_alias is not None:
        aliases[len(args)] = 0
        in_specs.append(pl.BlockSpec(memory_space=pl.ANY))
        args.append(dq_alias)
    if dkv_alias is not None:
        for n, piece_arr in enumerate(dkv_alias):
            aliases[len(args)] = 1 + n
            in_specs.append(pl.BlockSpec(memory_space=pl.ANY))
            args.append(piece_arr)

    kernel = make_kernel(tok, reach, remote, dq_part is not None, dq_final, len(aliases))
    if dq_final:
        dq_shape = jax.ShapeDtypeStruct((tok, width), jnp.bfloat16)
        dq_spec = pl.BlockSpec((tok, hb * HD), head_block)
    else:
        dq_shape = jax.ShapeDtypeStruct((tok, heads_per_group * HD), jnp.float32)
        dq_spec = pl.BlockSpec((tok, hb * HD), local_block)
    if remote:
        dkv_shape = jax.ShapeDtypeStruct((tok, kvh * 2 * HD), jnp.bfloat16)
        dkv_spec = pl.BlockSpec((tok, 2 * HD), lambda b, *f: (0, group))
    else:
        dkv_shape = jax.ShapeDtypeStruct((tok, kvh * 2 * HD), jnp.float32)
        dkv_spec = pl.BlockSpec((tok, 2 * HD), lambda b, *f: (0, group))

    body = kernel

    def kernel(*refs):
        body(None, *refs)

    grid_spec = pltpu.PrefetchScalarGridSpec(
        num_scalar_prefetch=0,
        grid=(nb,),
        in_specs=in_specs,
        out_specs=[dq_spec] + [dkv_spec] * n_pieces,
        scratch_shapes=[
            pltpu.VMEM((hb * tok, HD), jnp.bfloat16),
            pltpu.VMEM((hb * tok, HD), jnp.bfloat16),
            pltpu.VMEM((HD, hb * tok), jnp.float32),
            pltpu.VMEM((HD, n_pieces * tok), jnp.bfloat16),
            pltpu.VMEM((n_pieces, tok, 2 * HD), jnp.float32),
        ],
    )
    outs = pl.pallas_call(
        kernel,
        grid_spec=grid_spec,
        out_shape=[dq_shape] + [dkv_shape] * n_pieces,
        input_output_aliases=aliases,
        compiler_params=pltpu.CompilerParams(dimension_semantics=("arbitrary",)),
    )(*args)
    return outs[0], outs[1:]


def per_device(queries, keys, values, outputs, out_grad, logsumexp, doc_lengths):
    tok, width = queries.shape
    kvh = keys.shape[1] // HD
    reach = -(-(MOST - 1) // tok)
    win = (reach + 1) * tok
    scale = 1.0 / math.sqrt(HD)
    position = lax.axis_index("seq")
    doc_ends = jnp.cumsum(doc_lengths)

    def doc_of(places):
        return jnp.sum((doc_ends[None, :] <= places[:, None]).astype(jnp.int32), axis=1)

    key_places = (position - reach) * tok + jnp.arange(win, dtype=jnp.int32)
    key_ids = jnp.where(key_places >= 0, doc_of(key_places), -1)
    query_ids = key_ids[reach * tok:]
    query_index = jnp.arange(tok, dtype=jnp.int32)
    own_visible = (query_ids[:, None] == query_ids[None, :]) & (
        query_index[:, None] <= query_index[None, :])
    bias_own = jnp.where(own_visible, 0.0, -jnp.inf).astype(jnp.float32)
    remote_ids = key_ids[:reach * tok]
    bias_rem = jnp.where(remote_ids[:, None] == query_ids[None, :], 0.0, -jnp.inf
                         ).astype(jnp.float32)

    kv = jnp.concatenate(
        [part for g in range(kvh)
         for part in (keys[:, g * HD:(g + 1) * HD], values[:, g * HD:(g + 1) * HD])], axis=1)
    kv_pieces = [kv] + [shifted(kv, "seq", hop) for hop in range(1, reach + 1)]
    own = (None, queries, out_grad, outputs, logsumexp, bias_own, kv_pieces, reach)
    rem = (None, queries, out_grad, outputs, logsumexp, bias_rem, kv_pieces, reach)

    dq_part0, (dkv_own0,) = grads_call(0, False, *own)
    dq, dkv_rem = grads_call(0, True, *rem, dq_part=dq_part0)
    dq_part1, dkv_rem = grads_call(1, True, *rem, dkv_alias=dkv_rem)
    returned = [shifted(dkv_rem[reach - hop], "seq", -hop) for hop in range(1, reach + 1)]
    dq, (total,) = grads_call(1, False, *own, dq_part=dq_part1, dq_alias=dq,
                              dkv_alias=[dkv_own0])

    for r in returned:
        total = total + r.astype(jnp.float32)
    key_total = jnp.concatenate(
        [total[:, (2 * g) * HD:(2 * g + 1) * HD] for g in range(kvh)], axis=1)
    value_total = jnp.concatenate(
        [total[:, (2 * g + 1) * HD:(2 * g + 2) * HD] for g in range(kvh)], axis=1)
    return (
        dq,
        (key_total * scale).astype(jnp.bfloat16),
        value_total.astype(jnp.bfloat16),
    )


def solution(mesh):
    in_specs = (
        P(("parts", "seq"), None),
        P(("parts", "seq"), None),
        P(("parts", "seq"), None),
        P(("parts", "seq"), None),
        P(("parts", "seq"), None),
        P(None, ("parts", "seq")),
        P("parts"),
    )
    out_specs = (P(("parts", "seq"), None), P(("parts", "seq"), None), P(("parts", "seq"), None))
    return jax.shard_map(
        per_device, mesh=mesh, in_specs=in_specs, out_specs=out_specs, check_vma=False
    )
```

```python
import math

import jax
import jax.numpy as jnp
from jax import lax
from jax.experimental import pallas as pl
from jax.experimental.pallas import tpu as pltpu
from jax.sharding import PartitionSpec as P

HD = 128
MOST = 512
KEY_TILE = 256
HEADS_PER_STEP = 8
NT_DIMS = (((1,), (1,)), ((), ()))


def shifted(block, axis, distance):
    devices = range(lax.axis_size(axis))
    route = [(i - distance, i) for i in devices if i - distance in devices]
    return lax.ppermute(block, axis, route)


def make_kernel(tok, reach, remote, dq_in, dq_final, n_alias, delta_in):
    hb = HEADS_PER_STEP
    pieces = list(range(reach)) if remote else [reach]
    tiles_per_piece = tok // KEY_TILE
    n_rows = len(pieces) * tok
    scale = 1.0 / math.sqrt(HD)

    def kernel(flags_ref, q_ref, do_ref, o_ref, lse_ref, bias_ref, *rest):
        rest = list(rest)
        kv_refs = [rest.pop(0) for _ in pieces]
        dqp_ref = rest.pop(0) if dq_in else None
        rest = rest[n_alias:]
        dq_ref = rest.pop(0)
        dkv_refs = [rest.pop(0) for _ in pieces]
        dl_out = None if delta_in else rest.pop(0)
        qs_scr, dos_scr, dqt_scr, kt_scr, acc_scr = rest[-5:]
        b = pl.program_id(0)
        nb = pl.num_programs(0)

        @pl.when(b == 0)
        def _():
            acc_scr[...] = jnp.zeros_like(acc_scr)
            for n, kv in enumerate(kv_refs):
                kt_scr[:, n * tok:(n + 1) * tok] = (
                    kv[:, :HD].astype(jnp.float32).T.astype(jnp.bfloat16))

        delta_rows = []
        for i in range(hb):
            cols = slice(i * HD, (i + 1) * HD)
            qs_scr[i * tok:(i + 1) * tok, :] = q_ref[:, cols]
            dos_scr[i * tok:(i + 1) * tok, :] = do_ref[:, cols]
            if delta_in:
                delta_rows.append(o_ref[i:i + 1, :])
            else:
                prod = do_ref[:, cols].astype(jnp.float32) * o_ref[:, cols].astype(jnp.float32)
                row = jnp.sum(prod.T, axis=0, keepdims=True)
                dl_out[i:i + 1, :] = row
                delta_rows.append(row)
        dl_row = jnp.concatenate(delta_rows, axis=1)
        lse_row = jnp.concatenate([lse_ref[i:i + 1, :] for i in range(hb)], axis=1)
        dqt_scr[...] = jnp.zeros_like(dqt_scr)

        for n, piece in enumerate(pieces):
            kv = kv_refs[n]
            for t in range(tiles_per_piece):
                j = piece * tiles_per_piece + t
                rows = slice(t * KEY_TILE, (t + 1) * KEY_TILE)
                loc_rows = slice(n * tok + t * KEY_TILE, n * tok + (t + 1) * KEY_TILE)

                def tile(kv=kv, rows=rows, loc_rows=loc_rows, n=n):
                    k = kv[rows, :HD]
                    v = kv[rows, HD:]
                    qs = qs_scr[...]
                    dos = dos_scr[...]
                    st = lax.dot_general(k, qs, NT_DIMS, preferred_element_type=jnp.float32)
                    bias = bias_ref[loc_rows, :]
                    p = jnp.exp(st * scale - lse_row + jnp.concatenate([bias] * hb, axis=1))
                    dv = jnp.dot(p.astype(jnp.bfloat16), dos, preferred_element_type=jnp.float32)
                    dpt = lax.dot_general(v, dos, NT_DIMS, preferred_element_type=jnp.float32)
                    ds = (p * (dpt - dl_row)).astype(jnp.bfloat16)
                    dk = jnp.dot(ds, qs, preferred_element_type=jnp.float32)
                    acc_scr[n, rows, :HD] += dk
                    acc_scr[n, rows, HD:] += dv
                    dqt_scr[...] += jnp.dot(
                        kt_scr[:, loc_rows], ds, preferred_element_type=jnp.float32)

                tile()

        for i in range(hb):
            cols = slice(i * HD, (i + 1) * HD)
            part = dqt_scr[:, i * tok:(i + 1) * tok].T
            if dq_in:
                part = part + dqp_ref[:, cols]
            if dq_final:
                dq_ref[:, cols] = (part * scale).astype(dq_ref.dtype)
            else:
                dq_ref[:, cols] = part

        @pl.when(b == nb - 1)
        def _():
            for n, dkv_ref in enumerate(dkv_refs):
                dkv_ref[...] = acc_scr[n].astype(dkv_ref.dtype)

    return kernel


def grads_call(group, remote, flags, queries, out_grad, outputs, lse, bias, kv_pieces,
               reach, dq_part=None, dq_alias=None, dkv_alias=None, delta=None):
    tok, width = queries.shape
    n_heads = width // HD
    kvh = kv_pieces[0].shape[1] // (2 * HD)
    heads_per_group = n_heads // kvh
    hb = HEADS_PER_STEP
    nb = heads_per_group // hb
    dq_final = dq_part is not None
    pieces = list(range(reach)) if remote else [reach]
    n_pieces = len(pieces)

    def head_block(b, *f):
        return (0, group * nb + b)

    def lse_block(b, *f):
        return (group * nb + b, 0)

    def local_block(b, *f):
        return (0, b)

    def local_rows(b, *f):
        return (b, 0)

    def bias_block(b, *f):
        return (0, 0)

    def kv_block(b, *f):
        return (0, group)

    in_specs = [
        pl.BlockSpec((tok, hb * HD), head_block),
        pl.BlockSpec((tok, hb * HD), head_block),
        pl.BlockSpec((tok, hb * HD), head_block) if delta is None
        else pl.BlockSpec((hb, tok), local_rows),
        pl.BlockSpec((hb, tok), lse_block),
        pl.BlockSpec((n_pieces * tok, tok), bias_block),
    ] + [pl.BlockSpec((tok, 2 * HD), kv_block) for _ in pieces]
    args = [queries, out_grad, outputs if delta is None else delta, lse, bias] + [kv_pieces[reach - p] for p in pieces]
    if dq_part is not None:
        in_specs.append(pl.BlockSpec((tok, hb * HD), local_block))
        args.append(dq_part)
    aliases = {}
    if dq_alias is not None:
        aliases[len(args)] = 0
        in_specs.append(pl.BlockSpec(memory_space=pl.ANY))
        args.append(dq_alias)
    if dkv_alias is not None:
        for n, piece_arr in enumerate(dkv_alias):
            aliases[len(args)] = 1 + n
            in_specs.append(pl.BlockSpec(memory_space=pl.ANY))
            args.append(piece_arr)

    kernel = make_kernel(tok, reach, remote, dq_part is not None, dq_final, len(aliases),
                         delta is not None)
    extra_shape = [] if delta is not None else [
        jax.ShapeDtypeStruct((heads_per_group, tok), jnp.float32)]
    extra_spec = [] if delta is not None else [pl.BlockSpec((hb, tok), local_rows)]
    if dq_final:
        dq_shape = jax.ShapeDtypeStruct((tok, width), jnp.bfloat16)
        dq_spec = pl.BlockSpec((tok, hb * HD), head_block)
    else:
        dq_shape = jax.ShapeDtypeStruct((tok, heads_per_group * HD), jnp.float32)
        dq_spec = pl.BlockSpec((tok, hb * HD), local_block)
    if remote:
        dkv_shape = jax.ShapeDtypeStruct((tok, kvh * 2 * HD), jnp.bfloat16)
        dkv_spec = pl.BlockSpec((tok, 2 * HD), lambda b, *f: (0, group))
    else:
        dkv_shape = jax.ShapeDtypeStruct((tok, kvh * 2 * HD), jnp.float32)
        dkv_spec = pl.BlockSpec((tok, 2 * HD), lambda b, *f: (0, group))

    body = kernel

    def kernel(*refs):
        body(None, *refs)

    grid_spec = pltpu.PrefetchScalarGridSpec(
        num_scalar_prefetch=0,
        grid=(nb,),
        in_specs=in_specs,
        out_specs=[dq_spec] + [dkv_spec] * n_pieces + extra_spec,
        scratch_shapes=[
            pltpu.VMEM((hb * tok, HD), jnp.bfloat16),
            pltpu.VMEM((hb * tok, HD), jnp.bfloat16),
            pltpu.VMEM((HD, hb * tok), jnp.float32),
            pltpu.VMEM((HD, n_pieces * tok), jnp.bfloat16),
            pltpu.VMEM((n_pieces, tok, 2 * HD), jnp.float32),
        ],
    )
    outs = pl.pallas_call(
        kernel,
        grid_spec=grid_spec,
        out_shape=[dq_shape] + [dkv_shape] * n_pieces + extra_shape,
        input_output_aliases=aliases,
        compiler_params=pltpu.CompilerParams(dimension_semantics=("arbitrary",)),
    )(*args)
    return outs[0], outs[1:1 + n_pieces], (outs[-1] if delta is None else delta)


def per_device(queries, keys, values, outputs, out_grad, logsumexp, doc_lengths):
    tok, width = queries.shape
    kvh = keys.shape[1] // HD
    reach = -(-(MOST - 1) // tok)
    win = (reach + 1) * tok
    scale = 1.0 / math.sqrt(HD)
    position = lax.axis_index("seq")
    doc_ends = jnp.cumsum(doc_lengths)

    def doc_of(places):
        return jnp.sum((doc_ends[None, :] <= places[:, None]).astype(jnp.int32), axis=1)

    key_places = (position - reach) * tok + jnp.arange(win, dtype=jnp.int32)
    key_ids = jnp.where(key_places >= 0, doc_of(key_places), -1)
    query_ids = key_ids[reach * tok:]
    query_index = jnp.arange(tok, dtype=jnp.int32)
    own_visible = (query_ids[:, None] == query_ids[None, :]) & (
        query_index[:, None] <= query_index[None, :])
    bias_own = jnp.where(own_visible, 0.0, -jnp.inf).astype(jnp.float32)
    remote_ids = key_ids[:reach * tok]
    bias_rem = jnp.where(remote_ids[:, None] == query_ids[None, :], 0.0, -jnp.inf
                         ).astype(jnp.float32)

    kv = jnp.concatenate(
        [part for g in range(kvh)
         for part in (keys[:, g * HD:(g + 1) * HD], values[:, g * HD:(g + 1) * HD])], axis=1)
    kv_pieces = [kv] + [shifted(kv, "seq", hop) for hop in range(1, reach + 1)]
    own = (None, queries, out_grad, outputs, logsumexp, bias_own, kv_pieces, reach)
    rem = (None, queries, out_grad, outputs, logsumexp, bias_rem, kv_pieces, reach)

    dq_part0, (dkv_own0,), delta0 = grads_call(0, False, *own)
    dq, dkv_rem, _ = grads_call(0, True, *rem, dq_part=dq_part0, delta=delta0)
    dq_part1, dkv_rem, delta1 = grads_call(1, True, *rem, dkv_alias=dkv_rem)
    returned = [shifted(dkv_rem[reach - hop], "seq", -hop) for hop in range(1, reach + 1)]
    dq, (total,), _ = grads_call(1, False, *own, dq_part=dq_part1, dq_alias=dq,
                                 dkv_alias=[dkv_own0], delta=delta1)

    for r in returned:
        total = total + r.astype(jnp.float32)
    key_total = jnp.concatenate(
        [total[:, (2 * g) * HD:(2 * g + 1) * HD] for g in range(kvh)], axis=1)
    value_total = jnp.concatenate(
        [total[:, (2 * g + 1) * HD:(2 * g + 2) * HD] for g in range(kvh)], axis=1)
    return (
        dq,
        (key_total * scale).astype(jnp.bfloat16),
        value_total.astype(jnp.bfloat16),
    )


def solution(mesh):
    in_specs = (
        P(("parts", "seq"), None),
        P(("parts", "seq"), None),
        P(("parts", "seq"), None),
        P(("parts", "seq"), None),
        P(("parts", "seq"), None),
        P(None, ("parts", "seq")),
        P("parts"),
    )
    out_specs = (P(("parts", "seq"), None), P(("parts", "seq"), None), P(("parts", "seq"), None))
    return jax.shard_map(
        per_device, mesh=mesh, in_specs=in_specs, out_specs=out_specs, check_vma=False
    )
```

```python
import math

import jax
import jax.numpy as jnp
from jax import lax
from jax.experimental import pallas as pl
from jax.experimental.pallas import tpu as pltpu
from jax.sharding import PartitionSpec as P

HD = 128
MOST = 512
KEY_TILE = 256
HEADS_PER_STEP = 8
NT_DIMS = (((1,), (1,)), ((), ()))


def shifted(block, axis, distance):
    devices = range(lax.axis_size(axis))
    route = [(i - distance, i) for i in devices if i - distance in devices]
    return lax.ppermute(block, axis, route)


def make_kernel(tok, reach, remote, dq_in, dq_final, n_alias, delta_in):
    hb = HEADS_PER_STEP
    pieces = list(range(reach)) if remote else [reach]
    tiles_per_piece = tok // KEY_TILE
    n_rows = len(pieces) * tok
    scale = 1.0 / math.sqrt(HD)

    def kernel(flags_ref, q_ref, do_ref, o_ref, lse_ref, bias_ref, *rest):
        rest = list(rest)
        kv_refs = [rest.pop(0) for _ in pieces]
        dqp_ref = rest.pop(0) if dq_in else None
        rest = rest[n_alias:]
        dq_ref = rest.pop(0)
        dkv_refs = [rest.pop(0) for _ in pieces]
        dl_out = None if delta_in else rest.pop(0)
        qs_scr, dos_scr, dqt_scr, kt_scr, acc_scr = rest[-5:]
        b = pl.program_id(0)
        nb = pl.num_programs(0)

        @pl.when(b == 0)
        def _():
            acc_scr[...] = jnp.zeros_like(acc_scr)
            for n, kv in enumerate(kv_refs):
                kt_scr[:, n * tok:(n + 1) * tok] = (
                    kv[:, :HD].astype(jnp.float32).T.astype(jnp.bfloat16))

        delta_rows = []
        for i in range(hb):
            cols = slice(i * HD, (i + 1) * HD)
            qs_scr[i * tok:(i + 1) * tok, :] = q_ref[:, cols]
            dos_scr[i * tok:(i + 1) * tok, :] = do_ref[:, cols]
            if delta_in:
                delta_rows.append(o_ref[i:i + 1, :])
            else:
                prod = do_ref[:, cols].astype(jnp.float32) * o_ref[:, cols].astype(jnp.float32)
                row = jnp.sum(prod.T, axis=0, keepdims=True)
                dl_out[i:i + 1, :] = row
                delta_rows.append(row)
        dl_row = jnp.concatenate(delta_rows, axis=1)
        lse_row = jnp.concatenate([lse_ref[i:i + 1, :] for i in range(hb)], axis=1)
        dqt_scr[...] = jnp.zeros_like(dqt_scr)

        if tiles_per_piece == 1 and len(pieces) > 1:
            k = jnp.concatenate([kv[:, :HD] for kv in kv_refs], axis=0)
            v = jnp.concatenate([kv[:, HD:] for kv in kv_refs], axis=0)
            qs = qs_scr[...]
            dos = dos_scr[...]
            st = lax.dot_general(k, qs, NT_DIMS, preferred_element_type=jnp.float32)
            bias = bias_ref[...]
            p = jnp.exp(st * scale - lse_row + jnp.concatenate([bias] * hb, axis=1))
            dv = jnp.dot(p.astype(jnp.bfloat16), dos, preferred_element_type=jnp.float32)
            dpt = lax.dot_general(v, dos, NT_DIMS, preferred_element_type=jnp.float32)
            ds = (p * (dpt - dl_row)).astype(jnp.bfloat16)
            dk = jnp.dot(ds, qs, preferred_element_type=jnp.float32)
            for n in range(len(pieces)):
                acc_scr[n, :, :HD] += dk[n * tok:(n + 1) * tok]
                acc_scr[n, :, HD:] += dv[n * tok:(n + 1) * tok]
            dqt_scr[...] += jnp.dot(kt_scr[...], ds, preferred_element_type=jnp.float32)
            tiles_per_piece_loop = 0
        else:
            tiles_per_piece_loop = tiles_per_piece

        for n, piece in enumerate(pieces):
            kv = kv_refs[n]
            for t in range(tiles_per_piece_loop):
                j = piece * tiles_per_piece + t
                rows = slice(t * KEY_TILE, (t + 1) * KEY_TILE)
                loc_rows = slice(n * tok + t * KEY_TILE, n * tok + (t + 1) * KEY_TILE)

                def tile(kv=kv, rows=rows, loc_rows=loc_rows, n=n):
                    k = kv[rows, :HD]
                    v = kv[rows, HD:]
                    qs = qs_scr[...]
                    dos = dos_scr[...]
                    st = lax.dot_general(k, qs, NT_DIMS, preferred_element_type=jnp.float32)
                    bias = bias_ref[loc_rows, :]
                    p = jnp.exp(st * scale - lse_row + jnp.concatenate([bias] * hb, axis=1))
                    dv = jnp.dot(p.astype(jnp.bfloat16), dos, preferred_element_type=jnp.float32)
                    dpt = lax.dot_general(v, dos, NT_DIMS, preferred_element_type=jnp.float32)
                    ds = (p * (dpt - dl_row)).astype(jnp.bfloat16)
                    dk = jnp.dot(ds, qs, preferred_element_type=jnp.float32)
                    acc_scr[n, rows, :HD] += dk
                    acc_scr[n, rows, HD:] += dv
                    dqt_scr[...] += jnp.dot(
                        kt_scr[:, loc_rows], ds, preferred_element_type=jnp.float32)

                tile()

        for i in range(hb):
            cols = slice(i * HD, (i + 1) * HD)
            part = dqt_scr[:, i * tok:(i + 1) * tok].T
            if dq_in:
                part = part + dqp_ref[:, cols]
            if dq_final:
                dq_ref[:, cols] = (part * scale).astype(dq_ref.dtype)
            else:
                dq_ref[:, cols] = part

        @pl.when(b == nb - 1)
        def _():
            for n, dkv_ref in enumerate(dkv_refs):
                dkv_ref[...] = acc_scr[n].astype(dkv_ref.dtype)

    return kernel


def grads_call(group, remote, flags, queries, out_grad, outputs, lse, bias, kv_pieces,
               reach, dq_part=None, dq_alias=None, dkv_alias=None, delta=None):
    tok, width = queries.shape
    n_heads = width // HD
    kvh = kv_pieces[0].shape[1] // (2 * HD)
    heads_per_group = n_heads // kvh
    hb = HEADS_PER_STEP
    nb = heads_per_group // hb
    dq_final = dq_part is not None
    pieces = list(range(reach)) if remote else [reach]
    n_pieces = len(pieces)

    def head_block(b, *f):
        return (0, group * nb + b)

    def lse_block(b, *f):
        return (group * nb + b, 0)

    def local_block(b, *f):
        return (0, b)

    def local_rows(b, *f):
        return (b, 0)

    def bias_block(b, *f):
        return (0, 0)

    def kv_block(b, *f):
        return (0, group)

    in_specs = [
        pl.BlockSpec((tok, hb * HD), head_block),
        pl.BlockSpec((tok, hb * HD), head_block),
        pl.BlockSpec((tok, hb * HD), head_block) if delta is None
        else pl.BlockSpec((hb, tok), local_rows),
        pl.BlockSpec((hb, tok), lse_block),
        pl.BlockSpec((n_pieces * tok, tok), bias_block),
    ] + [pl.BlockSpec((tok, 2 * HD), kv_block) for _ in pieces]
    args = [queries, out_grad, outputs if delta is None else delta, lse, bias] + [kv_pieces[reach - p] for p in pieces]
    if dq_part is not None:
        in_specs.append(pl.BlockSpec((tok, hb * HD), local_block))
        args.append(dq_part)
    aliases = {}
    if dq_alias is not None:
        aliases[len(args)] = 0
        in_specs.append(pl.BlockSpec(memory_space=pl.ANY))
        args.append(dq_alias)
    if dkv_alias is not None:
        for n, piece_arr in enumerate(dkv_alias):
            aliases[len(args)] = 1 + n
            in_specs.append(pl.BlockSpec(memory_space=pl.ANY))
            args.append(piece_arr)

    kernel = make_kernel(tok, reach, remote, dq_part is not None, dq_final, len(aliases),
                         delta is not None)
    extra_shape = [] if delta is not None else [
        jax.ShapeDtypeStruct((heads_per_group, tok), jnp.float32)]
    extra_spec = [] if delta is not None else [pl.BlockSpec((hb, tok), local_rows)]
    if dq_final:
        dq_shape = jax.ShapeDtypeStruct((tok, width), jnp.bfloat16)
        dq_spec = pl.BlockSpec((tok, hb * HD), head_block)
    else:
        dq_shape = jax.ShapeDtypeStruct((tok, heads_per_group * HD), jnp.float32)
        dq_spec = pl.BlockSpec((tok, hb * HD), local_block)
    if remote:
        dkv_shape = jax.ShapeDtypeStruct((tok, kvh * 2 * HD), jnp.bfloat16)
        dkv_spec = pl.BlockSpec((tok, 2 * HD), lambda b, *f: (0, group))
    else:
        dkv_shape = jax.ShapeDtypeStruct((tok, kvh * 2 * HD), jnp.float32)
        dkv_spec = pl.BlockSpec((tok, 2 * HD), lambda b, *f: (0, group))

    body = kernel

    def kernel(*refs):
        body(None, *refs)

    grid_spec = pltpu.PrefetchScalarGridSpec(
        num_scalar_prefetch=0,
        grid=(nb,),
        in_specs=in_specs,
        out_specs=[dq_spec] + [dkv_spec] * n_pieces + extra_spec,
        scratch_shapes=[
            pltpu.VMEM((hb * tok, HD), jnp.bfloat16),
            pltpu.VMEM((hb * tok, HD), jnp.bfloat16),
            pltpu.VMEM((HD, hb * tok), jnp.float32),
            pltpu.VMEM((HD, n_pieces * tok), jnp.bfloat16),
            pltpu.VMEM((n_pieces, tok, 2 * HD), jnp.float32),
        ],
    )
    outs = pl.pallas_call(
        kernel,
        grid_spec=grid_spec,
        out_shape=[dq_shape] + [dkv_shape] * n_pieces + extra_shape,
        input_output_aliases=aliases,
        compiler_params=pltpu.CompilerParams(dimension_semantics=("arbitrary",)),
    )(*args)
    return outs[0], outs[1:1 + n_pieces], (outs[-1] if delta is None else delta)


def per_device(queries, keys, values, outputs, out_grad, logsumexp, doc_lengths):
    tok, width = queries.shape
    kvh = keys.shape[1] // HD
    reach = -(-(MOST - 1) // tok)
    win = (reach + 1) * tok
    scale = 1.0 / math.sqrt(HD)
    position = lax.axis_index("seq")
    doc_ends = jnp.cumsum(doc_lengths)

    def doc_of(places):
        return jnp.sum((doc_ends[None, :] <= places[:, None]).astype(jnp.int32), axis=1)

    key_places = (position - reach) * tok + jnp.arange(win, dtype=jnp.int32)
    key_ids = jnp.where(key_places >= 0, doc_of(key_places), -1)
    query_ids = key_ids[reach * tok:]
    query_index = jnp.arange(tok, dtype=jnp.int32)
    own_visible = (query_ids[:, None] == query_ids[None, :]) & (
        query_index[:, None] <= query_index[None, :])
    bias_own = jnp.where(own_visible, 0.0, -jnp.inf).astype(jnp.float32)
    remote_ids = key_ids[:reach * tok]
    bias_rem = jnp.where(remote_ids[:, None] == query_ids[None, :], 0.0, -jnp.inf
                         ).astype(jnp.float32)

    kv = jnp.concatenate(
        [part for g in range(kvh)
         for part in (keys[:, g * HD:(g + 1) * HD], values[:, g * HD:(g + 1) * HD])], axis=1)
    kv_pieces = [kv] + [shifted(kv, "seq", hop) for hop in range(1, reach + 1)]
    own = (None, queries, out_grad, outputs, logsumexp, bias_own, kv_pieces, reach)
    rem = (None, queries, out_grad, outputs, logsumexp, bias_rem, kv_pieces, reach)

    dq_part0, (dkv_own0,), delta0 = grads_call(0, False, *own)
    dq, dkv_rem, _ = grads_call(0, True, *rem, dq_part=dq_part0, delta=delta0)
    dq_part1, dkv_rem, delta1 = grads_call(1, True, *rem, dkv_alias=dkv_rem)
    returned = [shifted(dkv_rem[reach - hop], "seq", -hop) for hop in range(1, reach + 1)]
    dq, (total,), _ = grads_call(1, False, *own, dq_part=dq_part1, dq_alias=dq,
                                 dkv_alias=[dkv_own0], delta=delta1)

    for r in returned:
        total = total + r.astype(jnp.float32)
    key_total = jnp.concatenate(
        [total[:, (2 * g) * HD:(2 * g + 1) * HD] for g in range(kvh)], axis=1)
    value_total = jnp.concatenate(
        [total[:, (2 * g + 1) * HD:(2 * g + 2) * HD] for g in range(kvh)], axis=1)
    return (
        dq,
        (key_total * scale).astype(jnp.bfloat16),
        value_total.astype(jnp.bfloat16),
    )


def solution(mesh):
    in_specs = (
        P(("parts", "seq"), None),
        P(("parts", "seq"), None),
        P(("parts", "seq"), None),
        P(("parts", "seq"), None),
        P(("parts", "seq"), None),
        P(None, ("parts", "seq")),
        P("parts"),
    )
    out_specs = (P(("parts", "seq"), None), P(("parts", "seq"), None), P(("parts", "seq"), None))
    return jax.shard_map(
        per_device, mesh=mesh, in_specs=in_specs, out_specs=out_specs, check_vma=False
    )
```

```python
import math

import jax
import jax.numpy as jnp
from jax import lax
from jax.experimental import pallas as pl
from jax.experimental.pallas import tpu as pltpu
from jax.sharding import PartitionSpec as P

HD = 128
MOST = 512
KEY_TILE = 256
HEADS_PER_STEP = 8
NT_DIMS = (((1,), (1,)), ((), ()))


def shifted(block, axis, distance):
    devices = range(lax.axis_size(axis))
    route = [(i - distance, i) for i in devices if i - distance in devices]
    return lax.ppermute(block, axis, route)


def make_kernel(tok, reach, remote, dq_in, dq_final, n_alias, delta_in):
    hb = HEADS_PER_STEP
    pieces = list(range(reach)) if remote else [reach]
    tiles_per_piece = tok // KEY_TILE
    n_rows = len(pieces) * tok
    scale = 1.0 / math.sqrt(HD)

    def kernel(flags_ref, q_ref, do_ref, o_ref, lse_ref, bias_ref, *rest):
        rest = list(rest)
        kv_refs = [rest.pop(0) for _ in pieces]
        dqp_ref = rest.pop(0) if dq_in else None
        rest = rest[n_alias:]
        dq_ref = rest.pop(0)
        dkv_refs = [rest.pop(0) for _ in pieces]
        dl_out = None if delta_in else rest.pop(0)
        qs_out = None if delta_in else rest.pop(0)
        dos_out = None if delta_in else rest.pop(0)
        _, _, dqt_scr, kt_scr, acc_scr = rest[-5:]
        b = pl.program_id(0)
        nb = pl.num_programs(0)

        @pl.when(b == 0)
        def _():
            acc_scr[...] = jnp.zeros_like(acc_scr)
            for n, kv in enumerate(kv_refs):
                kt_scr[:, n * tok:(n + 1) * tok] = (
                    kv[:, :HD].astype(jnp.float32).T.astype(jnp.bfloat16))

        if delta_in:
            qs_scr, dos_scr = q_ref, do_ref
        else:
            qs_scr, dos_scr = qs_out, dos_out
        delta_rows = []
        for i in range(hb):
            cols = slice(i * HD, (i + 1) * HD)
            if not delta_in:
                qs_scr[i * tok:(i + 1) * tok, :] = q_ref[:, cols]
                dos_scr[i * tok:(i + 1) * tok, :] = do_ref[:, cols]
            if delta_in:
                delta_rows.append(o_ref[i:i + 1, :])
            else:
                prod = do_ref[:, cols].astype(jnp.float32) * o_ref[:, cols].astype(jnp.float32)
                row = jnp.sum(prod.T, axis=0, keepdims=True)
                dl_out[i:i + 1, :] = row
                delta_rows.append(row)
        dl_row = jnp.concatenate(delta_rows, axis=1)
        lse_row = jnp.concatenate([lse_ref[i:i + 1, :] for i in range(hb)], axis=1)
        dqt_scr[...] = jnp.zeros_like(dqt_scr)

        if tiles_per_piece == 1 and len(pieces) > 1:
            k = jnp.concatenate([kv[:, :HD] for kv in kv_refs], axis=0)
            v = jnp.concatenate([kv[:, HD:] for kv in kv_refs], axis=0)
            qs = qs_scr[...]
            dos = dos_scr[...]
            st = lax.dot_general(k, qs, NT_DIMS, preferred_element_type=jnp.float32)
            bias = bias_ref[...]
            p = jnp.exp(st * scale - lse_row + jnp.concatenate([bias] * hb, axis=1))
            dv = jnp.dot(p.astype(jnp.bfloat16), dos, preferred_element_type=jnp.float32)
            dpt = lax.dot_general(v, dos, NT_DIMS, preferred_element_type=jnp.float32)
            ds = (p * (dpt - dl_row)).astype(jnp.bfloat16)
            dk = jnp.dot(ds, qs, preferred_element_type=jnp.float32)
            for n in range(len(pieces)):
                acc_scr[n, :, :HD] += dk[n * tok:(n + 1) * tok]
                acc_scr[n, :, HD:] += dv[n * tok:(n + 1) * tok]
            dqt_scr[...] += jnp.dot(kt_scr[...], ds, preferred_element_type=jnp.float32)
            tiles_per_piece_loop = 0
        else:
            tiles_per_piece_loop = tiles_per_piece

        for n, piece in enumerate(pieces):
            kv = kv_refs[n]
            for t in range(tiles_per_piece_loop):
                j = piece * tiles_per_piece + t
                rows = slice(t * KEY_TILE, (t + 1) * KEY_TILE)
                loc_rows = slice(n * tok + t * KEY_TILE, n * tok + (t + 1) * KEY_TILE)

                def tile(kv=kv, rows=rows, loc_rows=loc_rows, n=n):
                    k = kv[rows, :HD]
                    v = kv[rows, HD:]
                    qs = qs_scr[...]
                    dos = dos_scr[...]
                    st = lax.dot_general(k, qs, NT_DIMS, preferred_element_type=jnp.float32)
                    bias = bias_ref[loc_rows, :]
                    p = jnp.exp(st * scale - lse_row + jnp.concatenate([bias] * hb, axis=1))
                    dv = jnp.dot(p.astype(jnp.bfloat16), dos, preferred_element_type=jnp.float32)
                    dpt = lax.dot_general(v, dos, NT_DIMS, preferred_element_type=jnp.float32)
                    ds = (p * (dpt - dl_row)).astype(jnp.bfloat16)
                    dk = jnp.dot(ds, qs, preferred_element_type=jnp.float32)
                    acc_scr[n, rows, :HD] += dk
                    acc_scr[n, rows, HD:] += dv
                    dqt_scr[...] += jnp.dot(
                        kt_scr[:, loc_rows], ds, preferred_element_type=jnp.float32)

                tile()

        for i in range(hb):
            cols = slice(i * HD, (i + 1) * HD)
            part = dqt_scr[:, i * tok:(i + 1) * tok].T
            if dq_in:
                part = part + dqp_ref[:, cols]
            if dq_final:
                dq_ref[:, cols] = (part * scale).astype(dq_ref.dtype)
            else:
                dq_ref[:, cols] = part

        @pl.when(b == nb - 1)
        def _():
            for n, dkv_ref in enumerate(dkv_refs):
                dkv_ref[...] = acc_scr[n].astype(dkv_ref.dtype)

    return kernel


def grads_call(group, remote, flags, queries, out_grad, outputs, lse, bias, kv_pieces,
               reach, dq_part=None, dq_alias=None, dkv_alias=None, delta=None):
    tok, width = queries.shape
    n_heads = width // HD
    kvh = kv_pieces[0].shape[1] // (2 * HD)
    heads_per_group = n_heads // kvh
    hb = HEADS_PER_STEP
    nb = heads_per_group // hb
    dq_final = dq_part is not None
    pieces = list(range(reach)) if remote else [reach]
    n_pieces = len(pieces)

    def head_block(b, *f):
        return (0, group * nb + b)

    def lse_block(b, *f):
        return (group * nb + b, 0)

    def local_block(b, *f):
        return (0, b)

    def local_rows(b, *f):
        return (b, 0)

    def bias_block(b, *f):
        return (0, 0)

    def kv_block(b, *f):
        return (0, group)

    stacked = pl.BlockSpec((hb * tok, HD), local_rows)
    in_specs = [
        pl.BlockSpec((tok, hb * HD), head_block) if delta is None else stacked,
        pl.BlockSpec((tok, hb * HD), head_block) if delta is None else stacked,
        pl.BlockSpec((tok, hb * HD), head_block) if delta is None
        else pl.BlockSpec((hb, tok), local_rows),
        pl.BlockSpec((hb, tok), lse_block),
        pl.BlockSpec((n_pieces * tok, tok), bias_block),
    ] + [pl.BlockSpec((tok, 2 * HD), kv_block) for _ in pieces]
    if delta is not None:
        delta, queries, out_grad = delta
    args = [queries, out_grad, outputs if delta is None else delta, lse, bias] + [kv_pieces[reach - p] for p in pieces]
    if dq_part is not None:
        in_specs.append(pl.BlockSpec((tok, hb * HD), local_block))
        args.append(dq_part)
    aliases = {}
    if dq_alias is not None:
        aliases[len(args)] = 0
        in_specs.append(pl.BlockSpec(memory_space=pl.ANY))
        args.append(dq_alias)
    if dkv_alias is not None:
        for n, piece_arr in enumerate(dkv_alias):
            aliases[len(args)] = 1 + n
            in_specs.append(pl.BlockSpec(memory_space=pl.ANY))
            args.append(piece_arr)

    kernel = make_kernel(tok, reach, remote, dq_part is not None, dq_final, len(aliases),
                         delta is not None)
    stack_shape = jax.ShapeDtypeStruct((heads_per_group * tok, HD), jnp.bfloat16)
    extra_shape = [] if delta is not None else [
        jax.ShapeDtypeStruct((heads_per_group, tok), jnp.float32), stack_shape, stack_shape]
    extra_spec = [] if delta is not None else [
        pl.BlockSpec((hb, tok), local_rows), pl.BlockSpec((hb * tok, HD), local_rows),
        pl.BlockSpec((hb * tok, HD), local_rows)]
    if dq_final:
        dq_shape = jax.ShapeDtypeStruct((tok, width), jnp.bfloat16)
        dq_spec = pl.BlockSpec((tok, hb * HD), head_block)
    else:
        dq_shape = jax.ShapeDtypeStruct((tok, heads_per_group * HD), jnp.float32)
        dq_spec = pl.BlockSpec((tok, hb * HD), local_block)
    if remote:
        dkv_shape = jax.ShapeDtypeStruct((tok, kvh * 2 * HD), jnp.bfloat16)
        dkv_spec = pl.BlockSpec((tok, 2 * HD), lambda b, *f: (0, group))
    else:
        dkv_shape = jax.ShapeDtypeStruct((tok, kvh * 2 * HD), jnp.float32)
        dkv_spec = pl.BlockSpec((tok, 2 * HD), lambda b, *f: (0, group))

    body = kernel

    def kernel(*refs):
        body(None, *refs)

    grid_spec = pltpu.PrefetchScalarGridSpec(
        num_scalar_prefetch=0,
        grid=(nb,),
        in_specs=in_specs,
        out_specs=[dq_spec] + [dkv_spec] * n_pieces + extra_spec,
        scratch_shapes=[
            pltpu.VMEM((hb * tok, HD), jnp.bfloat16),
            pltpu.VMEM((hb * tok, HD), jnp.bfloat16),
            pltpu.VMEM((HD, hb * tok), jnp.float32),
            pltpu.VMEM((HD, n_pieces * tok), jnp.bfloat16),
            pltpu.VMEM((n_pieces, tok, 2 * HD), jnp.float32),
        ],
    )
    outs = pl.pallas_call(
        kernel,
        grid_spec=grid_spec,
        out_shape=[dq_shape] + [dkv_shape] * n_pieces + extra_shape,
        input_output_aliases=aliases,
        compiler_params=pltpu.CompilerParams(dimension_semantics=("arbitrary",)),
    )(*args)
    return outs[0], outs[1:1 + n_pieces], (tuple(outs[-3:]) if delta is None else None)


def per_device(queries, keys, values, outputs, out_grad, logsumexp, doc_lengths):
    tok, width = queries.shape
    kvh = keys.shape[1] // HD
    reach = -(-(MOST - 1) // tok)
    win = (reach + 1) * tok
    scale = 1.0 / math.sqrt(HD)
    position = lax.axis_index("seq")
    doc_ends = jnp.cumsum(doc_lengths)

    def doc_of(places):
        return jnp.sum((doc_ends[None, :] <= places[:, None]).astype(jnp.int32), axis=1)

    key_places = (position - reach) * tok + jnp.arange(win, dtype=jnp.int32)
    key_ids = jnp.where(key_places >= 0, doc_of(key_places), -1)
    query_ids = key_ids[reach * tok:]
    query_index = jnp.arange(tok, dtype=jnp.int32)
    own_visible = (query_ids[:, None] == query_ids[None, :]) & (
        query_index[:, None] <= query_index[None, :])
    bias_own = jnp.where(own_visible, 0.0, -jnp.inf).astype(jnp.float32)
    remote_ids = key_ids[:reach * tok]
    bias_rem = jnp.where(remote_ids[:, None] == query_ids[None, :], 0.0, -jnp.inf
                         ).astype(jnp.float32)

    kv = jnp.concatenate(
        [part for g in range(kvh)
         for part in (keys[:, g * HD:(g + 1) * HD], values[:, g * HD:(g + 1) * HD])], axis=1)
    kv_pieces = [kv] + [shifted(kv, "seq", hop) for hop in range(1, reach + 1)]
    own = (None, queries, out_grad, outputs, logsumexp, bias_own, kv_pieces, reach)
    rem = (None, queries, out_grad, outputs, logsumexp, bias_rem, kv_pieces, reach)

    dq_part0, (dkv_own0,), delta0 = grads_call(0, False, *own)
    dq, dkv_rem, _ = grads_call(0, True, *rem, dq_part=dq_part0, delta=delta0)
    dq_part1, dkv_rem, delta1 = grads_call(1, True, *rem, dkv_alias=dkv_rem)
    returned = [shifted(dkv_rem[reach - hop], "seq", -hop) for hop in range(1, reach + 1)]
    dq, (total,), _ = grads_call(1, False, *own, dq_part=dq_part1, dq_alias=dq,
                                 dkv_alias=[dkv_own0], delta=delta1)

    for r in returned:
        total = total + r.astype(jnp.float32)
    key_total = jnp.concatenate(
        [total[:, (2 * g) * HD:(2 * g + 1) * HD] for g in range(kvh)], axis=1)
    value_total = jnp.concatenate(
        [total[:, (2 * g + 1) * HD:(2 * g + 2) * HD] for g in range(kvh)], axis=1)
    return (
        dq,
        (key_total * scale).astype(jnp.bfloat16),
        value_total.astype(jnp.bfloat16),
    )


def solution(mesh):
    in_specs = (
        P(("parts", "seq"), None),
        P(("parts", "seq"), None),
        P(("parts", "seq"), None),
        P(("parts", "seq"), None),
        P(("parts", "seq"), None),
        P(None, ("parts", "seq")),
        P("parts"),
    )
    out_specs = (P(("parts", "seq"), None), P(("parts", "seq"), None), P(("parts", "seq"), None))
    return jax.shard_map(
        per_device, mesh=mesh, in_specs=in_specs, out_specs=out_specs, check_vma=False
    )
```

```python
import math

import jax
import jax.numpy as jnp
from jax import lax
from jax.experimental import pallas as pl
from jax.experimental.pallas import tpu as pltpu
from jax.sharding import PartitionSpec as P

HD = 128
MOST = 512
KEY_TILE = 256
HEADS_PER_STEP = 16
NT_DIMS = (((1,), (1,)), ((), ()))


def shifted(block, axis, distance):
    devices = range(lax.axis_size(axis))
    route = [(i - distance, i) for i in devices if i - distance in devices]
    return lax.ppermute(block, axis, route)


def make_kernel(tok, reach, remote, dq_in, dq_final, n_alias, delta_in):
    hb = HEADS_PER_STEP
    pieces = list(range(reach)) if remote else [reach]
    tiles_per_piece = tok // KEY_TILE
    n_rows = len(pieces) * tok
    scale = 1.0 / math.sqrt(HD)

    def kernel(flags_ref, q_ref, do_ref, o_ref, lse_ref, bias_ref, *rest):
        rest = list(rest)
        kv_refs = [rest.pop(0) for _ in pieces]
        dqp_ref = rest.pop(0) if dq_in else None
        rest = rest[n_alias:]
        dq_ref = rest.pop(0)
        dkv_refs = [rest.pop(0) for _ in pieces]
        dl_out = None if delta_in else rest.pop(0)
        qs_out = None if delta_in else rest.pop(0)
        dos_out = None if delta_in else rest.pop(0)
        _, _, dqt_scr, kt_scr, acc_scr = rest[-5:]
        b = pl.program_id(0)
        nb = pl.num_programs(0)

        @pl.when(b == 0)
        def _():
            acc_scr[...] = jnp.zeros_like(acc_scr)
            for n, kv in enumerate(kv_refs):
                kt_scr[:, n * tok:(n + 1) * tok] = (
                    kv[:, :HD].astype(jnp.float32).T.astype(jnp.bfloat16))

        if delta_in:
            qs_scr, dos_scr = q_ref, do_ref
        else:
            qs_scr, dos_scr = qs_out, dos_out
        delta_rows = []
        for i in range(hb):
            cols = slice(i * HD, (i + 1) * HD)
            if not delta_in:
                qs_scr[i * tok:(i + 1) * tok, :] = q_ref[:, cols]
                dos_scr[i * tok:(i + 1) * tok, :] = do_ref[:, cols]
            if delta_in:
                delta_rows.append(o_ref[i:i + 1, :])
            else:
                prod = do_ref[:, cols].astype(jnp.float32) * o_ref[:, cols].astype(jnp.float32)
                row = jnp.sum(prod.T, axis=0, keepdims=True)
                dl_out[i:i + 1, :] = row
                delta_rows.append(row)
        dl_row = jnp.concatenate(delta_rows, axis=1)
        lse_row = jnp.concatenate([lse_ref[i:i + 1, :] for i in range(hb)], axis=1)
        dqt_scr[...] = jnp.zeros_like(dqt_scr)

        if tiles_per_piece == 1 and len(pieces) > 1:
            k = jnp.concatenate([kv[:, :HD] for kv in kv_refs], axis=0)
            v = jnp.concatenate([kv[:, HD:] for kv in kv_refs], axis=0)
            qs = qs_scr[...]
            dos = dos_scr[...]
            st = lax.dot_general(k, qs, NT_DIMS, preferred_element_type=jnp.float32)
            bias = bias_ref[...]
            p = jnp.exp(st * scale - lse_row + jnp.concatenate([bias] * hb, axis=1))
            dv = jnp.dot(p.astype(jnp.bfloat16), dos, preferred_element_type=jnp.float32)
            dpt = lax.dot_general(v, dos, NT_DIMS, preferred_element_type=jnp.float32)
            ds = (p * (dpt - dl_row)).astype(jnp.bfloat16)
            dk = jnp.dot(ds, qs, preferred_element_type=jnp.float32)
            for n in range(len(pieces)):
                acc_scr[n, :, :HD] += dk[n * tok:(n + 1) * tok]
                acc_scr[n, :, HD:] += dv[n * tok:(n + 1) * tok]
            dqt_scr[...] += jnp.dot(kt_scr[...], ds, preferred_element_type=jnp.float32)
            tiles_per_piece_loop = 0
        else:
            tiles_per_piece_loop = tiles_per_piece

        for n, piece in enumerate(pieces):
            kv = kv_refs[n]
            for t in range(tiles_per_piece_loop):
                j = piece * tiles_per_piece + t
                rows = slice(t * KEY_TILE, (t + 1) * KEY_TILE)
                loc_rows = slice(n * tok + t * KEY_TILE, n * tok + (t + 1) * KEY_TILE)

                def tile(kv=kv, rows=rows, loc_rows=loc_rows, n=n):
                    k = kv[rows, :HD]
                    v = kv[rows, HD:]
                    qs = qs_scr[...]
                    dos = dos_scr[...]
                    st = lax.dot_general(k, qs, NT_DIMS, preferred_element_type=jnp.float32)
                    bias = bias_ref[loc_rows, :]
                    p = jnp.exp(st * scale - lse_row + jnp.concatenate([bias] * hb, axis=1))
                    dv = jnp.dot(p.astype(jnp.bfloat16), dos, preferred_element_type=jnp.float32)
                    dpt = lax.dot_general(v, dos, NT_DIMS, preferred_element_type=jnp.float32)
                    ds = (p * (dpt - dl_row)).astype(jnp.bfloat16)
                    dk = jnp.dot(ds, qs, preferred_element_type=jnp.float32)
                    acc_scr[n, rows, :HD] += dk
                    acc_scr[n, rows, HD:] += dv
                    dqt_scr[...] += jnp.dot(
                        kt_scr[:, loc_rows], ds, preferred_element_type=jnp.float32)

                tile()

        for i in range(hb):
            cols = slice(i * HD, (i + 1) * HD)
            part = dqt_scr[:, i * tok:(i + 1) * tok].T
            if dq_in:
                part = part + dqp_ref[:, cols]
            if dq_final:
                dq_ref[:, cols] = (part * scale).astype(dq_ref.dtype)
            else:
                dq_ref[:, cols] = part

        @pl.when(b == nb - 1)
        def _():
            for n, dkv_ref in enumerate(dkv_refs):
                dkv_ref[...] = acc_scr[n].astype(dkv_ref.dtype)

    return kernel


def grads_call(group, remote, flags, queries, out_grad, outputs, lse, bias, kv_pieces,
               reach, dq_part=None, dq_alias=None, dkv_alias=None, delta=None):
    tok, width = queries.shape
    n_heads = width // HD
    kvh = kv_pieces[0].shape[1] // (2 * HD)
    heads_per_group = n_heads // kvh
    hb = HEADS_PER_STEP
    nb = heads_per_group // hb
    dq_final = dq_part is not None
    pieces = list(range(reach)) if remote else [reach]
    n_pieces = len(pieces)

    def head_block(b, *f):
        return (0, group * nb + b)

    def lse_block(b, *f):
        return (group * nb + b, 0)

    def local_block(b, *f):
        return (0, b)

    def local_rows(b, *f):
        return (b, 0)

    def bias_block(b, *f):
        return (0, 0)

    def kv_block(b, *f):
        return (0, group)

    stacked = pl.BlockSpec((hb * tok, HD), local_rows)
    in_specs = [
        pl.BlockSpec((tok, hb * HD), head_block) if delta is None else stacked,
        pl.BlockSpec((tok, hb * HD), head_block) if delta is None else stacked,
        pl.BlockSpec((tok, hb * HD), head_block) if delta is None
        else pl.BlockSpec((hb, tok), local_rows),
        pl.BlockSpec((hb, tok), lse_block),
        pl.BlockSpec((n_pieces * tok, tok), bias_block),
    ] + [pl.BlockSpec((tok, 2 * HD), kv_block) for _ in pieces]
    if delta is not None:
        delta, queries, out_grad = delta
    args = [queries, out_grad, outputs if delta is None else delta, lse, bias] + [kv_pieces[reach - p] for p in pieces]
    if dq_part is not None:
        in_specs.append(pl.BlockSpec((tok, hb * HD), local_block))
        args.append(dq_part)
    aliases = {}
    if dq_alias is not None:
        aliases[len(args)] = 0
        in_specs.append(pl.BlockSpec(memory_space=pl.ANY))
        args.append(dq_alias)
    if dkv_alias is not None:
        for n, piece_arr in enumerate(dkv_alias):
            aliases[len(args)] = 1 + n
            in_specs.append(pl.BlockSpec(memory_space=pl.ANY))
            args.append(piece_arr)

    kernel = make_kernel(tok, reach, remote, dq_part is not None, dq_final, len(aliases),
                         delta is not None)
    stack_shape = jax.ShapeDtypeStruct((heads_per_group * tok, HD), jnp.bfloat16)
    extra_shape = [] if delta is not None else [
        jax.ShapeDtypeStruct((heads_per_group, tok), jnp.float32), stack_shape, stack_shape]
    extra_spec = [] if delta is not None else [
        pl.BlockSpec((hb, tok), local_rows), pl.BlockSpec((hb * tok, HD), local_rows),
        pl.BlockSpec((hb * tok, HD), local_rows)]
    if dq_final:
        dq_shape = jax.ShapeDtypeStruct((tok, width), jnp.bfloat16)
        dq_spec = pl.BlockSpec((tok, hb * HD), head_block)
    else:
        dq_shape = jax.ShapeDtypeStruct((tok, heads_per_group * HD), jnp.float32)
        dq_spec = pl.BlockSpec((tok, hb * HD), local_block)
    if remote:
        dkv_shape = jax.ShapeDtypeStruct((tok, kvh * 2 * HD), jnp.bfloat16)
        dkv_spec = pl.BlockSpec((tok, 2 * HD), lambda b, *f: (0, group))
    else:
        dkv_shape = jax.ShapeDtypeStruct((tok, kvh * 2 * HD), jnp.float32)
        dkv_spec = pl.BlockSpec((tok, 2 * HD), lambda b, *f: (0, group))

    body = kernel

    def kernel(*refs):
        body(None, *refs)

    grid_spec = pltpu.PrefetchScalarGridSpec(
        num_scalar_prefetch=0,
        grid=(nb,),
        in_specs=in_specs,
        out_specs=[dq_spec] + [dkv_spec] * n_pieces + extra_spec,
        scratch_shapes=[
            pltpu.VMEM((hb * tok, HD), jnp.bfloat16),
            pltpu.VMEM((hb * tok, HD), jnp.bfloat16),
            pltpu.VMEM((HD, hb * tok), jnp.float32),
            pltpu.VMEM((HD, n_pieces * tok), jnp.bfloat16),
            pltpu.VMEM((n_pieces, tok, 2 * HD), jnp.float32),
        ],
    )
    outs = pl.pallas_call(
        kernel,
        grid_spec=grid_spec,
        out_shape=[dq_shape] + [dkv_shape] * n_pieces + extra_shape,
        input_output_aliases=aliases,
        compiler_params=pltpu.CompilerParams(dimension_semantics=("arbitrary",)),
    )(*args)
    return outs[0], outs[1:1 + n_pieces], (tuple(outs[-3:]) if delta is None else None)


def per_device(queries, keys, values, outputs, out_grad, logsumexp, doc_lengths):
    tok, width = queries.shape
    kvh = keys.shape[1] // HD
    reach = -(-(MOST - 1) // tok)
    win = (reach + 1) * tok
    scale = 1.0 / math.sqrt(HD)
    position = lax.axis_index("seq")
    doc_ends = jnp.cumsum(doc_lengths)

    def doc_of(places):
        return jnp.sum((doc_ends[None, :] <= places[:, None]).astype(jnp.int32), axis=1)

    key_places = (position - reach) * tok + jnp.arange(win, dtype=jnp.int32)
    key_ids = jnp.where(key_places >= 0, doc_of(key_places), -1)
    query_ids = key_ids[reach * tok:]
    query_index = jnp.arange(tok, dtype=jnp.int32)
    own_visible = (query_ids[:, None] == query_ids[None, :]) & (
        query_index[:, None] <= query_index[None, :])
    bias_own = jnp.where(own_visible, 0.0, -jnp.inf).astype(jnp.float32)
    remote_ids = key_ids[:reach * tok]
    bias_rem = jnp.where(remote_ids[:, None] == query_ids[None, :], 0.0, -jnp.inf
                         ).astype(jnp.float32)

    kv = jnp.concatenate(
        [part for g in range(kvh)
         for part in (keys[:, g * HD:(g + 1) * HD], values[:, g * HD:(g + 1) * HD])], axis=1)
    kv_pieces = [kv] + [shifted(kv, "seq", hop) for hop in range(1, reach + 1)]
    own = (None, queries, out_grad, outputs, logsumexp, bias_own, kv_pieces, reach)
    rem = (None, queries, out_grad, outputs, logsumexp, bias_rem, kv_pieces, reach)

    dq_part0, (dkv_own0,), delta0 = grads_call(0, False, *own)
    dq, dkv_rem, _ = grads_call(0, True, *rem, dq_part=dq_part0, delta=delta0)
    dq_part1, dkv_rem, delta1 = grads_call(1, True, *rem, dkv_alias=dkv_rem)
    returned = [shifted(dkv_rem[reach - hop], "seq", -hop) for hop in range(1, reach + 1)]
    dq, (total,), _ = grads_call(1, False, *own, dq_part=dq_part1, dq_alias=dq,
                                 dkv_alias=[dkv_own0], delta=delta1)

    for r in returned:
        total = total + r.astype(jnp.float32)
    key_total = jnp.concatenate(
        [total[:, (2 * g) * HD:(2 * g + 1) * HD] for g in range(kvh)], axis=1)
    value_total = jnp.concatenate(
        [total[:, (2 * g + 1) * HD:(2 * g + 2) * HD] for g in range(kvh)], axis=1)
    return (
        dq,
        (key_total * scale).astype(jnp.bfloat16),
        value_total.astype(jnp.bfloat16),
    )


def solution(mesh):
    in_specs = (
        P(("parts", "seq"), None),
        P(("parts", "seq"), None),
        P(("parts", "seq"), None),
        P(("parts", "seq"), None),
        P(("parts", "seq"), None),
        P(None, ("parts", "seq")),
        P("parts"),
    )
    out_specs = (P(("parts", "seq"), None), P(("parts", "seq"), None), P(("parts", "seq"), None))
    return jax.shard_map(
        per_device, mesh=mesh, in_specs=in_specs, out_specs=out_specs, check_vma=False
    )
```

```python
import math

import jax
import jax.numpy as jnp
from jax import lax
from jax.experimental import pallas as pl
from jax.experimental.pallas import tpu as pltpu
from jax.sharding import PartitionSpec as P

HD = 128
MOST = 512
KEY_TILE = 256
HEADS_PER_STEP = 16
OWN_HEADS_PER_STEP = 8
NT_DIMS = (((1,), (1,)), ((), ()))


def shifted(block, axis, distance):
    devices = range(lax.axis_size(axis))
    route = [(i - distance, i) for i in devices if i - distance in devices]
    return lax.ppermute(block, axis, route)


def make_kernel(tok, reach, remote, dq_in, dq_final, n_alias, delta_in):
    hb = HEADS_PER_STEP if remote else OWN_HEADS_PER_STEP
    pieces = list(range(reach)) if remote else [reach]
    tiles_per_piece = tok // KEY_TILE
    n_rows = len(pieces) * tok
    scale = 1.0 / math.sqrt(HD)

    def kernel(flags_ref, q_ref, do_ref, o_ref, lse_ref, bias_ref, *rest):
        rest = list(rest)
        kv_refs = [rest.pop(0) for _ in pieces]
        dqp_ref = rest.pop(0) if dq_in else None
        rest = rest[n_alias:]
        dq_ref = rest.pop(0)
        dkv_refs = [rest.pop(0) for _ in pieces]
        dl_out = None if delta_in else rest.pop(0)
        qs_out = None if delta_in else rest.pop(0)
        dos_out = None if delta_in else rest.pop(0)
        _, _, dqt_scr, kt_scr, acc_scr = rest[-5:]
        b = pl.program_id(0)
        nb = pl.num_programs(0)

        @pl.when(b == 0)
        def _():
            acc_scr[...] = jnp.zeros_like(acc_scr)
            for n, kv in enumerate(kv_refs):
                kt_scr[:, n * tok:(n + 1) * tok] = (
                    kv[:, :HD].astype(jnp.float32).T.astype(jnp.bfloat16))

        if delta_in:
            qs_scr, dos_scr = q_ref, do_ref
        else:
            qs_scr, dos_scr = qs_out, dos_out
        delta_rows = []
        for i in range(hb):
            cols = slice(i * HD, (i + 1) * HD)
            if not delta_in:
                qs_scr[i * tok:(i + 1) * tok, :] = q_ref[:, cols]
                dos_scr[i * tok:(i + 1) * tok, :] = do_ref[:, cols]
            if delta_in:
                delta_rows.append(o_ref[i:i + 1, :])
            else:
                prod = do_ref[:, cols].astype(jnp.float32) * o_ref[:, cols].astype(jnp.float32)
                row = jnp.sum(prod.T, axis=0, keepdims=True)
                dl_out[i:i + 1, :] = row
                delta_rows.append(row)
        dl_row = jnp.concatenate(delta_rows, axis=1)
        lse_row = jnp.concatenate([lse_ref[i:i + 1, :] for i in range(hb)], axis=1)
        dqt_scr[...] = jnp.zeros_like(dqt_scr)

        if tiles_per_piece == 1 and len(pieces) > 1:
            k = jnp.concatenate([kv[:, :HD] for kv in kv_refs], axis=0)
            v = jnp.concatenate([kv[:, HD:] for kv in kv_refs], axis=0)
            qs = qs_scr[...]
            dos = dos_scr[...]
            st = lax.dot_general(k, qs, NT_DIMS, preferred_element_type=jnp.float32)
            bias = bias_ref[...]
            p = jnp.exp(st * scale - lse_row + jnp.concatenate([bias] * hb, axis=1))
            dv = jnp.dot(p.astype(jnp.bfloat16), dos, preferred_element_type=jnp.float32)
            dpt = lax.dot_general(v, dos, NT_DIMS, preferred_element_type=jnp.float32)
            ds = (p * (dpt - dl_row)).astype(jnp.bfloat16)
            dk = jnp.dot(ds, qs, preferred_element_type=jnp.float32)
            for n in range(len(pieces)):
                acc_scr[n, :, :HD] += dk[n * tok:(n + 1) * tok]
                acc_scr[n, :, HD:] += dv[n * tok:(n + 1) * tok]
            dqt_scr[...] += jnp.dot(kt_scr[...], ds, preferred_element_type=jnp.float32)
            tiles_per_piece_loop = 0
        else:
            tiles_per_piece_loop = tiles_per_piece

        for n, piece in enumerate(pieces):
            kv = kv_refs[n]
            for t in range(tiles_per_piece_loop):
                j = piece * tiles_per_piece + t
                rows = slice(t * KEY_TILE, (t + 1) * KEY_TILE)
                loc_rows = slice(n * tok + t * KEY_TILE, n * tok + (t + 1) * KEY_TILE)

                def tile(kv=kv, rows=rows, loc_rows=loc_rows, n=n):
                    k = kv[rows, :HD]
                    v = kv[rows, HD:]
                    qs = qs_scr[...]
                    dos = dos_scr[...]
                    st = lax.dot_general(k, qs, NT_DIMS, preferred_element_type=jnp.float32)
                    bias = bias_ref[loc_rows, :]
                    p = jnp.exp(st * scale - lse_row + jnp.concatenate([bias] * hb, axis=1))
                    dv = jnp.dot(p.astype(jnp.bfloat16), dos, preferred_element_type=jnp.float32)
                    dpt = lax.dot_general(v, dos, NT_DIMS, preferred_element_type=jnp.float32)
                    ds = (p * (dpt - dl_row)).astype(jnp.bfloat16)
                    dk = jnp.dot(ds, qs, preferred_element_type=jnp.float32)
                    acc_scr[n, rows, :HD] += dk
                    acc_scr[n, rows, HD:] += dv
                    dqt_scr[...] += jnp.dot(
                        kt_scr[:, loc_rows], ds, preferred_element_type=jnp.float32)

                tile()

        for i in range(hb):
            cols = slice(i * HD, (i + 1) * HD)
            part = dqt_scr[:, i * tok:(i + 1) * tok].T
            if dq_in:
                part = part + dqp_ref[:, cols]
            if dq_final:
                dq_ref[:, cols] = (part * scale).astype(dq_ref.dtype)
            else:
                dq_ref[:, cols] = part

        @pl.when(b == nb - 1)
        def _():
            for n, dkv_ref in enumerate(dkv_refs):
                dkv_ref[...] = acc_scr[n].astype(dkv_ref.dtype)

    return kernel


def grads_call(group, remote, flags, queries, out_grad, outputs, lse, bias, kv_pieces,
               reach, dq_part=None, dq_alias=None, dkv_alias=None, delta=None):
    tok, width = queries.shape
    n_heads = width // HD
    kvh = kv_pieces[0].shape[1] // (2 * HD)
    heads_per_group = n_heads // kvh
    hb = HEADS_PER_STEP if remote else OWN_HEADS_PER_STEP
    nb = heads_per_group // hb
    dq_final = dq_part is not None
    pieces = list(range(reach)) if remote else [reach]
    n_pieces = len(pieces)

    def head_block(b, *f):
        return (0, group * nb + b)

    def lse_block(b, *f):
        return (group * nb + b, 0)

    def local_block(b, *f):
        return (0, b)

    def local_rows(b, *f):
        return (b, 0)

    def bias_block(b, *f):
        return (0, 0)

    def kv_block(b, *f):
        return (0, group)

    stacked = pl.BlockSpec((hb * tok, HD), local_rows)
    in_specs = [
        pl.BlockSpec((tok, hb * HD), head_block) if delta is None else stacked,
        pl.BlockSpec((tok, hb * HD), head_block) if delta is None else stacked,
        pl.BlockSpec((tok, hb * HD), head_block) if delta is None
        else pl.BlockSpec((hb, tok), local_rows),
        pl.BlockSpec((hb, tok), lse_block),
        pl.BlockSpec((n_pieces * tok, tok), bias_block),
    ] + [pl.BlockSpec((tok, 2 * HD), kv_block) for _ in pieces]
    if delta is not None:
        delta, queries, out_grad = delta
    args = [queries, out_grad, outputs if delta is None else delta, lse, bias] + [kv_pieces[reach - p] for p in pieces]
    if dq_part is not None:
        in_specs.append(pl.BlockSpec((tok, hb * HD), local_block))
        args.append(dq_part)
    aliases = {}
    if dq_alias is not None:
        aliases[len(args)] = 0
        in_specs.append(pl.BlockSpec(memory_space=pl.ANY))
        args.append(dq_alias)
    if dkv_alias is not None:
        for n, piece_arr in enumerate(dkv_alias):
            aliases[len(args)] = 1 + n
            in_specs.append(pl.BlockSpec(memory_space=pl.ANY))
            args.append(piece_arr)

    kernel = make_kernel(tok, reach, remote, dq_part is not None, dq_final, len(aliases),
                         delta is not None)
    stack_shape = jax.ShapeDtypeStruct((heads_per_group * tok, HD), jnp.bfloat16)
    extra_shape = [] if delta is not None else [
        jax.ShapeDtypeStruct((heads_per_group, tok), jnp.float32), stack_shape, stack_shape]
    extra_spec = [] if delta is not None else [
        pl.BlockSpec((hb, tok), local_rows), pl.BlockSpec((hb * tok, HD), local_rows),
        pl.BlockSpec((hb * tok, HD), local_rows)]
    if dq_final:
        dq_shape = jax.ShapeDtypeStruct((tok, width), jnp.bfloat16)
        dq_spec = pl.BlockSpec((tok, hb * HD), head_block)
    else:
        dq_shape = jax.ShapeDtypeStruct((tok, heads_per_group * HD), jnp.float32)
        dq_spec = pl.BlockSpec((tok, hb * HD), local_block)
    if remote:
        dkv_shape = jax.ShapeDtypeStruct((tok, kvh * 2 * HD), jnp.bfloat16)
        dkv_spec = pl.BlockSpec((tok, 2 * HD), lambda b, *f: (0, group))
    else:
        dkv_shape = jax.ShapeDtypeStruct((tok, kvh * 2 * HD), jnp.float32)
        dkv_spec = pl.BlockSpec((tok, 2 * HD), lambda b, *f: (0, group))

    body = kernel

    def kernel(*refs):
        body(None, *refs)

    grid_spec = pltpu.PrefetchScalarGridSpec(
        num_scalar_prefetch=0,
        grid=(nb,),
        in_specs=in_specs,
        out_specs=[dq_spec] + [dkv_spec] * n_pieces + extra_spec,
        scratch_shapes=[
            pltpu.VMEM((hb * tok, HD), jnp.bfloat16),
            pltpu.VMEM((hb * tok, HD), jnp.bfloat16),
            pltpu.VMEM((HD, hb * tok), jnp.float32),
            pltpu.VMEM((HD, n_pieces * tok), jnp.bfloat16),
            pltpu.VMEM((n_pieces, tok, 2 * HD), jnp.float32),
        ],
    )
    outs = pl.pallas_call(
        kernel,
        grid_spec=grid_spec,
        out_shape=[dq_shape] + [dkv_shape] * n_pieces + extra_shape,
        input_output_aliases=aliases,
        compiler_params=pltpu.CompilerParams(dimension_semantics=("arbitrary",)),
    )(*args)
    return outs[0], outs[1:1 + n_pieces], (tuple(outs[-3:]) if delta is None else None)


def per_device(queries, keys, values, outputs, out_grad, logsumexp, doc_lengths):
    tok, width = queries.shape
    kvh = keys.shape[1] // HD
    reach = -(-(MOST - 1) // tok)
    win = (reach + 1) * tok
    scale = 1.0 / math.sqrt(HD)
    position = lax.axis_index("seq")
    doc_ends = jnp.cumsum(doc_lengths)

    def doc_of(places):
        return jnp.sum((doc_ends[None, :] <= places[:, None]).astype(jnp.int32), axis=1)

    key_places = (position - reach) * tok + jnp.arange(win, dtype=jnp.int32)
    key_ids = jnp.where(key_places >= 0, doc_of(key_places), -1)
    query_ids = key_ids[reach * tok:]
    query_index = jnp.arange(tok, dtype=jnp.int32)
    own_visible = (query_ids[:, None] == query_ids[None, :]) & (
        query_index[:, None] <= query_index[None, :])
    bias_own = jnp.where(own_visible, 0.0, -jnp.inf).astype(jnp.float32)
    remote_ids = key_ids[:reach * tok]
    bias_rem = jnp.where(remote_ids[:, None] == query_ids[None, :], 0.0, -jnp.inf
                         ).astype(jnp.float32)

    kv = jnp.concatenate(
        [part for g in range(kvh)
         for part in (keys[:, g * HD:(g + 1) * HD], values[:, g * HD:(g + 1) * HD])], axis=1)
    kv_pieces = [kv] + [shifted(kv, "seq", hop) for hop in range(1, reach + 1)]
    own = (None, queries, out_grad, outputs, logsumexp, bias_own, kv_pieces, reach)
    rem = (None, queries, out_grad, outputs, logsumexp, bias_rem, kv_pieces, reach)

    dq_part0, (dkv_own0,), delta0 = grads_call(0, False, *own)
    dq, dkv_rem, _ = grads_call(0, True, *rem, dq_part=dq_part0, delta=delta0)
    dq_part1, dkv_rem, delta1 = grads_call(1, True, *rem, dkv_alias=dkv_rem)
    returned = [shifted(dkv_rem[reach - hop], "seq", -hop) for hop in range(1, reach + 1)]
    dq, (total,), _ = grads_call(1, False, *own, dq_part=dq_part1, dq_alias=dq,
                                 dkv_alias=[dkv_own0], delta=delta1)

    for r in returned:
        total = total + r.astype(jnp.float32)
    key_total = jnp.concatenate(
        [total[:, (2 * g) * HD:(2 * g + 1) * HD] for g in range(kvh)], axis=1)
    value_total = jnp.concatenate(
        [total[:, (2 * g + 1) * HD:(2 * g + 2) * HD] for g in range(kvh)], axis=1)
    return (
        dq,
        (key_total * scale).astype(jnp.bfloat16),
        value_total.astype(jnp.bfloat16),
    )


def solution(mesh):
    in_specs = (
        P(("parts", "seq"), None),
        P(("parts", "seq"), None),
        P(("parts", "seq"), None),
        P(("parts", "seq"), None),
        P(("parts", "seq"), None),
        P(None, ("parts", "seq")),
        P("parts"),
    )
    out_specs = (P(("parts", "seq"), None), P(("parts", "seq"), None), P(("parts", "seq"), None))
    return jax.shard_map(
        per_device, mesh=mesh, in_specs=in_specs, out_specs=out_specs, check_vma=False
    )
```
